32 devices in a mesh: pipe: 2 (over y), ctx: 4 (over z), dp: 4 (over x, core).
Axes of the slice: x: 2, y: 2, z: 4, core: 2. Of those that a mesh axis runs over, the one named last changes fastest.
Arguments:
- query: bfloat16 [8, 512, 2048], P(('dp', 'pipe'), 'ctx'), parts along dimension 0, may hold values from -6 to 6
- keys: bfloat16 [8, 512, 512], P(('dp', 'pipe'), 'ctx'), parts along dimension 0, may hold values from -6 to 6
- values: bfloat16 [8, 512, 512], P(('dp', 'pipe'), 'ctx'), parts along dimension 0, may hold values from -6 to 6
- grad_out: bfloat16 [8, 512, 2048], P(('dp', 'pipe'), 'ctx'), parts along dimension 0, may hold values from -6 to 6
- random_blocks: int32 [2, 8, 16, 8], P('pipe', 'ctx'), may hold values from 0 to 1, as said below
- global_ids: int32 [2, 2], P('pipe'), may hold values from 0 to 7, as said below
Outputs:
- next_input: bfloat16 [8, 512, 2048], P(('dp', 'pipe'), 'ctx'), parts along dimension 0
- grad_query: bfloat16 [8, 512, 2048], P(('dp', 'pipe'), 'ctx'), parts along dimension 0
- grad_key: bfloat16 [8, 512, 512], P(('dp', 'pipe'), 'ctx'), parts along dimension 0
- grad_value: bfloat16 [8, 512, 512], P(('dp', 'pipe'), 'ctx'), parts along dimension 0
The draws below stay inside these ranges and needn't reach their ends.
There are 4 independent parts, one for each index of `dp`. The reference program is written for one: setup_inputs(seed, part) draws one part's arguments, and reference() takes and returns one part's arrays. A program takes and returns all parts, laid end to end along the dimension named above; an argument that names none is the same for every part. Nothing has to cross between parts.
Inputs may be any that keep to these rules, and one draw needn't show every extreme that they name: `random_blocks`: for each section, query block and head exactly 3 entries are 1 and the others 0. `global_ids`: for each section, 2 different block numbers; those of section 0 include block 0 and block 7.
All inputs are finite; a program needn't handle non-finite values.
Results may differ from the reference program's by a relative error of at most 0.014.
Values may be sent and summed in bfloat16 or wider, within the bound.
No kernel may reach another device: no remote copies, remote signals or barrier semaphores. Data moves between devices by JAX's collectives and lax.ppermute only.
A program may use at most 64 MiB of HBM per device.

```python
import jax
import jax.numpy as jnp
from jax import lax

H = 16
KVH = 4
HD = 128
BLOCK = 64
RAND = 3
NGLOB = 2
TOK_DEV = 128
QW = 2048
KVW = 512
SECTIONS = 2
SEQ = 512
NB = 8
N_CTX = 4


def base_values(key, shape):
    return jnp.clip(jax.random.normal(key, shape, jnp.float32), -6.0, 6.0)


def draw_query(key, part):
    drawn_values = base_values(jax.random.fold_in(key, 1), (SECTIONS, SEQ, QW))
    return drawn_values.astype(jnp.bfloat16)


def draw_keys(key, part):
    drawn_values = base_values(jax.random.fold_in(key, 2), (SECTIONS, SEQ, KVW))
    return drawn_values.astype(jnp.bfloat16)


def draw_random_blocks(key, part):
    block_ids = jnp.arange(NB, dtype=jnp.int32)
    scores = jax.random.randint(jax.random.fold_in(key, 11), (SECTIONS, NB, H, NB), 0, 1 << 20) * NB + block_ids
    top_values, picked = lax.top_k(scores, RAND)
    picked_mask = jnp.any(picked[..., :, None] == block_ids, axis=-2)
    return picked_mask.astype(jnp.int32)


def draw_global_ids(key, part):
    block_ids = jnp.arange(NB, dtype=jnp.int32)
    section_ids = jnp.arange(SECTIONS, dtype=jnp.int32)
    scores = jax.random.randint(jax.random.fold_in(key, 12), (SECTIONS, NB), 0, 1 << 20) * NB + block_ids
    forced = (section_ids[:, None] == 0) & ((block_ids[None, :] == 0) | (block_ids[None, :] == NB - 1))
    scores = scores + jnp.where(forced, (1 << 20) * NB, 0).astype(jnp.int32)
    top_values, picked = lax.top_k(scores, NGLOB)
    return picked.astype(jnp.int32)


def block_levels(own_key, extent, pieces, least, top_value):
    def one(position, blocks):
        draws = jax.random.uniform(jax.random.fold_in(jax.random.fold_in(own_key, 6), position), (blocks,), jnp.float32, least / len(pieces), top_value / len(pieces))
        return jnp.repeat(jnp.exp(draws), extent[position] // blocks).reshape((-1,) + (1,) * (len(extent) - position - 1))

    level = one(*pieces[0])
    for cut in pieces[1:]:
        level = level * one(*cut)
    return level


def bell_draw(key, dims, width, reach, split=(), held_as=jnp.bfloat16):
    gain = block_levels(key, dims, split, -0.22, 0.18) if split else 1.0
    result = jax.random.normal(key, dims, jnp.float32) * width * gain
    return jnp.minimum(jnp.maximum(result, -reach), reach).astype(held_as)


def setup_inputs(seed: int = 0, part: int = 0) -> dict:
    streams_of = jax.random.split(jax.random.key(seed), 7)
    part_keys = jax.random.split(jax.random.fold_in(streams_of[6], part), 7)
    return {
        "query": draw_query(jax.random.fold_in(jax.random.fold_in(streams_of[6], part), 71), part),
        "keys": draw_keys(jax.random.fold_in(jax.random.fold_in(streams_of[6], part), 71), part),
        "values": bell_draw(part_keys[2], (SECTIONS, SEQ, KVW), 1.0, 6.0, ((0, 2), (1, 4))),
        "grad_out": bell_draw(part_keys[3], (SECTIONS, SEQ, QW), 1.0, 6.0, ((0, 2), (1, 4))),
        "random_blocks": draw_random_blocks(jax.random.fold_in(streams_of[6], 71), part),
        "global_ids": draw_global_ids(jax.random.fold_in(streams_of[6], 71), part),
    }


NEG_FILL = -1e30


def block_table(random_rows, global_row, first_block):
    query_blocks, head_count, key_blocks = random_rows.shape
    query_ids = first_block + jnp.arange(query_blocks, dtype=jnp.int32)
    key_ids = jnp.arange(key_blocks, dtype=jnp.int32)
    query_global = jnp.any(query_ids[:, None] == global_row[None, :], axis=1)
    key_global = jnp.any(key_ids[:, None] == global_row[None, :], axis=1)
    nearby = jnp.abs(query_ids[:, None] - key_ids[None, :]) <= 1
    fixed_part = nearby | query_global[:, None] | key_global[None, :]
    return (random_rows > 0) | fixed_part[:, None, :]


def token_mask(table_part, first_query, first_key):
    query_blocks, head_count, key_blocks = table_part.shape
    expanded = jnp.broadcast_to(table_part[:, None, :, :, None], (query_blocks, BLOCK, head_count, key_blocks, BLOCK))
    expanded = expanded.reshape(query_blocks * BLOCK, head_count, key_blocks * BLOCK)
    query_pos = first_query + jnp.arange(query_blocks * BLOCK, dtype=jnp.int32)
    key_pos = first_key + jnp.arange(key_blocks * BLOCK, dtype=jnp.int32)
    return expanded & (key_pos[None, None, :] <= query_pos[:, None, None])


def round_trip(array):
    return lax.optimization_barrier(array.astype(jnp.bfloat16)).astype(jnp.float32)


def section_pass(query_s, keys_s, values_s, grad_s, random_s, global_s):
    group_size = H // KVH
    score_scale = HD ** -0.5
    table = block_table(random_s, global_s, 0)
    key_heads = keys_s.astype(jnp.float32).reshape(SEQ, KVH, HD)
    value_heads = values_s.astype(jnp.float32).reshape(SEQ, KVH, HD)

    def shard_step(sums, shard):
        first_query = shard * TOK_DEV
        query_rows = lax.dynamic_slice_in_dim(query_s, first_query, TOK_DEV, 0).astype(jnp.float32).reshape(TOK_DEV, KVH, group_size, HD)
        grad_rows = lax.dynamic_slice_in_dim(grad_s, first_query, TOK_DEV, 0).astype(jnp.float32).reshape(TOK_DEV, KVH, group_size, HD)
        table_rows = lax.dynamic_slice_in_dim(table, shard * (TOK_DEV // BLOCK), TOK_DEV // BLOCK, 0)
        allowed = token_mask(table_rows, first_query, 0).reshape(TOK_DEV, KVH, group_size, SEQ)
        raw_scores = jnp.einsum("tkgd,ukd->tkgu", query_rows, key_heads) * score_scale
        row_high = jnp.max(jnp.where(allowed, raw_scores, NEG_FILL), axis=-1)
        shifted = jnp.where(allowed, jnp.exp(raw_scores - row_high[..., None]), 0.0)
        row_total = jnp.sum(shifted, axis=-1)
        log_total = row_high + jnp.log(row_total)
        attended = (jnp.einsum("tkgu,ukd->tkgd", round_trip(shifted), value_heads) / row_total[..., None]).astype(jnp.bfloat16)
        delta = jnp.sum(grad_rows * attended.astype(jnp.float32), axis=-1)
        row_probs = jnp.where(allowed, jnp.exp(raw_scores - log_total[..., None]), 0.0)
        value_part = jnp.einsum("tkgu,tkgd->ukd", round_trip(row_probs), grad_rows)
        prob_grads = jnp.einsum("tkgd,ukd->tkgu", grad_rows, value_heads)
        score_grads = round_trip(row_probs * (prob_grads - delta[..., None]))
        query_grad = (jnp.einsum("tkgu,ukd->tkgd", score_grads, key_heads) * score_scale).astype(jnp.bfloat16)
        key_part = jnp.einsum("tkgu,tkgd->ukd", score_grads, query_rows) * score_scale
        key_sum = sums[0] + round_trip(key_part.reshape(SEQ, KVW))
        value_sum = sums[1] + round_trip(value_part.reshape(SEQ, KVW))
        return (key_sum, value_sum), (attended.reshape(TOK_DEV, QW), query_grad.reshape(TOK_DEV, QW))

    start_sums = (jnp.zeros((SEQ, KVW), jnp.float32), jnp.zeros((SEQ, KVW), jnp.float32))
    final_sums, row_outs = lax.scan(shard_step, start_sums, jnp.arange(N_CTX, dtype=jnp.int32))
    attended_all = row_outs[0].reshape(SEQ, QW)
    query_all = row_outs[1].reshape(SEQ, QW)
    return attended_all, query_all, final_sums[0].astype(jnp.bfloat16), final_sums[1].astype(jnp.bfloat16)


def reference(query, keys, values, grad_out, random_blocks, global_ids):
    def one_section(section):
        return section_pass(query[section], keys[section], values[section], grad_out[section], random_blocks[section], global_ids[section])

    attended, query_grad, key_grad, value_grad = lax.map(one_section, jnp.arange(SECTIONS, dtype=jnp.int32))
    next_input = jnp.roll(attended, 1, axis=0)
    return (next_input, jnp.roll(query_grad, -1, axis=0), jnp.roll(key_grad, -1, axis=0), jnp.roll(value_grad, -1, axis=0))
```

```python
import jax
import jax.numpy as jnp
from jax import lax
from jax.sharding import PartitionSpec as P

H = 16
KVH = 4
HD = 128
BLOCK = 64


NEG_FILL = -1e30


def passed_along(value, axis, steps):
    count = lax.axis_size(axis)
    pairs = [(source, (source + steps) % count) for source in range(count)]
    return lax.ppermute(value, axis, pairs)


def shifted_open(value, axis, steps):
    count = lax.axis_size(axis)
    pairs = [(source, source + steps) for source in range(count) if 0 <= source + steps < count]
    return lax.ppermute(value, axis, pairs)


def piece_mask(random_rows, global_row, ctx_index, shift, tok_rows, group_size):
    query_blocks, head_count, block_count = random_rows.shape
    key_shard = ctx_index - shift
    query_ids = ctx_index * query_blocks + jnp.arange(query_blocks, dtype=jnp.int32)
    key_ids = key_shard * query_blocks + jnp.arange(query_blocks, dtype=jnp.int32)
    start = jnp.clip(key_shard * query_blocks, 0, block_count - query_blocks)
    random_part = lax.dynamic_slice_in_dim(random_rows, start, query_blocks, 2) > 0
    query_global = jnp.any(query_ids[:, None] == global_row[None, :], axis=1)
    key_global = jnp.any(key_ids[:, None] == global_row[None, :], axis=1)
    nearby = jnp.abs(query_ids[:, None] - key_ids[None, :]) <= 1
    fixed_part = nearby | query_global[:, None] | key_global[None, :]
    table = (random_part | fixed_part[:, None, :]) & (key_shard >= 0)
    table = table.reshape(query_blocks, KVH, group_size, query_blocks)
    row_pos = lax.broadcasted_iota(jnp.int32, (tok_rows, 1, 1, tok_rows), 0)
    col_pos = lax.broadcasted_iota(jnp.int32, (tok_rows, 1, 1, tok_rows), 3)
    row_block = row_pos // BLOCK
    col_block = col_pos // BLOCK
    allowed = jnp.zeros((tok_rows, KVH, group_size, tok_rows), jnp.bool_)
    for qi in range(query_blocks):
        for kj in range(query_blocks):
            hit = (row_block == qi) & (col_block == kj)
            allowed = allowed | (hit & table[qi, :, :, kj][None, :, :, None])
    causal = key_shard * tok_rows + col_pos <= ctx_index * tok_rows + row_pos
    return allowed & causal


def local(query, keys, values, grad_out, random_blocks, global_ids):
    tok_rows = query.shape[1]
    query_width = query.shape[2]
    key_width = keys.shape[2]
    ctx_count = lax.axis_size("ctx")
    group_size = H // KVH
    score_scale = HD ** (-0.5)
    ctx_index = lax.axis_index("ctx")
    random_rows = random_blocks[0]
    global_row = global_ids[0]
    query_heads = query[0].reshape(tok_rows, KVH, group_size, HD)
    grad_heads = grad_out[0].reshape(tok_rows, KVH, group_size, HD)

    own = (keys[0], values[0])
    pieces = [own] + [shifted_open(own, "ctx", shift) for shift in range(1, ctx_count)]

    masks = []
    scores = []
    highs = []
    for shift in range(ctx_count):
        key_piece = pieces[shift][0].reshape(tok_rows, KVH, HD)
        allowed = piece_mask(random_rows, global_row, ctx_index, shift, tok_rows, group_size)
        raw = (
            jnp.einsum("tkgd,ukd->tkgu", query_heads, key_piece, preferred_element_type=jnp.float32)
            * score_scale
        )
        masks.append(allowed)
        scores.append(raw)
        highs.append(jnp.max(jnp.where(allowed, raw, NEG_FILL), axis=-1))
    row_high = highs[0]
    for more in highs[1:]:
        row_high = jnp.maximum(row_high, more)

    row_total = None
    accumulated = None
    for shift in range(ctx_count):
        value_piece = pieces[shift][1].reshape(tok_rows, KVH, HD)
        weights = jnp.where(masks[shift], jnp.exp(scores[shift] - row_high[..., None]), 0.0)
        part_total = jnp.sum(weights, axis=-1)
        part_acc = jnp.einsum(
            "tkgu,ukd->tkgd",
            weights.astype(jnp.bfloat16),
            value_piece,
            preferred_element_type=jnp.float32,
        )
        row_total = part_total if row_total is None else row_total + part_total
        accumulated = part_acc if accumulated is None else accumulated + part_acc
    attended = (accumulated / row_total[..., None]).astype(jnp.bfloat16)
    log_total = row_high + jnp.log(row_total)
    next_input = passed_along(attended.reshape(tok_rows, query_width)[None], "pipe", 1)
    delta = jnp.sum(grad_heads.astype(jnp.float32) * attended.astype(jnp.float32), axis=-1)

    query_accum = None
    key_own = None
    value_own = None
    received = []
    recompute = ctx_count * tok_rows > 512
    for shift in reversed(range(ctx_count)):
        key_piece = pieces[shift][0].reshape(tok_rows, KVH, HD)
        value_piece = pieces[shift][1].reshape(tok_rows, KVH, HD)
        raw = scores[shift]
        allowed = masks[shift]
        if recompute:
            key_piece, value_piece, log_total = lax.optimization_barrier(
                (key_piece, value_piece, log_total)
            )
            allowed = piece_mask(random_rows, global_row, ctx_index, shift, tok_rows, group_size)
            raw = (
                jnp.einsum("tkgd,ukd->tkgu", query_heads, key_piece, preferred_element_type=jnp.float32)
                * score_scale
            )
        row_probs = jnp.where(allowed, jnp.exp(raw - log_total[..., None]), 0.0)
        value_term = jnp.einsum(
            "tkgu,tkgd->ukd",
            row_probs.astype(jnp.bfloat16),
            grad_heads,
            preferred_element_type=jnp.float32,
        ).astype(jnp.bfloat16)
        prob_grads = jnp.einsum(
            "tkgd,ukd->tkgu", grad_heads, value_piece, preferred_element_type=jnp.float32
        )
        score_grads = (row_probs * (prob_grads - delta[..., None])).astype(jnp.bfloat16)
        part_q = jnp.einsum(
            "tkgu,ukd->tkgd", score_grads, key_piece, preferred_element_type=jnp.float32
        )
        query_accum = part_q if query_accum is None else query_accum + part_q
        key_term = (
            jnp.einsum("tkgu,tkgd->ukd", score_grads, query_heads, preferred_element_type=jnp.float32)
            * score_scale
        ).astype(jnp.bfloat16)
        key_term = key_term.reshape(tok_rows, key_width)
        value_term = value_term.reshape(tok_rows, key_width)
        if shift == 0:
            key_own = key_term
            value_own = value_term
        else:
            received.append(shifted_open((key_term, value_term), "ctx", -shift))

    query_grad = (query_accum * score_scale).astype(jnp.bfloat16).reshape(tok_rows, query_width)
    grad_query = passed_along(query_grad[None], "pipe", -1)
    key_sum = key_own.astype(jnp.float32)
    value_sum = value_own.astype(jnp.float32)
    for key_in, value_in in received:
        key_sum = key_sum + key_in.astype(jnp.float32)
        value_sum = value_sum + value_in.astype(jnp.float32)
    returned = passed_along(
        (key_sum.astype(jnp.bfloat16)[None], value_sum.astype(jnp.bfloat16)[None]), "pipe", -1
    )
    grad_key, grad_value = returned
    return (next_input, grad_query, grad_key, grad_value)


def solution(mesh):
    placed = (
        P(("dp", "pipe"), "ctx", None),
        P(("dp", "pipe"), "ctx", None),
        P(("dp", "pipe"), "ctx", None),
        P(("dp", "pipe"), "ctx", None),
        P("pipe", "ctx", None, None),
        P("pipe", None),
    )
    return jax.shard_map(
        local,
        mesh=mesh,
        in_specs=placed,
        out_specs=(
            P(("dp", "pipe"), "ctx", None),
            P(("dp", "pipe"), "ctx", None),
            P(("dp", "pipe"), "ctx", None),
            P(("dp", "pipe"), "ctx", None),
        ),
        check_vma=False,
    )
```

```python
import functools

import jax
import jax.numpy as jnp
from jax import lax
from jax.experimental import pallas as pl
from jax.experimental.pallas import tpu as pltpu
from jax.sharding import PartitionSpec as P

H = 16
KVH = 4
HD = 128
BLOCK = 64


NEG_FILL = -1e30


def passed_along(value, axis, steps):
    count = lax.axis_size(axis)
    pairs = [(source, (source + steps) % count) for source in range(count)]
    return lax.ppermute(value, axis, pairs)


def shifted_open(value, axis, steps):
    count = lax.axis_size(axis)
    pairs = [(source, source + steps) for source in range(count) if 0 <= source + steps < count]
    return lax.ppermute(value, axis, pairs)


def block_masks(random_rows, global_row, ctx_index, piece_count, tok_rows):
    query_blocks, head_count, block_count = random_rows.shape
    shifts = jnp.arange(piece_count, dtype=jnp.int32)
    key_shard = ctx_index - shifts
    query_ids = ctx_index * query_blocks + jnp.arange(query_blocks, dtype=jnp.int32)
    key_ids = key_shard[:, None] * query_blocks + jnp.arange(query_blocks, dtype=jnp.int32)[None, :]
    safe_ids = jnp.clip(key_ids, 0, block_count - 1).reshape(-1)
    random_part = jnp.take(random_rows, safe_ids, axis=2).reshape(
        query_blocks, head_count, piece_count, query_blocks
    )
    random_part = jnp.transpose(random_part, (2, 1, 0, 3)) > 0
    query_global = jnp.any(query_ids[:, None] == global_row[None, :], axis=1)
    key_global = jnp.any(key_ids[:, :, None] == global_row[None, None, :], axis=2)
    nearby = jnp.abs(query_ids[None, :, None] - key_ids[:, None, :]) <= 1
    fixed_part = nearby | query_global[None, :, None] | key_global[:, None, :]
    table = (random_part | fixed_part[:, None, :, :]) & (key_shard >= 0)[:, None, None, None]
    expanded = jnp.repeat(table, tok_rows // query_blocks, axis=3)
    return expanded.astype(jnp.float32)


def piece_allowed(mask_rows, shift, tok_rows):
    query_blocks = mask_rows.shape[0]
    row = lax.broadcasted_iota(jnp.int32, (tok_rows, tok_rows), 0)
    picked = jnp.broadcast_to(mask_rows[0:1, :], (tok_rows, tok_rows))
    for block in range(1, query_blocks):
        picked = jnp.where(row // BLOCK == block, mask_rows[block : block + 1, :], picked)
    allowed = picked > 0.5
    if shift == 0:
        col = lax.broadcasted_iota(jnp.int32, (tok_rows, tok_rows), 1)
        allowed = allowed & (col <= row)
    return allowed


def dot_nt(a, b):
    return lax.dot_general(a, b, (((1,), (1,)), ((), ())), preferred_element_type=jnp.float32)


def dot_tn(a, b):
    return lax.dot_general(a, b, (((0,), (0,)), ((), ())), preferred_element_type=jnp.float32)


def forward_kernel(piece_count, group_size, query_ref, kv_ref, mask_ref, out_ref, lse_ref, score_ref):
    tok_rows = query_ref.shape[0]
    score_scale = HD ** (-0.5)
    for head in range(group_size):
        cols = slice(head * HD, (head + 1) * HD)
        query_head = query_ref[:, cols]
        row_high = jnp.full((tok_rows, 1), NEG_FILL, jnp.float32)
        for shift in range(piece_count):
            raw = dot_nt(query_head, kv_ref[shift, 0]) * score_scale
            score_ref[shift] = raw
            allowed = piece_allowed(mask_ref[shift, head], shift, tok_rows)
            row_high = jnp.maximum(
                row_high, jnp.max(jnp.where(allowed, raw, NEG_FILL), axis=1, keepdims=True)
            )
        row_total = jnp.zeros((tok_rows, 1), jnp.float32)
        accumulated = jnp.zeros((tok_rows, HD), jnp.float32)
        for shift in range(piece_count):
            allowed = piece_allowed(mask_ref[shift, head], shift, tok_rows)
            weights = jnp.where(allowed, jnp.exp(score_ref[shift] - row_high), 0.0)
            row_total = row_total + jnp.sum(weights, axis=1, keepdims=True)
            accumulated = accumulated + jnp.dot(
                weights.astype(jnp.bfloat16), kv_ref[shift, 1], preferred_element_type=jnp.float32
            )
        out_ref[:, cols] = (accumulated / row_total).astype(out_ref.dtype)
        lse_ref[0, :, head : head + 1] = row_high + jnp.log(row_total)


def backward_kernel(
    piece_count, group_size, query_ref, grad_ref, out_ref, kv_ref, mask_ref, lse_ref,
    dq_ref, dkv_ref, dk_acc, dv_acc,
):
    tok_rows = query_ref.shape[0]
    score_scale = HD ** (-0.5)
    for head in range(group_size):
        cols = slice(head * HD, (head + 1) * HD)
        query_head = query_ref[:, cols]
        grad_head = grad_ref[:, cols]
        delta = jnp.sum(
            grad_head.astype(jnp.float32) * out_ref[:, cols].astype(jnp.float32), axis=1, keepdims=True
        )
        log_total = lse_ref[0, :, head : head + 1]
        query_accum = jnp.zeros((tok_rows, HD), jnp.float32)
        for shift in range(piece_count):
            key_piece = kv_ref[shift, 0]
            value_piece = kv_ref[shift, 1]
            raw = dot_nt(query_head, key_piece) * score_scale
            allowed = piece_allowed(mask_ref[shift, head], shift, tok_rows)
            row_probs = jnp.where(allowed, jnp.exp(raw - log_total), 0.0)
            value_term = dot_tn(row_probs.astype(jnp.bfloat16), grad_head)
            prob_grads = dot_nt(grad_head, value_piece)
            score_grads = (row_probs * (prob_grads - delta)).astype(jnp.bfloat16)
            query_accum = query_accum + jnp.dot(
                score_grads, key_piece, preferred_element_type=jnp.float32
            )
            key_term = dot_tn(score_grads, query_head)
            if head == 0:
                dk_acc[shift] = key_term
                dv_acc[shift] = value_term
            else:
                dk_acc[shift] = dk_acc[shift] + key_term
                dv_acc[shift] = dv_acc[shift] + value_term
        dq_ref[:, cols] = (query_accum * score_scale).astype(dq_ref.dtype)
    for shift in range(piece_count):
        dkv_ref[shift, 0] = (dk_acc[shift] * score_scale).astype(dkv_ref.dtype)
        dkv_ref[shift, 1] = dv_acc[shift].astype(dkv_ref.dtype)


def attention_forward(query_rows, kv_pieces, masks):
    tok_rows, query_width = query_rows.shape
    piece_count = kv_pieces.shape[0]
    group_size = H // KVH
    group_width = group_size * HD
    flops = 4 * tok_rows * tok_rows * HD * H * piece_count
    return pl.pallas_call(
        functools.partial(forward_kernel, piece_count, group_size),
        grid=(KVH,),
        in_specs=[
            pl.BlockSpec((tok_rows, group_width), lambda g: (0, g)),
            pl.BlockSpec((piece_count, 2, tok_rows, HD), lambda g: (0, 0, 0, g)),
            pl.BlockSpec((piece_count, group_size) + masks.shape[2:], lambda g: (0, g, 0, 0)),
        ],
        out_specs=[
            pl.BlockSpec((tok_rows, group_width), lambda g: (0, g)),
            pl.BlockSpec((1, tok_rows, group_size), lambda g: (g, 0, 0)),
        ],
        out_shape=[
            jax.ShapeDtypeStruct((tok_rows, query_width), jnp.bfloat16),
            jax.ShapeDtypeStruct((KVH, tok_rows, group_size), jnp.float32),
        ],
        scratch_shapes=[pltpu.VMEM((piece_count, tok_rows, tok_rows), jnp.float32)],
        cost_estimate=pl.CostEstimate(
            flops=flops,
            transcendentals=tok_rows * tok_rows * H * piece_count,
            bytes_accessed=2 * query_rows.size * 2 + kv_pieces.size * 2,
        ),
    )(query_rows, kv_pieces, masks)


def attention_backward(query_rows, grad_rows, attended, kv_pieces, masks, log_total):
    tok_rows, query_width = query_rows.shape
    piece_count = kv_pieces.shape[0]
    group_size = H // KVH
    group_width = group_size * HD
    flops = 10 * tok_rows * tok_rows * HD * H * piece_count
    return pl.pallas_call(
        functools.partial(backward_kernel, piece_count, group_size),
        grid=(KVH,),
        in_specs=[
            pl.BlockSpec((tok_rows, group_width), lambda g: (0, g)),
            pl.BlockSpec((tok_rows, group_width), lambda g: (0, g)),
            pl.BlockSpec((tok_rows, group_width), lambda g: (0, g)),
            pl.BlockSpec((piece_count, 2, tok_rows, HD), lambda g: (0, 0, 0, g)),
            pl.BlockSpec((piece_count, group_size) + masks.shape[2:], lambda g: (0, g, 0, 0)),
            pl.BlockSpec((1, tok_rows, group_size), lambda g: (g, 0, 0)),
        ],
        out_specs=[
            pl.BlockSpec((tok_rows, group_width), lambda g: (0, g)),
            pl.BlockSpec((piece_count, 2, tok_rows, HD), lambda g: (0, 0, 0, g)),
        ],
        out_shape=[
            jax.ShapeDtypeStruct((tok_rows, query_width), jnp.bfloat16),
            jax.ShapeDtypeStruct(kv_pieces.shape, jnp.bfloat16),
        ],
        scratch_shapes=[
            pltpu.VMEM((piece_count, tok_rows, HD), jnp.float32),
            pltpu.VMEM((piece_count, tok_rows, HD), jnp.float32),
        ],
        cost_estimate=pl.CostEstimate(
            flops=flops,
            transcendentals=tok_rows * tok_rows * H * piece_count,
            bytes_accessed=4 * query_rows.size * 2 + 2 * kv_pieces.size * 2,
        ),
    )(query_rows, grad_rows, attended, kv_pieces, masks, log_total)


def local(query, keys, values, grad_out, random_blocks, global_ids):
    tok_rows = query.shape[1]
    ctx_count = lax.axis_size("ctx")
    ctx_index = lax.axis_index("ctx")
    masks = block_masks(random_blocks[0], global_ids[0], ctx_index, ctx_count, tok_rows)

    own = jnp.stack([keys[0], values[0]])
    pieces = [own] + [shifted_open(own, "ctx", shift) for shift in range(1, ctx_count)]
    kv_pieces = jnp.stack(pieces)

    attended, log_total = attention_forward(query[0], kv_pieces, masks)
    next_input = passed_along(attended[None], "pipe", 1)

    query_grad, kv_terms = attention_backward(
        query[0], grad_out[0], attended, kv_pieces, masks, log_total
    )
    grad_query = passed_along(query_grad[None], "pipe", -1)

    kv_sum = kv_terms[0].astype(jnp.float32)
    for shift in range(1, ctx_count):
        kv_sum = kv_sum + shifted_open(kv_terms[shift], "ctx", -shift).astype(jnp.float32)
    returned = passed_along(kv_sum.astype(jnp.bfloat16), "pipe", -1)
    grad_key = returned[0:1]
    grad_value = returned[1:2]
    return (next_input, grad_query, grad_key, grad_value)


def solution(mesh):
    placed = (
        P(("dp", "pipe"), "ctx", None),
        P(("dp", "pipe"), "ctx", None),
        P(("dp", "pipe"), "ctx", None),
        P(("dp", "pipe"), "ctx", None),
        P("pipe", "ctx", None, None),
        P("pipe", None),
    )
    return jax.shard_map(
        local,
        mesh=mesh,
        in_specs=placed,
        out_specs=(
            P(("dp", "pipe"), "ctx", None),
            P(("dp", "pipe"), "ctx", None),
            P(("dp", "pipe"), "ctx", None),
            P(("dp", "pipe"), "ctx", None),
        ),
        check_vma=False,
    )
```

```python
import functools

import jax
import jax.numpy as jnp
from jax import lax
from jax.experimental import pallas as pl
from jax.experimental.pallas import tpu as pltpu
from jax.sharding import PartitionSpec as P

H = 16
KVH = 4
HD = 128
BLOCK = 64


NEG_FILL = -1e30


def passed_along(value, axis, steps):
    count = lax.axis_size(axis)
    pairs = [(source, (source + steps) % count) for source in range(count)]
    return lax.ppermute(value, axis, pairs)


def shifted_open(value, axis, steps):
    count = lax.axis_size(axis)
    pairs = [(source, source + steps) for source in range(count) if 0 <= source + steps < count]
    return lax.ppermute(value, axis, pairs)


def block_masks(random_rows, global_row, ctx_index, piece_count, tok_rows):
    query_blocks, head_count, block_count = random_rows.shape
    shifts = jnp.arange(piece_count, dtype=jnp.int32)
    key_shard = ctx_index - shifts
    query_ids = ctx_index * query_blocks + jnp.arange(query_blocks, dtype=jnp.int32)
    key_ids = key_shard[:, None] * query_blocks + jnp.arange(query_blocks, dtype=jnp.int32)[None, :]
    safe_ids = jnp.clip(key_ids, 0, block_count - 1).reshape(-1)
    random_part = jnp.take(random_rows, safe_ids, axis=2).reshape(
        query_blocks, head_count, piece_count, query_blocks
    )
    random_part = jnp.transpose(random_part, (2, 1, 0, 3)) > 0
    query_global = jnp.any(query_ids[:, None] == global_row[None, :], axis=1)
    key_global = jnp.any(key_ids[:, :, None] == global_row[None, None, :], axis=2)
    nearby = jnp.abs(query_ids[None, :, None] - key_ids[:, None, :]) <= 1
    fixed_part = nearby | query_global[None, :, None] | key_global[:, None, :]
    table = (random_part | fixed_part[:, None, :, :]) & (key_shard >= 0)[:, None, None, None]
    expanded = jnp.repeat(table, tok_rows // query_blocks, axis=3)
    return expanded.astype(jnp.float32)


def piece_allowed(mask_ref, shift, group_size, tok_rows):
    query_blocks = mask_ref.shape[2]
    rows = group_size * tok_rows
    row = lax.broadcasted_iota(jnp.int32, (rows, tok_rows), 0)
    row_block = row // BLOCK
    picked = jnp.broadcast_to(mask_ref[shift, 0, 0:1, :], (rows, tok_rows))
    for head in range(group_size):
        for block in range(query_blocks):
            if head == 0 and block == 0:
                continue
            picked = jnp.where(
                row_block == head * query_blocks + block,
                mask_ref[shift, head, block : block + 1, :],
                picked,
            )
    allowed = picked > 0.5
    if shift == 0:
        col = lax.broadcasted_iota(jnp.int32, (rows, tok_rows), 1)
        allowed = allowed & (col <= row % tok_rows)
    return allowed


def dot_nt(a, b):
    return lax.dot_general(a, b, (((1,), (1,)), ((), ())), preferred_element_type=jnp.float32)


def dot_tn(a, b):
    return lax.dot_general(a, b, (((0,), (0,)), ((), ())), preferred_element_type=jnp.float32)


def stacked(ref, group_size):
    return jnp.concatenate([ref[:, head * HD : (head + 1) * HD] for head in range(group_size)], axis=0)


def forward_kernel(
    piece_count, group_size, query_ref, grad_ref, kv_ref, mask_ref, out_ref, lse_ref, delta_ref, score_ref
):
    tok_rows = query_ref.shape[0]
    rows = group_size * tok_rows
    score_scale = HD ** (-0.5)
    query_rows = stacked(query_ref, group_size)
    row_high = jnp.full((rows, 1), NEG_FILL, jnp.float32)
    for shift in range(piece_count):
        raw = dot_nt(query_rows, kv_ref[shift, 0]) * score_scale
        score_ref[shift] = raw
        allowed = piece_allowed(mask_ref, shift, group_size, tok_rows)
        row_high = jnp.maximum(
            row_high, jnp.max(jnp.where(allowed, raw, NEG_FILL), axis=1, keepdims=True)
        )
    row_total = jnp.zeros((rows, 1), jnp.float32)
    accumulated = jnp.zeros((rows, HD), jnp.float32)
    for shift in range(piece_count):
        allowed = piece_allowed(mask_ref, shift, group_size, tok_rows)
        weights = jnp.where(allowed, jnp.exp(score_ref[shift] - row_high), 0.0)
        row_total = row_total + jnp.sum(weights, axis=1, keepdims=True)
        accumulated = accumulated + jnp.dot(
            weights.astype(jnp.bfloat16), kv_ref[shift, 1], preferred_element_type=jnp.float32
        )
    attended = (accumulated / row_total).astype(out_ref.dtype)
    for head in range(group_size):
        out_ref[:, head * HD : (head + 1) * HD] = attended[head * tok_rows : (head + 1) * tok_rows]
    lse_ref[0] = row_high + jnp.log(row_total)
    grad_rows = stacked(grad_ref, group_size)
    delta_ref[0] = jnp.sum(
        grad_rows.astype(jnp.float32) * attended.astype(jnp.float32), axis=1, keepdims=True
    )


def backward_kernel(
    piece_count, group_size, query_ref, grad_ref, kv_ref, mask_ref, lse_ref, delta_ref, *rest
):
    dq_ref, dkv_ref = rest[-2:]
    tok_rows = query_ref.shape[0]
    score_scale = HD ** (-0.5)
    query_rows = stacked(query_ref, group_size)
    grad_rows = stacked(grad_ref, group_size)
    log_total = lse_ref[0]
    delta = delta_ref[0]
    query_accum = None
    for shift in range(piece_count):
        key_piece = kv_ref[shift, 0]
        value_piece = kv_ref[shift, 1]
        raw = dot_nt(query_rows, key_piece) * score_scale
        allowed = piece_allowed(mask_ref, shift, group_size, tok_rows)
        row_probs = jnp.where(allowed, jnp.exp(raw - log_total), 0.0)
        dkv_ref[shift, 1] = dot_tn(row_probs.astype(jnp.bfloat16), grad_rows).astype(dkv_ref.dtype)
        prob_grads = dot_nt(grad_rows, value_piece)
        score_grads = (row_probs * (prob_grads - delta)).astype(jnp.bfloat16)
        part_q = jnp.dot(score_grads, key_piece, preferred_element_type=jnp.float32)
        query_accum = part_q if query_accum is None else query_accum + part_q
        dkv_ref[shift, 0] = (dot_tn(score_grads, query_rows) * score_scale).astype(dkv_ref.dtype)
    query_grad = (query_accum * score_scale).astype(dq_ref.dtype)
    for head in range(group_size):
        dq_ref[:, head * HD : (head + 1) * HD] = query_grad[head * tok_rows : (head + 1) * tok_rows]


def attention_forward(query_rows, grad_rows, kv_pieces, masks):
    tok_rows, query_width = query_rows.shape
    piece_count = kv_pieces.shape[0]
    group_size = H // KVH
    group_width = group_size * HD
    rows = group_size * tok_rows
    flops = 4 * tok_rows * tok_rows * HD * H * piece_count
    return pl.pallas_call(
        functools.partial(forward_kernel, piece_count, group_size),
        grid=(KVH,),
        in_specs=[
            pl.BlockSpec((tok_rows, group_width), lambda g: (0, g)),
            pl.BlockSpec((tok_rows, group_width), lambda g: (0, g)),
            pl.BlockSpec((piece_count, 2, tok_rows, HD), lambda g: (0, 0, 0, g)),
            pl.BlockSpec((piece_count, group_size) + masks.shape[2:], lambda g: (0, g, 0, 0)),
        ],
        out_specs=[
            pl.BlockSpec((tok_rows, group_width), lambda g: (0, g)),
            pl.BlockSpec((1, rows, 1), lambda g: (g, 0, 0)),
            pl.BlockSpec((1, rows, 1), lambda g: (g, 0, 0)),
        ],
        out_shape=[
            jax.ShapeDtypeStruct((tok_rows, query_width), jnp.bfloat16),
            jax.ShapeDtypeStruct((KVH, rows, 1), jnp.float32),
            jax.ShapeDtypeStruct((KVH, rows, 1), jnp.float32),
        ],
        scratch_shapes=[pltpu.VMEM((piece_count, rows, tok_rows), jnp.float32)],
        cost_estimate=pl.CostEstimate(
            flops=flops,
            transcendentals=tok_rows * tok_rows * H * piece_count,
            bytes_accessed=3 * query_rows.size * 2 + kv_pieces.size * 2,
        ),
    )(query_rows, grad_rows, kv_pieces, masks)


def attention_backward(query_rows, grad_rows, kv_pieces, masks, log_total, delta, first_group, group_count, extra):
    tok_rows, query_width = query_rows.shape
    piece_count = kv_pieces.shape[0]
    group_size = H // KVH
    group_width = group_size * HD
    rows = group_size * tok_rows
    flops = 10 * tok_rows * tok_rows * HD * group_size * group_count * piece_count
    aliases = {}
    if extra and extra[0] is not None:
        aliases = {6: 0, 7: 1}
    else:
        extra = extra[1:] if extra else extra
    shift_g = lambda g: g + first_group
    return pl.pallas_call(
        functools.partial(backward_kernel, piece_count, group_size),
        grid=(group_count,),
        in_specs=[
            pl.BlockSpec((tok_rows, group_width), lambda g: (0, shift_g(g))),
            pl.BlockSpec((tok_rows, group_width), lambda g: (0, shift_g(g))),
            pl.BlockSpec((piece_count, 2, tok_rows, HD), lambda g: (0, 0, 0, shift_g(g))),
            pl.BlockSpec((piece_count, group_size) + masks.shape[2:], lambda g: (0, shift_g(g), 0, 0)),
            pl.BlockSpec((1, rows, 1), lambda g: (shift_g(g), 0, 0)),
            pl.BlockSpec((1, rows, 1), lambda g: (shift_g(g), 0, 0)),
        ]
        + [pl.BlockSpec(memory_space=pl.ANY) for _ in extra],
        out_specs=[
            pl.BlockSpec((tok_rows, group_width), lambda g: (0, shift_g(g))),
            pl.BlockSpec((piece_count, 2, tok_rows, HD), lambda g: (0, 0, 0, shift_g(g))),
        ],
        out_shape=[
            jax.ShapeDtypeStruct((tok_rows, query_width), jnp.bfloat16),
            jax.ShapeDtypeStruct(kv_pieces.shape, jnp.bfloat16),
        ],
        input_output_aliases=aliases,
        cost_estimate=pl.CostEstimate(
            flops=flops,
            transcendentals=tok_rows * tok_rows * group_size * group_count * piece_count,
            bytes_accessed=(2 * query_rows.size * 2 + 2 * kv_pieces.size * 2) * group_count // KVH,
        ),
    )(query_rows, grad_rows, kv_pieces, masks, log_total, delta, *extra)


def local(query, keys, values, grad_out, random_blocks, global_ids):
    tok_rows = query.shape[1]
    ctx_count = lax.axis_size("ctx")
    ctx_index = lax.axis_index("ctx")
    masks = block_masks(random_blocks[0], global_ids[0], ctx_index, ctx_count, tok_rows)

    own = jnp.stack([keys[0], values[0]])
    pieces = [own] + [shifted_open(own, "ctx", shift) for shift in range(1, ctx_count)]
    kv_pieces = jnp.stack(pieces)

    attended, log_total, delta = attention_forward(query[0], grad_out[0], kv_pieces, masks)
    next_input = passed_along(attended[None], "pipe", 1)

    half = KVH // 2
    first_dq, first_dkv = attention_backward(
        query[0], grad_out[0], kv_pieces, masks, log_total, delta, 0, half, [None]
    )
    query_grad, kv_terms = attention_backward(
        query[0], grad_out[0], kv_pieces, masks, log_total, delta, half, KVH - half,
        [first_dq, first_dkv, next_input],
    )
    grad_query = passed_along(query_grad[None], "pipe", -1)

    kv_sum = kv_terms[0].astype(jnp.float32)
    for shift in range(1, ctx_count):
        kv_sum = kv_sum + shifted_open(kv_terms[shift], "ctx", -shift).astype(jnp.float32)
    returned = passed_along(kv_sum.astype(jnp.bfloat16), "pipe", -1)
    grad_key = returned[0:1]
    grad_value = returned[1:2]
    return (next_input, grad_query, grad_key, grad_value)


def solution(mesh):
    placed = (
        P(("dp", "pipe"), "ctx", None),
        P(("dp", "pipe"), "ctx", None),
        P(("dp", "pipe"), "ctx", None),
        P(("dp", "pipe"), "ctx", None),
        P("pipe", "ctx", None, None),
        P("pipe", None),
    )
    return jax.shard_map(
        local,
        mesh=mesh,
        in_specs=placed,
        out_specs=(
            P(("dp", "pipe"), "ctx", None),
            P(("dp", "pipe"), "ctx", None),
            P(("dp", "pipe"), "ctx", None),
            P(("dp", "pipe"), "ctx", None),
        ),
        check_vma=False,
    )
```

```python
import functools

import jax
import jax.numpy as jnp
from jax import lax
from jax.experimental import pallas as pl
from jax.experimental.pallas import tpu as pltpu
from jax.sharding import PartitionSpec as P

H = 16
KVH = 4
HD = 128
BLOCK = 64


NEG_FILL = -1e30


def passed_along(value, axis, steps):
    count = lax.axis_size(axis)
    pairs = [(source, (source + steps) % count) for source in range(count)]
    return lax.ppermute(value, axis, pairs)


def shifted_open(value, axis, steps):
    count = lax.axis_size(axis)
    pairs = [(source, source + steps) for source in range(count) if 0 <= source + steps < count]
    return lax.ppermute(value, axis, pairs)


def block_masks(random_rows, global_row, ctx_index, piece_count, tok_rows):
    query_blocks, head_count, block_count = random_rows.shape
    shifts = jnp.arange(piece_count, dtype=jnp.int32)
    key_shard = ctx_index - shifts
    query_ids = ctx_index * query_blocks + jnp.arange(query_blocks, dtype=jnp.int32)
    key_ids = key_shard[:, None] * query_blocks + jnp.arange(query_blocks, dtype=jnp.int32)[None, :]
    safe_ids = jnp.clip(key_ids, 0, block_count - 1).reshape(-1)
    random_part = jnp.take(random_rows, safe_ids, axis=2).reshape(
        query_blocks, head_count, piece_count, query_blocks
    )
    random_part = jnp.transpose(random_part, (2, 1, 0, 3)) > 0
    query_global = jnp.any(query_ids[:, None] == global_row[None, :], axis=1)
    key_global = jnp.any(key_ids[:, :, None] == global_row[None, None, :], axis=2)
    nearby = jnp.abs(query_ids[None, :, None] - key_ids[:, None, :]) <= 1
    fixed_part = nearby | query_global[None, :, None] | key_global[:, None, :]
    table = (random_part | fixed_part[:, None, :, :]) & (key_shard >= 0)[:, None, None, None]
    expanded = jnp.repeat(table, tok_rows // query_blocks, axis=3)
    return expanded.astype(jnp.float32)


def piece_allowed(mask_ref, shift, group_size, tok_rows):
    query_blocks = mask_ref.shape[2]
    rows = group_size * tok_rows
    row = lax.broadcasted_iota(jnp.int32, (rows, tok_rows), 0)
    row_block = row // BLOCK
    picked = jnp.broadcast_to(mask_ref[shift, 0, 0:1, :], (rows, tok_rows))
    for head in range(group_size):
        for block in range(query_blocks):
            if head == 0 and block == 0:
                continue
            picked = jnp.where(
                row_block == head * query_blocks + block,
                mask_ref[shift, head, block : block + 1, :],
                picked,
            )
    allowed = picked > 0.5
    if shift == 0:
        col = lax.broadcasted_iota(jnp.int32, (rows, tok_rows), 1)
        allowed = allowed & (col <= row % tok_rows)
    return allowed


def dot_nt(a, b):
    return lax.dot_general(a, b, (((1,), (1,)), ((), ())), preferred_element_type=jnp.float32)


def dot_tn(a, b):
    return lax.dot_general(a, b, (((0,), (0,)), ((), ())), preferred_element_type=jnp.float32)


def stacked(ref, group_size):
    return jnp.concatenate([ref[:, head * HD : (head + 1) * HD] for head in range(group_size)], axis=0)


def forward_kernel(
    piece_count, group_size, query_ref, grad_ref, kv_ref, mask_ref, out_ref, lse_ref, delta_ref, score_ref
):
    tok_rows = query_ref.shape[0]
    rows = group_size * tok_rows
    score_scale = HD ** (-0.5)
    query_rows = stacked(query_ref, group_size)
    row_high = jnp.full((rows, 1), NEG_FILL, jnp.float32)
    for shift in range(piece_count):
        raw = dot_nt(query_rows, kv_ref[shift, 0]) * score_scale
        score_ref[shift] = raw
        allowed = piece_allowed(mask_ref, shift, group_size, tok_rows)
        row_high = jnp.maximum(
            row_high, jnp.max(jnp.where(allowed, raw, NEG_FILL), axis=1, keepdims=True)
        )
    row_total = jnp.zeros((rows, 1), jnp.float32)
    accumulated = jnp.zeros((rows, HD), jnp.float32)
    for shift in range(piece_count):
        allowed = piece_allowed(mask_ref, shift, group_size, tok_rows)
        weights = jnp.where(allowed, jnp.exp(score_ref[shift] - row_high), 0.0)
        row_total = row_total + jnp.sum(weights, axis=1, keepdims=True)
        accumulated = accumulated + jnp.dot(
            weights.astype(jnp.bfloat16), kv_ref[shift, 1], preferred_element_type=jnp.float32
        )
    attended = (accumulated / row_total).astype(out_ref.dtype)
    for head in range(group_size):
        out_ref[:, head * HD : (head + 1) * HD] = attended[head * tok_rows : (head + 1) * tok_rows]
    lse_ref[0] = row_high + jnp.log(row_total)
    grad_rows = stacked(grad_ref, group_size)
    delta_ref[0] = jnp.sum(
        grad_rows.astype(jnp.float32) * attended.astype(jnp.float32), axis=1, keepdims=True
    )


def backward_kernel(
    piece_count, group_size, query_ref, grad_ref, kv_ref, mask_ref, lse_ref, delta_ref, *rest
):
    dq_ref, dkv_ref = rest[-2:]
    tok_rows = query_ref.shape[0]
    score_scale = HD ** (-0.5)
    query_rows = stacked(query_ref, group_size)
    grad_rows = stacked(grad_ref, group_size)
    log_total = lse_ref[0]
    delta = delta_ref[0]
    query_accum = None
    for shift in range(piece_count):
        key_piece = kv_ref[shift, 0]
        value_piece = kv_ref[shift, 1]
        raw = dot_nt(query_rows, key_piece) * score_scale
        allowed = piece_allowed(mask_ref, shift, group_size, tok_rows)
        row_probs = jnp.where(allowed, jnp.exp(raw - log_total), 0.0)
        dkv_ref[shift, 1] = dot_tn(row_probs.astype(jnp.bfloat16), grad_rows).astype(dkv_ref.dtype)
        prob_grads = dot_nt(grad_rows, value_piece)
        score_grads = (row_probs * (prob_grads - delta)).astype(jnp.bfloat16)
        part_q = jnp.dot(score_grads, key_piece, preferred_element_type=jnp.float32)
        query_accum = part_q if query_accum is None else query_accum + part_q
        dkv_ref[shift, 0] = (dot_tn(score_grads, query_rows) * score_scale).astype(dkv_ref.dtype)
    query_grad = (query_accum * score_scale).astype(dq_ref.dtype)
    for head in range(group_size):
        dq_ref[:, head * HD : (head + 1) * HD] = query_grad[head * tok_rows : (head + 1) * tok_rows]


def attention_forward(query_rows, grad_rows, kv_pieces, masks):
    tok_rows, query_width = query_rows.shape
    piece_count = kv_pieces.shape[0]
    group_size = H // KVH
    group_width = group_size * HD
    rows = group_size * tok_rows
    flops = 4 * tok_rows * tok_rows * HD * H * piece_count
    return pl.pallas_call(
        functools.partial(forward_kernel, piece_count, group_size),
        grid=(KVH,),
        in_specs=[
            pl.BlockSpec((tok_rows, group_width), lambda g: (0, g)),
            pl.BlockSpec((tok_rows, group_width), lambda g: (0, g)),
            pl.BlockSpec((piece_count, 2, tok_rows, HD), lambda g: (0, 0, 0, g)),
            pl.BlockSpec((piece_count, group_size) + masks.shape[2:], lambda g: (0, g, 0, 0)),
        ],
        out_specs=[
            pl.BlockSpec((tok_rows, group_width), lambda g: (0, g)),
            pl.BlockSpec((1, rows, 1), lambda g: (g, 0, 0)),
            pl.BlockSpec((1, rows, 1), lambda g: (g, 0, 0)),
        ],
        out_shape=[
            jax.ShapeDtypeStruct((tok_rows, query_width), jnp.bfloat16),
            jax.ShapeDtypeStruct((KVH, rows, 1), jnp.float32),
            jax.ShapeDtypeStruct((KVH, rows, 1), jnp.float32),
        ],
        scratch_shapes=[pltpu.VMEM((piece_count, rows, tok_rows), jnp.float32)],
        cost_estimate=pl.CostEstimate(
            flops=flops,
            transcendentals=tok_rows * tok_rows * H * piece_count,
            bytes_accessed=3 * query_rows.size * 2 + kv_pieces.size * 2,
        ),
    )(query_rows, grad_rows, kv_pieces, masks)


def attention_backward(query_rows, grad_rows, kv_pieces, masks, log_total, delta, first_group, group_count, extra):
    tok_rows, query_width = query_rows.shape
    piece_count = kv_pieces.shape[0]
    group_size = H // KVH
    group_width = group_size * HD
    rows = group_size * tok_rows
    flops = 10 * tok_rows * tok_rows * HD * group_size * group_count * piece_count
    aliases = {}
    if extra and extra[0] is not None:
        aliases = {6: 0, 7: 1}
    else:
        extra = extra[1:] if extra else extra
    shift_g = lambda g: g + first_group
    return pl.pallas_call(
        functools.partial(backward_kernel, piece_count, group_size),
        grid=(group_count,),
        in_specs=[
            pl.BlockSpec((tok_rows, group_width), lambda g: (0, shift_g(g))),
            pl.BlockSpec((tok_rows, group_width), lambda g: (0, shift_g(g))),
            pl.BlockSpec((piece_count, 2, tok_rows, HD), lambda g: (0, 0, 0, shift_g(g))),
            pl.BlockSpec((piece_count, group_size) + masks.shape[2:], lambda g: (0, shift_g(g), 0, 0)),
            pl.BlockSpec((1, rows, 1), lambda g: (shift_g(g), 0, 0)),
            pl.BlockSpec((1, rows, 1), lambda g: (shift_g(g), 0, 0)),
        ]
        + [pl.BlockSpec(memory_space=pl.ANY) for _ in extra],
        out_specs=[
            pl.BlockSpec((tok_rows, group_width), lambda g: (0, shift_g(g))),
            pl.BlockSpec((piece_count, 2, tok_rows, HD), lambda g: (0, 0, 0, shift_g(g))),
        ],
        out_shape=[
            jax.ShapeDtypeStruct((tok_rows, query_width), jnp.bfloat16),
            jax.ShapeDtypeStruct(kv_pieces.shape, jnp.bfloat16),
        ],
        input_output_aliases=aliases,
        cost_estimate=pl.CostEstimate(
            flops=flops,
            transcendentals=tok_rows * tok_rows * group_size * group_count * piece_count,
            bytes_accessed=(2 * query_rows.size * 2 + 2 * kv_pieces.size * 2) * group_count // KVH,
        ),
    )(query_rows, grad_rows, kv_pieces, masks, log_total, delta, *extra)


def local(query, keys, values, grad_out, random_blocks, global_ids):
    tok_rows = query.shape[1]
    ctx_count = lax.axis_size("ctx")
    ctx_index = lax.axis_index("ctx")
    masks = block_masks(random_blocks[0], global_ids[0], ctx_index, ctx_count, tok_rows)

    own = jnp.stack([keys[0], values[0]])
    pieces = [own]
    for shift in range(1, ctx_count):
        pieces.append(shifted_open(pieces[-1], "ctx", 1))
    kv_pieces = jnp.stack(pieces)

    attended, log_total, delta = attention_forward(query[0], grad_out[0], kv_pieces, masks)
    next_input = passed_along(attended[None], "pipe", 1)

    query_grad, kv_terms = attention_backward(
        query[0], grad_out[0], kv_pieces, masks, log_total, delta, 0, KVH, [None]
    )
    next_input, kv_terms = lax.optimization_barrier((next_input, kv_terms))
    grad_query = passed_along(query_grad[None], "pipe", -1)

    carried = None
    for step in range(1, ctx_count):
        part = kv_terms[ctx_count - step].astype(jnp.float32)
        if carried is not None:
            part = part + carried.astype(jnp.float32)
        carried = shifted_open(part.astype(jnp.bfloat16), "ctx", -1)
    kv_sum = kv_terms[0].astype(jnp.float32)
    if carried is not None:
        grad_query, carried = lax.optimization_barrier((grad_query, carried))
        kv_sum = kv_sum + carried.astype(jnp.float32)
    returned = passed_along(kv_sum.astype(jnp.bfloat16), "pipe", -1)
    grad_key = returned[0:1]
    grad_value = returned[1:2]
    return (next_input, grad_query, grad_key, grad_value)


def solution(mesh):
    placed = (
        P(("dp", "pipe"), "ctx", None),
        P(("dp", "pipe"), "ctx", None),
        P(("dp", "pipe"), "ctx", None),
        P(("dp", "pipe"), "ctx", None),
        P("pipe", "ctx", None, None),
        P("pipe", None),
    )
    return jax.shard_map(
        local,
        mesh=mesh,
        in_specs=placed,
        out_specs=(
            P(("dp", "pipe"), "ctx", None),
            P(("dp", "pipe"), "ctx", None),
            P(("dp", "pipe"), "ctx", None),
            P(("dp", "pipe"), "ctx", None),
        ),
        check_vma=False,
    )
```

```python
import functools

import jax
import jax.numpy as jnp
from jax import lax
from jax.experimental import pallas as pl
from jax.experimental.pallas import tpu as pltpu
from jax.sharding import PartitionSpec as P

H = 16
KVH = 4
HD = 128
BLOCK = 64


NEG_FILL = -1e30


def passed_along(value, axis, steps):
    count = lax.axis_size(axis)
    pairs = [(source, (source + steps) % count) for source in range(count)]
    return lax.ppermute(value, axis, pairs)


def shifted_open(value, axis, steps):
    count = lax.axis_size(axis)
    pairs = [(source, source + steps) for source in range(count) if 0 <= source + steps < count]
    return lax.ppermute(value, axis, pairs)


def block_masks(random_rows, global_row, ctx_index, piece_count, tok_rows):
    query_blocks, head_count, block_count = random_rows.shape
    shifts = jnp.arange(piece_count, dtype=jnp.int32)
    key_shard = ctx_index - shifts
    query_ids = ctx_index * query_blocks + jnp.arange(query_blocks, dtype=jnp.int32)
    key_ids = key_shard[:, None] * query_blocks + jnp.arange(query_blocks, dtype=jnp.int32)[None, :]
    safe_ids = jnp.clip(key_ids, 0, block_count - 1).reshape(-1)
    random_part = jnp.take(random_rows, safe_ids, axis=2).reshape(
        query_blocks, head_count, piece_count, query_blocks
    )
    random_part = jnp.transpose(random_part, (2, 1, 0, 3)) > 0
    query_global = jnp.any(query_ids[:, None] == global_row[None, :], axis=1)
    key_global = jnp.any(key_ids[:, :, None] == global_row[None, None, :], axis=2)
    nearby = jnp.abs(query_ids[None, :, None] - key_ids[:, None, :]) <= 1
    fixed_part = nearby | query_global[None, :, None] | key_global[:, None, :]
    table = (random_part | fixed_part[:, None, :, :]) & (key_shard >= 0)[:, None, None, None]
    expanded = jnp.repeat(table, tok_rows // query_blocks, axis=3)
    return expanded.astype(jnp.float32)


def piece_allowed(mask_ref, shift, group_size, tok_rows):
    query_blocks = mask_ref.shape[2]
    rows = group_size * tok_rows
    row = lax.broadcasted_iota(jnp.int32, (rows, tok_rows), 0)
    row_block = row // BLOCK
    picked = jnp.broadcast_to(mask_ref[shift, 0, 0:1, :], (rows, tok_rows))
    for head in range(group_size):
        for block in range(query_blocks):
            if head == 0 and block == 0:
                continue
            picked = jnp.where(
                row_block == head * query_blocks + block,
                mask_ref[shift, head, block : block + 1, :],
                picked,
            )
    allowed = picked > 0.5
    if shift == 0:
        col = lax.broadcasted_iota(jnp.int32, (rows, tok_rows), 1)
        allowed = allowed & (col <= row % tok_rows)
    return allowed


def dot_nt(a, b):
    return lax.dot_general(a, b, (((1,), (1,)), ((), ())), preferred_element_type=jnp.float32)


def dot_tn(a, b):
    return lax.dot_general(a, b, (((0,), (0,)), ((), ())), preferred_element_type=jnp.float32)


def stacked(ref, group_size):
    return jnp.concatenate([ref[:, head * HD : (head + 1) * HD] for head in range(group_size)], axis=0)


def forward_kernel(
    piece_count, group_size, query_ref, grad_ref, kv_ref, mask_ref, out_ref, lse_ref, delta_ref, score_ref
):
    tok_rows = query_ref.shape[0]
    rows = group_size * tok_rows
    score_scale = HD ** (-0.5)
    query_rows = stacked(query_ref, group_size)
    row_high = jnp.full((rows, 1), NEG_FILL, jnp.float32)
    for shift in range(piece_count):
        raw = dot_nt(query_rows, kv_ref[shift, 0]) * score_scale
        score_ref[shift] = raw
        allowed = piece_allowed(mask_ref, shift, group_size, tok_rows)
        row_high = jnp.maximum(
            row_high, jnp.max(jnp.where(allowed, raw, NEG_FILL), axis=1, keepdims=True)
        )
    row_total = jnp.zeros((rows, 1), jnp.float32)
    accumulated = jnp.zeros((rows, HD), jnp.float32)
    for shift in range(piece_count):
        allowed = piece_allowed(mask_ref, shift, group_size, tok_rows)
        weights = jnp.where(allowed, jnp.exp(score_ref[shift] - row_high), 0.0)
        row_total = row_total + jnp.sum(weights, axis=1, keepdims=True)
        accumulated = accumulated + jnp.dot(
            weights.astype(jnp.bfloat16), kv_ref[shift, 1], preferred_element_type=jnp.float32
        )
    attended = (accumulated / row_total).astype(out_ref.dtype)
    for head in range(group_size):
        out_ref[:, head * HD : (head + 1) * HD] = attended[head * tok_rows : (head + 1) * tok_rows]
    lse_ref[0] = row_high + jnp.log(row_total)
    grad_rows = stacked(grad_ref, group_size)
    delta_ref[0] = jnp.sum(
        grad_rows.astype(jnp.float32) * attended.astype(jnp.float32), axis=1, keepdims=True
    )


def backward_kernel(
    piece_ids, group_size, last, query_ref, grad_ref, kv_ref, mask_ref, lse_ref, delta_ref, *rest
):
    if len(rest) == 3:
        acc_in_ref, dq_ref, dkv_ref = rest[0], rest[-2], rest[-1]
    else:
        acc_in_ref, dq_ref, dkv_ref = None, rest[-2], rest[-1]
    tok_rows = query_ref.shape[0]
    score_scale = HD ** (-0.5)
    query_rows = stacked(query_ref, group_size)
    grad_rows = stacked(grad_ref, group_size)
    log_total = lse_ref[0]
    delta = delta_ref[0]
    query_accum = None if acc_in_ref is None else stacked(acc_in_ref, group_size)
    for place, shift in enumerate(piece_ids):
        key_piece = kv_ref[shift, 0]
        value_piece = kv_ref[shift, 1]
        raw = dot_nt(query_rows, key_piece) * score_scale
        allowed = piece_allowed(mask_ref, shift, group_size, tok_rows)
        row_probs = jnp.where(allowed, jnp.exp(raw - log_total), 0.0)
        dkv_ref[place, 1] = dot_tn(row_probs.astype(jnp.bfloat16), grad_rows).astype(dkv_ref.dtype)
        prob_grads = dot_nt(grad_rows, value_piece)
        score_grads = (row_probs * (prob_grads - delta)).astype(jnp.bfloat16)
        part_q = jnp.dot(score_grads, key_piece, preferred_element_type=jnp.float32)
        query_accum = part_q if query_accum is None else query_accum + part_q
        dkv_ref[place, 0] = (dot_tn(score_grads, query_rows) * score_scale).astype(dkv_ref.dtype)
    if last:
        query_accum = query_accum * score_scale
    query_accum = query_accum.astype(dq_ref.dtype)
    for head in range(group_size):
        dq_ref[:, head * HD : (head + 1) * HD] = query_accum[head * tok_rows : (head + 1) * tok_rows]


def attention_forward(query_rows, grad_rows, kv_pieces, masks):
    tok_rows, query_width = query_rows.shape
    piece_count = kv_pieces.shape[0]
    group_size = H // KVH
    group_width = group_size * HD
    rows = group_size * tok_rows
    flops = 4 * tok_rows * tok_rows * HD * H * piece_count
    return pl.pallas_call(
        functools.partial(forward_kernel, piece_count, group_size),
        grid=(KVH,),
        in_specs=[
            pl.BlockSpec((tok_rows, group_width), lambda g: (0, g)),
            pl.BlockSpec((tok_rows, group_width), lambda g: (0, g)),
            pl.BlockSpec((piece_count, 2, tok_rows, HD), lambda g: (0, 0, 0, g)),
            pl.BlockSpec((piece_count, group_size) + masks.shape[2:], lambda g: (0, g, 0, 0)),
        ],
        out_specs=[
            pl.BlockSpec((tok_rows, group_width), lambda g: (0, g)),
            pl.BlockSpec((1, rows, 1), lambda g: (g, 0, 0)),
            pl.BlockSpec((1, rows, 1), lambda g: (g, 0, 0)),
        ],
        out_shape=[
            jax.ShapeDtypeStruct((tok_rows, query_width), jnp.bfloat16),
            jax.ShapeDtypeStruct((KVH, rows, 1), jnp.float32),
            jax.ShapeDtypeStruct((KVH, rows, 1), jnp.float32),
        ],
        scratch_shapes=[pltpu.VMEM((piece_count, rows, tok_rows), jnp.float32)],
        cost_estimate=pl.CostEstimate(
            flops=flops,
            transcendentals=tok_rows * tok_rows * H * piece_count,
            bytes_accessed=3 * query_rows.size * 2 + kv_pieces.size * 2,
        ),
    )(query_rows, grad_rows, kv_pieces, masks)


def attention_backward(query_rows, grad_rows, kv_pieces, masks, log_total, delta, piece_ids, acc_in, last):
    tok_rows, query_width = query_rows.shape
    piece_count = kv_pieces.shape[0]
    group_size = H // KVH
    group_width = group_size * HD
    rows = group_size * tok_rows
    flops = 10 * tok_rows * tok_rows * HD * H * len(piece_ids)
    group_block = pl.BlockSpec((tok_rows, group_width), lambda g: (0, g))
    extra = [] if acc_in is None else [acc_in]
    return pl.pallas_call(
        functools.partial(backward_kernel, tuple(piece_ids), group_size, last),
        grid=(KVH,),
        in_specs=[
            group_block,
            group_block,
            pl.BlockSpec((piece_count, 2, tok_rows, HD), lambda g: (0, 0, 0, g)),
            pl.BlockSpec((piece_count, group_size) + masks.shape[2:], lambda g: (0, g, 0, 0)),
            pl.BlockSpec((1, rows, 1), lambda g: (g, 0, 0)),
            pl.BlockSpec((1, rows, 1), lambda g: (g, 0, 0)),
        ]
        + [group_block for _ in extra],
        out_specs=[
            group_block,
            pl.BlockSpec((len(piece_ids), 2, tok_rows, HD), lambda g: (0, 0, 0, g)),
        ],
        out_shape=[
            jax.ShapeDtypeStruct((tok_rows, query_width), jnp.bfloat16 if last else jnp.float32),
            jax.ShapeDtypeStruct((len(piece_ids),) + kv_pieces.shape[1:], jnp.bfloat16),
        ],
        cost_estimate=pl.CostEstimate(
            flops=flops,
            transcendentals=tok_rows * tok_rows * H * len(piece_ids),
            bytes_accessed=2 * query_rows.size * 2 + 2 * kv_pieces.size * 2 * len(piece_ids) // piece_count,
        ),
    )(query_rows, grad_rows, kv_pieces, masks, log_total, delta, *extra)


def local(query, keys, values, grad_out, random_blocks, global_ids):
    tok_rows = query.shape[1]
    ctx_count = lax.axis_size("ctx")
    ctx_index = lax.axis_index("ctx")
    masks = block_masks(random_blocks[0], global_ids[0], ctx_index, ctx_count, tok_rows)

    own = jnp.stack([keys[0], values[0]])
    pieces = [own]
    for shift in range(1, ctx_count):
        pieces.append(shifted_open(pieces[-1], "ctx", 1))
    kv_pieces = jnp.stack(pieces)

    attended, log_total, delta = attention_forward(query[0], grad_out[0], kv_pieces, masks)
    next_input = passed_along(attended[None], "pipe", 1)

    acc = None
    carried = None
    for step in range(1, ctx_count):
        shift = ctx_count - step
        acc, term = attention_backward(
            query[0], grad_out[0], kv_pieces, masks, log_total, delta, [shift], acc, False
        )
        if step == min(2, ctx_count - 1):
            next_input, term = lax.optimization_barrier((next_input, term))
        part = term[0].astype(jnp.float32)
        if carried is not None:
            part = part + carried.astype(jnp.float32)
        carried = shifted_open(part.astype(jnp.bfloat16), "ctx", -1)
    query_grad, kv_own = attention_backward(
        query[0], grad_out[0], kv_pieces, masks, log_total, delta, [0], acc, True
    )
    grad_query = passed_along(query_grad[None], "pipe", -1)
    kv_terms = kv_own

    kv_sum = kv_terms[0].astype(jnp.float32)
    if carried is not None:
        grad_query, carried = lax.optimization_barrier((grad_query, carried))
        kv_sum = kv_sum + carried.astype(jnp.float32)
    returned = passed_along(kv_sum.astype(jnp.bfloat16), "pipe", -1)
    grad_key = returned[0:1]
    grad_value = returned[1:2]
    return (next_input, grad_query, grad_key, grad_value)


def solution(mesh):
    placed = (
        P(("dp", "pipe"), "ctx", None),
        P(("dp", "pipe"), "ctx", None),
        P(("dp", "pipe"), "ctx", None),
        P(("dp", "pipe"), "ctx", None),
        P("pipe", "ctx", None, None),
        P("pipe", None),
    )
    return jax.shard_map(
        local,
        mesh=mesh,
        in_specs=placed,
        out_specs=(
            P(("dp", "pipe"), "ctx", None),
            P(("dp", "pipe"), "ctx", None),
            P(("dp", "pipe"), "ctx", None),
            P(("dp", "pipe"), "ctx", None),
        ),
        check_vma=False,
    )
```

```python
import functools

import jax
import jax.numpy as jnp
from jax import lax
from jax.experimental import pallas as pl
from jax.experimental.pallas import tpu as pltpu
from jax.sharding import PartitionSpec as P

H = 16
KVH = 4
HD = 128
BLOCK = 64


NEG_FILL = -1e30


def passed_along(value, axis, steps):
    count = lax.axis_size(axis)
    pairs = [(source, (source + steps) % count) for source in range(count)]
    return lax.ppermute(value, axis, pairs)


def shifted_open(value, axis, steps):
    count = lax.axis_size(axis)
    pairs = [(source, source + steps) for source in range(count) if 0 <= source + steps < count]
    return lax.ppermute(value, axis, pairs)


def block_masks(random_rows, global_row, ctx_index, piece_count, tok_rows):
    query_blocks, head_count, block_count = random_rows.shape
    shifts = jnp.arange(piece_count, dtype=jnp.int32)
    key_shard = ctx_index - shifts
    query_ids = ctx_index * query_blocks + jnp.arange(query_blocks, dtype=jnp.int32)
    key_ids = key_shard[:, None] * query_blocks + jnp.arange(query_blocks, dtype=jnp.int32)[None, :]
    safe_ids = jnp.clip(key_ids, 0, block_count - 1).reshape(-1)
    random_part = jnp.take(random_rows, safe_ids, axis=2).reshape(
        query_blocks, head_count, piece_count, query_blocks
    )
    random_part = jnp.transpose(random_part, (2, 1, 0, 3)) > 0
    query_global = jnp.any(query_ids[:, None] == global_row[None, :], axis=1)
    key_global = jnp.any(key_ids[:, :, None] == global_row[None, None, :], axis=2)
    nearby = jnp.abs(query_ids[None, :, None] - key_ids[:, None, :]) <= 1
    fixed_part = nearby | query_global[None, :, None] | key_global[:, None, :]
    table = (random_part | fixed_part[:, None, :, :]) & (key_shard >= 0)[:, None, None, None]
    expanded = jnp.repeat(table, tok_rows // query_blocks, axis=3)
    return expanded.astype(jnp.float32)


def piece_allowed(mask_ref, shift, group_size, tok_rows):
    query_blocks = mask_ref.shape[2]
    rows = group_size * tok_rows
    parts = [
        jnp.broadcast_to(mask_ref[shift, head, block : block + 1, :], (tok_rows // query_blocks, tok_rows))
        for head in range(group_size)
        for block in range(query_blocks)
    ]
    allowed = jnp.concatenate(parts, axis=0) > 0.5
    if shift == 0:
        row = lax.broadcasted_iota(jnp.int32, (rows, tok_rows), 0)
        col = lax.broadcasted_iota(jnp.int32, (rows, tok_rows), 1)
        allowed = allowed & (col <= row % tok_rows)
    return allowed


def dot_nt(a, b):
    return lax.dot_general(a, b, (((1,), (1,)), ((), ())), preferred_element_type=jnp.float32)


def dot_tn(a, b):
    return lax.dot_general(a, b, (((0,), (0,)), ((), ())), preferred_element_type=jnp.float32)


def stacked(ref, group_size):
    return jnp.concatenate([ref[:, head * HD : (head + 1) * HD] for head in range(group_size)], axis=0)


def forward_kernel(
    piece_count, group_size, query_ref, grad_ref, kv_ref, mask_ref, out_ref, lse_ref, delta_ref, score_ref
):
    tok_rows = query_ref.shape[0]
    rows = group_size * tok_rows
    score_scale = HD ** (-0.5)
    query_rows = stacked(query_ref, group_size)
    row_high = jnp.full((rows, 1), NEG_FILL, jnp.float32)
    for shift in range(piece_count):
        raw = dot_nt(query_rows, kv_ref[shift, 0]) * score_scale
        allowed = piece_allowed(mask_ref, shift, group_size, tok_rows)
        masked = jnp.where(allowed, raw, NEG_FILL)
        score_ref[shift] = masked
        row_high = jnp.maximum(row_high, jnp.max(masked, axis=1, keepdims=True))
    row_total = jnp.zeros((rows, 1), jnp.float32)
    accumulated = jnp.zeros((rows, HD), jnp.float32)
    for shift in range(piece_count):
        weights = jnp.exp(score_ref[shift] - row_high)
        row_total = row_total + jnp.sum(weights, axis=1, keepdims=True)
        accumulated = accumulated + jnp.dot(
            weights.astype(jnp.bfloat16), kv_ref[shift, 1], preferred_element_type=jnp.float32
        )
    attended = (accumulated / row_total).astype(out_ref.dtype)
    for head in range(group_size):
        out_ref[:, head * HD : (head + 1) * HD] = attended[head * tok_rows : (head + 1) * tok_rows]
    lse_ref[0] = row_high + jnp.log(row_total)
    grad_rows = stacked(grad_ref, group_size)
    delta_ref[0] = jnp.sum(
        grad_rows.astype(jnp.float32) * attended.astype(jnp.float32), axis=1, keepdims=True
    )


def backward_kernel(
    piece_count, group_size, query_ref, grad_ref, kv_ref, mask_ref, lse_ref, delta_ref, *rest
):
    dq_ref, dkv_ref = rest[-2:]
    tok_rows = query_ref.shape[0]
    score_scale = HD ** (-0.5)
    query_rows = stacked(query_ref, group_size)
    grad_rows = stacked(grad_ref, group_size)
    log_total = lse_ref[0]
    delta = delta_ref[0]
    query_accum = None
    for shift in range(piece_count):
        key_piece = kv_ref[shift, 0]
        value_piece = kv_ref[shift, 1]
        raw = dot_nt(query_rows, key_piece) * score_scale
        allowed = piece_allowed(mask_ref, shift, group_size, tok_rows)
        row_probs = jnp.exp(jnp.where(allowed, raw, NEG_FILL) - log_total)
        dkv_ref[shift, 1] = dot_tn(row_probs.astype(jnp.bfloat16), grad_rows).astype(dkv_ref.dtype)
        prob_grads = dot_nt(grad_rows, value_piece)
        score_grads = (row_probs * (prob_grads - delta)).astype(jnp.bfloat16)
        part_q = jnp.dot(score_grads, key_piece, preferred_element_type=jnp.float32)
        query_accum = part_q if query_accum is None else query_accum + part_q
        dkv_ref[shift, 0] = (dot_tn(score_grads, query_rows) * score_scale).astype(dkv_ref.dtype)
    query_grad = (query_accum * score_scale).astype(dq_ref.dtype)
    for head in range(group_size):
        dq_ref[:, head * HD : (head + 1) * HD] = query_grad[head * tok_rows : (head + 1) * tok_rows]


def attention_forward(query_rows, grad_rows, kv_pieces, masks):
    tok_rows, query_width = query_rows.shape
    piece_count = kv_pieces.shape[0]
    group_size = H // KVH
    group_width = group_size * HD
    rows = group_size * tok_rows
    flops = 4 * tok_rows * tok_rows * HD * H * piece_count
    return pl.pallas_call(
        functools.partial(forward_kernel, piece_count, group_size),
        grid=(KVH,),
        in_specs=[
            pl.BlockSpec((tok_rows, group_width), lambda g: (0, g)),
            pl.BlockSpec((tok_rows, group_width), lambda g: (0, g)),
            pl.BlockSpec((piece_count, 2, tok_rows, HD), lambda g: (0, 0, 0, g)),
            pl.BlockSpec((piece_count, group_size) + masks.shape[2:], lambda g: (0, g, 0, 0)),
        ],
        out_specs=[
            pl.BlockSpec((tok_rows, group_width), lambda g: (0, g)),
            pl.BlockSpec((1, rows, 1), lambda g: (g, 0, 0)),
            pl.BlockSpec((1, rows, 1), lambda g: (g, 0, 0)),
        ],
        out_shape=[
            jax.ShapeDtypeStruct((tok_rows, query_width), jnp.bfloat16),
            jax.ShapeDtypeStruct((KVH, rows, 1), jnp.float32),
            jax.ShapeDtypeStruct((KVH, rows, 1), jnp.float32),
        ],
        scratch_shapes=[pltpu.VMEM((piece_count, rows, tok_rows), jnp.float32)],
        cost_estimate=pl.CostEstimate(
            flops=flops,
            transcendentals=tok_rows * tok_rows * H * piece_count,
            bytes_accessed=3 * query_rows.size * 2 + kv_pieces.size * 2,
        ),
    )(query_rows, grad_rows, kv_pieces, masks)


def attention_backward(query_rows, grad_rows, kv_pieces, masks, log_total, delta, first_group, group_count, extra):
    tok_rows, query_width = query_rows.shape
    piece_count = kv_pieces.shape[0]
    group_size = H // KVH
    group_width = group_size * HD
    rows = group_size * tok_rows
    flops = 10 * tok_rows * tok_rows * HD * group_size * group_count * piece_count
    aliases = {}
    if extra and extra[0] is not None:
        aliases = {6: 0, 7: 1}
    else:
        extra = extra[1:] if extra else extra
    shift_g = lambda g: g + first_group
    return pl.pallas_call(
        functools.partial(backward_kernel, piece_count, group_size),
        grid=(group_count,),
        in_specs=[
            pl.BlockSpec((tok_rows, group_width), lambda g: (0, shift_g(g))),
            pl.BlockSpec((tok_rows, group_width), lambda g: (0, shift_g(g))),
            pl.BlockSpec((piece_count, 2, tok_rows, HD), lambda g: (0, 0, 0, shift_g(g))),
            pl.BlockSpec((piece_count, group_size) + masks.shape[2:], lambda g: (0, shift_g(g), 0, 0)),
            pl.BlockSpec((1, rows, 1), lambda g: (shift_g(g), 0, 0)),
            pl.BlockSpec((1, rows, 1), lambda g: (shift_g(g), 0, 0)),
        ]
        + [pl.BlockSpec(memory_space=pl.ANY) for _ in extra],
        out_specs=[
            pl.BlockSpec((tok_rows, group_width), lambda g: (0, shift_g(g))),
            pl.BlockSpec((piece_count, 2, tok_rows, HD), lambda g: (0, 0, 0, shift_g(g))),
        ],
        out_shape=[
            jax.ShapeDtypeStruct((tok_rows, query_width), jnp.bfloat16),
            jax.ShapeDtypeStruct(kv_pieces.shape, jnp.bfloat16),
        ],
        input_output_aliases=aliases,
        cost_estimate=pl.CostEstimate(
            flops=flops,
            transcendentals=tok_rows * tok_rows * group_size * group_count * piece_count,
            bytes_accessed=(2 * query_rows.size * 2 + 2 * kv_pieces.size * 2) * group_count // KVH,
        ),
    )(query_rows, grad_rows, kv_pieces, masks, log_total, delta, *extra)


def local(query, keys, values, grad_out, random_blocks, global_ids):
    tok_rows = query.shape[1]
    ctx_count = lax.axis_size("ctx")
    ctx_index = lax.axis_index("ctx")
    masks = block_masks(random_blocks[0], global_ids[0], ctx_index, ctx_count, tok_rows)

    own = jnp.stack([keys[0], values[0]])
    pieces = [own]
    for shift in range(1, ctx_count):
        pieces.append(shifted_open(pieces[-1], "ctx", 1))
    kv_pieces = jnp.stack(pieces)

    attended, log_total, delta = attention_forward(query[0], grad_out[0], kv_pieces, masks)
    next_input = passed_along(attended[None], "pipe", 1)

    query_grad, kv_terms = attention_backward(
        query[0], grad_out[0], kv_pieces, masks, log_total, delta, 0, KVH, [None]
    )
    next_input, kv_terms = lax.optimization_barrier((next_input, kv_terms))
    grad_query = passed_along(query_grad[None], "pipe", -1)

    carried = None
    for step in range(1, ctx_count):
        part = kv_terms[ctx_count - step].astype(jnp.float32)
        if carried is not None:
            part = part + carried.astype(jnp.float32)
        carried = shifted_open(part.astype(jnp.bfloat16), "ctx", -1)
    kv_sum = kv_terms[0].astype(jnp.float32)
    if carried is not None:
        grad_query, carried = lax.optimization_barrier((grad_query, carried))
        kv_sum = kv_sum + carried.astype(jnp.float32)
    returned = passed_along(kv_sum.astype(jnp.bfloat16), "pipe", -1)
    grad_key = returned[0:1]
    grad_value = returned[1:2]
    return (next_input, grad_query, grad_key, grad_value)


def solution(mesh):
    placed = (
        P(("dp", "pipe"), "ctx", None),
        P(("dp", "pipe"), "ctx", None),
        P(("dp", "pipe"), "ctx", None),
        P(("dp", "pipe"), "ctx", None),
        P("pipe", "ctx", None, None),
        P("pipe", None),
    )
    return jax.shard_map(
        local,
        mesh=mesh,
        in_specs=placed,
        out_specs=(
            P(("dp", "pipe"), "ctx", None),
            P(("dp", "pipe"), "ctx", None),
            P(("dp", "pipe"), "ctx", None),
            P(("dp", "pipe"), "ctx", None),
        ),
        check_vma=False,
    )
```

```python
import functools

import jax
import jax.numpy as jnp
from jax import lax
from jax.experimental import pallas as pl
from jax.experimental.pallas import tpu as pltpu
from jax.sharding import PartitionSpec as P

H = 16
KVH = 4
HD = 128
BLOCK = 64


NEG_FILL = -1e30


def passed_along(value, axis, steps):
    count = lax.axis_size(axis)
    pairs = [(source, (source + steps) % count) for source in range(count)]
    return lax.ppermute(value, axis, pairs)


def shifted_open(value, axis, steps):
    count = lax.axis_size(axis)
    pairs = [(source, source + steps) for source in range(count) if 0 <= source + steps < count]
    return lax.ppermute(value, axis, pairs)


def block_masks(random_rows, global_row, ctx_index, piece_count, tok_rows):
    query_blocks, head_count, block_count = random_rows.shape
    shifts = jnp.arange(piece_count, dtype=jnp.int32)
    key_shard = ctx_index - shifts
    query_ids = ctx_index * query_blocks + jnp.arange(query_blocks, dtype=jnp.int32)
    key_ids = key_shard[:, None] * query_blocks + jnp.arange(query_blocks, dtype=jnp.int32)[None, :]
    safe_ids = jnp.clip(key_ids, 0, block_count - 1).reshape(-1)
    random_part = jnp.take(random_rows, safe_ids, axis=2).reshape(
        query_blocks, head_count, piece_count, query_blocks
    )
    random_part = jnp.transpose(random_part, (2, 1, 0, 3)) > 0
    query_global = jnp.any(query_ids[:, None] == global_row[None, :], axis=1)
    key_global = jnp.any(key_ids[:, :, None] == global_row[None, None, :], axis=2)
    nearby = jnp.abs(query_ids[None, :, None] - key_ids[:, None, :]) <= 1
    fixed_part = nearby | query_global[None, :, None] | key_global[:, None, :]
    table = (random_part | fixed_part[:, None, :, :]) & (key_shard >= 0)[:, None, None, None]
    expanded = jnp.repeat(table, tok_rows // query_blocks, axis=3)
    return expanded.astype(jnp.float32)


def piece_allowed(mask_ref, shift, group_size, tok_rows):
    query_blocks = mask_ref.shape[2]
    rows = group_size * tok_rows
    parts = [
        jnp.broadcast_to(mask_ref[shift, head, block : block + 1, :], (tok_rows // query_blocks, tok_rows))
        for head in range(group_size)
        for block in range(query_blocks)
    ]
    allowed = jnp.concatenate(parts, axis=0) > 0.5
    if shift == 0:
        row = lax.broadcasted_iota(jnp.int32, (rows, tok_rows), 0)
        col = lax.broadcasted_iota(jnp.int32, (rows, tok_rows), 1)
        allowed = allowed & (col <= row % tok_rows)
    return allowed


def dot_nt(a, b):
    return lax.dot_general(a, b, (((1,), (1,)), ((), ())), preferred_element_type=jnp.float32)


def dot_tn(a, b):
    return lax.dot_general(a, b, (((0,), (0,)), ((), ())), preferred_element_type=jnp.float32)


def stacked(ref, group_size):
    return jnp.concatenate([ref[:, head * HD : (head + 1) * HD] for head in range(group_size)], axis=0)


def forward_kernel(
    piece_count, group_size, query_ref, grad_ref, kv_ref, mask_ref, out_ref, lse_ref, delta_ref, score_ref
):
    tok_rows = query_ref.shape[0]
    rows = group_size * tok_rows
    score_scale = HD ** (-0.5)
    query_rows = stacked(query_ref, group_size)
    row_high = jnp.full((rows, 1), NEG_FILL, jnp.float32)
    for shift in range(piece_count):
        raw = dot_nt(query_rows, kv_ref[shift, 0]) * score_scale
        allowed = piece_allowed(mask_ref, shift, group_size, tok_rows)
        masked = jnp.where(allowed, raw, NEG_FILL)
        score_ref[shift] = masked
        row_high = jnp.maximum(row_high, jnp.max(masked, axis=1, keepdims=True))
    row_total = jnp.zeros((rows, 1), jnp.float32)
    accumulated = jnp.zeros((rows, HD), jnp.float32)
    for shift in range(piece_count):
        weights = jnp.exp(score_ref[shift] - row_high)
        row_total = row_total + jnp.sum(weights, axis=1, keepdims=True)
        accumulated = accumulated + jnp.dot(
            weights.astype(jnp.bfloat16), kv_ref[shift, 1], preferred_element_type=jnp.float32
        )
    attended = (accumulated / row_total).astype(out_ref.dtype)
    for head in range(group_size):
        out_ref[:, head * HD : (head + 1) * HD] = attended[head * tok_rows : (head + 1) * tok_rows]
    lse_ref[0] = row_high + jnp.log(row_total)
    grad_rows = stacked(grad_ref, group_size)
    delta_ref[0] = jnp.sum(
        grad_rows.astype(jnp.float32) * attended.astype(jnp.float32), axis=1, keepdims=True
    )


def backward_kernel(
    piece_count, group_size, query_ref, grad_ref, kv_ref, mask_ref, lse_ref, delta_ref, *rest
):
    dq_ref, dkv_ref = rest[-2:]
    tok_rows = query_ref.shape[0]
    score_scale = HD ** (-0.5)
    query_rows = stacked(query_ref, group_size)
    grad_rows = stacked(grad_ref, group_size)
    log_total = lse_ref[0]
    delta = delta_ref[0]
    query_accum = None
    for shift in range(piece_count):
        key_piece = kv_ref[shift, 0]
        value_piece = kv_ref[shift, 1]
        raw = dot_nt(query_rows, key_piece) * score_scale
        allowed = piece_allowed(mask_ref, shift, group_size, tok_rows)
        row_probs = jnp.exp(jnp.where(allowed, raw, NEG_FILL) - log_total)
        dkv_ref[shift, 1] = dot_tn(row_probs.astype(jnp.bfloat16), grad_rows).astype(dkv_ref.dtype)
        prob_grads = dot_nt(grad_rows, value_piece)
        score_grads = (row_probs * (prob_grads - delta)).astype(jnp.bfloat16)
        part_q = jnp.dot(score_grads, key_piece, preferred_element_type=jnp.float32)
        query_accum = part_q if query_accum is None else query_accum + part_q
        dkv_ref[shift, 0] = (dot_tn(score_grads, query_rows) * score_scale).astype(dkv_ref.dtype)
    query_grad = (query_accum * score_scale).astype(dq_ref.dtype)
    for head in range(group_size):
        dq_ref[:, head * HD : (head + 1) * HD] = query_grad[head * tok_rows : (head + 1) * tok_rows]


def attention_forward(query_rows, grad_rows, kv_pieces, masks):
    tok_rows, query_width = query_rows.shape
    piece_count = kv_pieces.shape[0]
    group_size = H // KVH
    group_width = group_size * HD
    rows = group_size * tok_rows
    flops = 4 * tok_rows * tok_rows * HD * H * piece_count
    return pl.pallas_call(
        functools.partial(forward_kernel, piece_count, group_size),
        grid=(KVH,),
        in_specs=[
            pl.BlockSpec((tok_rows, group_width), lambda g: (0, g)),
            pl.BlockSpec((tok_rows, group_width), lambda g: (0, g)),
            pl.BlockSpec((piece_count, 2, tok_rows, HD), lambda g: (0, 0, 0, g)),
            pl.BlockSpec((piece_count, group_size) + masks.shape[2:], lambda g: (0, g, 0, 0)),
        ],
        out_specs=[
            pl.BlockSpec((tok_rows, group_width), lambda g: (0, g)),
            pl.BlockSpec((1, rows, 1), lambda g: (g, 0, 0)),
            pl.BlockSpec((1, rows, 1), lambda g: (g, 0, 0)),
        ],
        out_shape=[
            jax.ShapeDtypeStruct((tok_rows, query_width), jnp.bfloat16),
            jax.ShapeDtypeStruct((KVH, rows, 1), jnp.float32),
            jax.ShapeDtypeStruct((KVH, rows, 1), jnp.float32),
        ],
        scratch_shapes=[pltpu.VMEM((piece_count, rows, tok_rows), jnp.float32)],
        cost_estimate=pl.CostEstimate(
            flops=flops,
            transcendentals=tok_rows * tok_rows * H * piece_count,
            bytes_accessed=3 * query_rows.size * 2 + kv_pieces.size * 2,
        ),
    )(query_rows, grad_rows, kv_pieces, masks)


def attention_backward(query_rows, grad_rows, kv_pieces, masks, log_total, delta, first_group, group_count, extra):
    tok_rows, query_width = query_rows.shape
    piece_count = kv_pieces.shape[0]
    group_size = H // KVH
    group_width = group_size * HD
    rows = group_size * tok_rows
    flops = 10 * tok_rows * tok_rows * HD * group_size * group_count * piece_count
    aliases = {}
    if extra and extra[0] is not None:
        aliases = {6: 0, 7: 1}
    else:
        extra = extra[1:] if extra else extra
    shift_g = lambda g: g + first_group
    return pl.pallas_call(
        functools.partial(backward_kernel, piece_count, group_size),
        grid=(group_count,),
        in_specs=[
            pl.BlockSpec((tok_rows, group_width), lambda g: (0, shift_g(g))),
            pl.BlockSpec((tok_rows, group_width), lambda g: (0, shift_g(g))),
            pl.BlockSpec((piece_count, 2, tok_rows, HD), lambda g: (0, 0, 0, shift_g(g))),
            pl.BlockSpec((piece_count, group_size) + masks.shape[2:], lambda g: (0, shift_g(g), 0, 0)),
            pl.BlockSpec((1, rows, 1), lambda g: (shift_g(g), 0, 0)),
            pl.BlockSpec((1, rows, 1), lambda g: (shift_g(g), 0, 0)),
        ]
        + [pl.BlockSpec(memory_space=pl.ANY) for _ in extra],
        out_specs=[
            pl.BlockSpec((tok_rows, group_width), lambda g: (0, shift_g(g))),
            pl.BlockSpec((piece_count, 2, tok_rows, HD), lambda g: (0, 0, 0, shift_g(g))),
        ],
        out_shape=[
            jax.ShapeDtypeStruct((tok_rows, query_width), jnp.bfloat16),
            jax.ShapeDtypeStruct(kv_pieces.shape, jnp.bfloat16),
        ],
        input_output_aliases=aliases,
        cost_estimate=pl.CostEstimate(
            flops=flops,
            transcendentals=tok_rows * tok_rows * group_size * group_count * piece_count,
            bytes_accessed=(2 * query_rows.size * 2 + 2 * kv_pieces.size * 2) * group_count // KVH,
        ),
    )(query_rows, grad_rows, kv_pieces, masks, log_total, delta, *extra)


def local(query, keys, values, grad_out, random_blocks, global_ids):
    tok_rows = query.shape[1]
    ctx_count = lax.axis_size("ctx")
    ctx_index = lax.axis_index("ctx")
    masks = block_masks(random_blocks[0], global_ids[0], ctx_index, ctx_count, tok_rows)

    own = jnp.stack([keys[0], values[0]])
    if ctx_count == 4:
        step_one = shifted_open(own, "ctx", 1)
        step_three = shifted_open(own, "ctx", 3)
        pieces = [own, step_one, shifted_open(step_one, "ctx", 1), step_three]
    else:
        pieces = [own]
        for shift in range(1, ctx_count):
            pieces.append(shifted_open(pieces[-1], "ctx", 1))
    kv_pieces = jnp.stack(pieces)

    attended, log_total, delta = attention_forward(query[0], grad_out[0], kv_pieces, masks)
    next_input = passed_along(attended[None], "pipe", 1)

    query_grad, kv_terms = attention_backward(
        query[0], grad_out[0], kv_pieces, masks, log_total, delta, 0, KVH, [None]
    )
    next_input, kv_terms = lax.optimization_barrier((next_input, kv_terms))
    grad_query = passed_along(query_grad[None], "pipe", -1)

    carried = None
    for step in range(1, ctx_count):
        part = kv_terms[ctx_count - step].astype(jnp.float32)
        if carried is not None:
            if step == 2:
                next_input = jnp.where(ctx_index < 0, jnp.zeros_like(next_input), next_input)
                next_input, carried = lax.optimization_barrier((next_input, carried))
            part = part + carried.astype(jnp.float32)
        carried = shifted_open(part.astype(jnp.bfloat16), "ctx", -1)
    kv_sum = kv_terms[0].astype(jnp.float32)
    if carried is not None:
        grad_query, carried = lax.optimization_barrier((grad_query, carried))
        kv_sum = kv_sum + carried.astype(jnp.float32)
    returned = passed_along(kv_sum.astype(jnp.bfloat16), "pipe", -1)
    grad_key = returned[0:1]
    grad_value = returned[1:2]
    return (next_input, grad_query, grad_key, grad_value)


def solution(mesh):
    placed = (
        P(("dp", "pipe"), "ctx", None),
        P(("dp", "pipe"), "ctx", None),
        P(("dp", "pipe"), "ctx", None),
        P(("dp", "pipe"), "ctx", None),
        P("pipe", "ctx", None, None),
        P("pipe", None),
    )
    return jax.shard_map(
        local,
        mesh=mesh,
        in_specs=placed,
        out_specs=(
            P(("dp", "pipe"), "ctx", None),
            P(("dp", "pipe"), "ctx", None),
            P(("dp", "pipe"), "ctx", None),
            P(("dp", "pipe"), "ctx", None),
        ),
        check_vma=False,
    )
```

```python
import functools

import jax
import jax.numpy as jnp
from jax import lax
from jax.experimental import pallas as pl
from jax.experimental.pallas import tpu as pltpu
from jax.sharding import PartitionSpec as P

H = 16
KVH = 4
HD = 128
BLOCK = 64


NEG_FILL = -1e30


def passed_along(value, axis, steps):
    count = lax.axis_size(axis)
    pairs = [(source, (source + steps) % count) for source in range(count)]
    return lax.ppermute(value, axis, pairs)


def shifted_open(value, axis, steps):
    count = lax.axis_size(axis)
    pairs = [(source, source + steps) for source in range(count) if 0 <= source + steps < count]
    return lax.ppermute(value, axis, pairs)


def block_masks(random_rows, global_row, ctx_index, piece_count, tok_rows):
    query_blocks, head_count, block_count = random_rows.shape
    shifts = jnp.arange(piece_count, dtype=jnp.int32)
    key_shard = ctx_index - shifts
    query_ids = ctx_index * query_blocks + jnp.arange(query_blocks, dtype=jnp.int32)
    key_ids = key_shard[:, None] * query_blocks + jnp.arange(query_blocks, dtype=jnp.int32)[None, :]
    safe_ids = jnp.clip(key_ids, 0, block_count - 1).reshape(-1)
    random_part = jnp.take(random_rows, safe_ids, axis=2).reshape(
        query_blocks, head_count, piece_count, query_blocks
    )
    random_part = jnp.transpose(random_part, (2, 1, 0, 3)) > 0
    query_global = jnp.any(query_ids[:, None] == global_row[None, :], axis=1)
    key_global = jnp.any(key_ids[:, :, None] == global_row[None, None, :], axis=2)
    nearby = jnp.abs(query_ids[None, :, None] - key_ids[:, None, :]) <= 1
    fixed_part = nearby | query_global[None, :, None] | key_global[:, None, :]
    table = (random_part | fixed_part[:, None, :, :]) & (key_shard >= 0)[:, None, None, None]
    expanded = jnp.repeat(table, tok_rows // query_blocks, axis=3)
    return expanded.astype(jnp.float32)


def piece_allowed(mask_ref, shift, group_size, tok_rows):
    query_blocks = mask_ref.shape[2]
    rows = group_size * tok_rows
    parts = [
        jnp.broadcast_to(mask_ref[shift, head, block : block + 1, :], (tok_rows // query_blocks, tok_rows))
        for head in range(group_size)
        for block in range(query_blocks)
    ]
    allowed = jnp.concatenate(parts, axis=0) > 0.5
    if shift == 0:
        row = lax.broadcasted_iota(jnp.int32, (rows, tok_rows), 0)
        col = lax.broadcasted_iota(jnp.int32, (rows, tok_rows), 1)
        allowed = allowed & (col <= row % tok_rows)
    return allowed


def dot_nt(a, b):
    return lax.dot_general(a, b, (((1,), (1,)), ((), ())), preferred_element_type=jnp.float32)


def dot_tn(a, b):
    return lax.dot_general(a, b, (((0,), (0,)), ((), ())), preferred_element_type=jnp.float32)


def stacked(ref, group_size):
    return jnp.concatenate([ref[:, head * HD : (head + 1) * HD] for head in range(group_size)], axis=0)


def all_allowed(mask_ref, piece_count, group_size, tok_rows):
    return jnp.concatenate(
        [piece_allowed(mask_ref, shift, group_size, tok_rows) for shift in range(piece_count)], axis=1
    )


def forward_kernel(piece_count, group_size, query_ref, grad_ref, kv_ref, mask_ref, out_ref, lse_ref, delta_ref):
    tok_rows = query_ref.shape[0]
    score_scale = HD ** (-0.5)
    query_rows = stacked(query_ref, group_size)
    all_keys = kv_ref[:, 0].reshape(piece_count * tok_rows, HD)
    all_values = kv_ref[:, 1].reshape(piece_count * tok_rows, HD)
    raw = dot_nt(query_rows, all_keys) * score_scale
    masked = jnp.where(all_allowed(mask_ref, piece_count, group_size, tok_rows), raw, NEG_FILL)
    row_high = jnp.max(masked, axis=1, keepdims=True)
    weights = jnp.exp(masked - row_high)
    row_total = jnp.sum(weights, axis=1, keepdims=True)
    accumulated = jnp.dot(weights.astype(jnp.bfloat16), all_values, preferred_element_type=jnp.float32)
    attended = (accumulated / row_total).astype(out_ref.dtype)
    for head in range(group_size):
        out_ref[:, head * HD : (head + 1) * HD] = attended[head * tok_rows : (head + 1) * tok_rows]
    lse_ref[0] = row_high + jnp.log(row_total)
    grad_rows = stacked(grad_ref, group_size)
    delta_ref[0] = jnp.sum(
        grad_rows.astype(jnp.float32) * attended.astype(jnp.float32), axis=1, keepdims=True
    )


def backward_kernel(
    piece_count, group_size, query_ref, grad_ref, kv_ref, mask_ref, lse_ref, delta_ref, *rest
):
    dq_ref, dkv_ref = rest[-2:]
    tok_rows = query_ref.shape[0]
    score_scale = HD ** (-0.5)
    query_rows = stacked(query_ref, group_size)
    grad_rows = stacked(grad_ref, group_size)
    all_keys = kv_ref[:, 0].reshape(piece_count * tok_rows, HD)
    all_values = kv_ref[:, 1].reshape(piece_count * tok_rows, HD)
    raw = dot_nt(query_rows, all_keys) * score_scale
    masked = jnp.where(all_allowed(mask_ref, piece_count, group_size, tok_rows), raw, NEG_FILL)
    row_probs = jnp.exp(masked - lse_ref[0])
    value_terms = dot_tn(row_probs.astype(jnp.bfloat16), grad_rows)
    prob_grads = dot_nt(grad_rows, all_values)
    score_grads = (row_probs * (prob_grads - delta_ref[0])).astype(jnp.bfloat16)
    query_grad = jnp.dot(score_grads, all_keys, preferred_element_type=jnp.float32)
    key_terms = dot_tn(score_grads, query_rows) * score_scale
    dkv_ref[:, 0] = key_terms.reshape(piece_count, tok_rows, HD).astype(dkv_ref.dtype)
    dkv_ref[:, 1] = value_terms.reshape(piece_count, tok_rows, HD).astype(dkv_ref.dtype)
    query_grad = (query_grad * score_scale).astype(dq_ref.dtype)
    for head in range(group_size):
        dq_ref[:, head * HD : (head + 1) * HD] = query_grad[head * tok_rows : (head + 1) * tok_rows]


def attention_forward(query_rows, grad_rows, kv_pieces, masks):
    tok_rows, query_width = query_rows.shape
    piece_count = kv_pieces.shape[0]
    group_size = H // KVH
    group_width = group_size * HD
    rows = group_size * tok_rows
    flops = 4 * tok_rows * tok_rows * HD * H * piece_count
    return pl.pallas_call(
        functools.partial(forward_kernel, piece_count, group_size),
        grid=(KVH,),
        in_specs=[
            pl.BlockSpec((tok_rows, group_width), lambda g: (0, g)),
            pl.BlockSpec((tok_rows, group_width), lambda g: (0, g)),
            pl.BlockSpec((piece_count, 2, tok_rows, HD), lambda g: (0, 0, 0, g)),
            pl.BlockSpec((piece_count, group_size) + masks.shape[2:], lambda g: (0, g, 0, 0)),
        ],
        out_specs=[
            pl.BlockSpec((tok_rows, group_width), lambda g: (0, g)),
            pl.BlockSpec((1, rows, 1), lambda g: (g, 0, 0)),
            pl.BlockSpec((1, rows, 1), lambda g: (g, 0, 0)),
        ],
        out_shape=[
            jax.ShapeDtypeStruct((tok_rows, query_width), jnp.bfloat16),
            jax.ShapeDtypeStruct((KVH, rows, 1), jnp.float32),
            jax.ShapeDtypeStruct((KVH, rows, 1), jnp.float32),
        ],
        cost_estimate=pl.CostEstimate(
            flops=flops,
            transcendentals=tok_rows * tok_rows * H * piece_count,
            bytes_accessed=3 * query_rows.size * 2 + kv_pieces.size * 2,
        ),
    )(query_rows, grad_rows, kv_pieces, masks)


def attention_backward(query_rows, grad_rows, kv_pieces, masks, log_total, delta, first_group, group_count, extra):
    tok_rows, query_width = query_rows.shape
    piece_count = kv_pieces.shape[0]
    group_size = H // KVH
    group_width = group_size * HD
    rows = group_size * tok_rows
    flops = 10 * tok_rows * tok_rows * HD * group_size * group_count * piece_count
    aliases = {}
    if extra and extra[0] is not None:
        aliases = {6: 0, 7: 1}
    else:
        extra = extra[1:] if extra else extra
    shift_g = lambda g: g + first_group
    return pl.pallas_call(
        functools.partial(backward_kernel, piece_count, group_size),
        grid=(group_count,),
        in_specs=[
            pl.BlockSpec((tok_rows, group_width), lambda g: (0, shift_g(g))),
            pl.BlockSpec((tok_rows, group_width), lambda g: (0, shift_g(g))),
            pl.BlockSpec((piece_count, 2, tok_rows, HD), lambda g: (0, 0, 0, shift_g(g))),
            pl.BlockSpec((piece_count, group_size) + masks.shape[2:], lambda g: (0, shift_g(g), 0, 0)),
            pl.BlockSpec((1, rows, 1), lambda g: (shift_g(g), 0, 0)),
            pl.BlockSpec((1, rows, 1), lambda g: (shift_g(g), 0, 0)),
        ]
        + [pl.BlockSpec(memory_space=pl.ANY) for _ in extra],
        out_specs=[
            pl.BlockSpec((tok_rows, group_width), lambda g: (0, shift_g(g))),
            pl.BlockSpec((piece_count, 2, tok_rows, HD), lambda g: (0, 0, 0, shift_g(g))),
        ],
        out_shape=[
            jax.ShapeDtypeStruct((tok_rows, query_width), jnp.bfloat16),
            jax.ShapeDtypeStruct(kv_pieces.shape, jnp.bfloat16),
        ],
        input_output_aliases=aliases,
        cost_estimate=pl.CostEstimate(
            flops=flops,
            transcendentals=tok_rows * tok_rows * group_size * group_count * piece_count,
            bytes_accessed=(2 * query_rows.size * 2 + 2 * kv_pieces.size * 2) * group_count // KVH,
        ),
    )(query_rows, grad_rows, kv_pieces, masks, log_total, delta, *extra)


def local(query, keys, values, grad_out, random_blocks, global_ids):
    tok_rows = query.shape[1]
    ctx_count = lax.axis_size("ctx")
    ctx_index = lax.axis_index("ctx")
    masks = block_masks(random_blocks[0], global_ids[0], ctx_index, ctx_count, tok_rows)

    own = jnp.stack([keys[0], values[0]])
    if ctx_count == 4:
        step_one = shifted_open(own, "ctx", 1)
        step_three = shifted_open(own, "ctx", 3)
        pieces = [own, step_one, shifted_open(step_one, "ctx", 1), step_three]
    else:
        pieces = [own]
        for shift in range(1, ctx_count):
            pieces.append(shifted_open(pieces[-1], "ctx", 1))
    kv_pieces = jnp.stack(pieces)

    attended, log_total, delta = attention_forward(query[0], grad_out[0], kv_pieces, masks)
    next_input = passed_along(attended[None], "pipe", 1)

    query_grad, kv_terms = attention_backward(
        query[0], grad_out[0], kv_pieces, masks, log_total, delta, 0, KVH, [None]
    )
    next_input, kv_terms = lax.optimization_barrier((next_input, kv_terms))
    grad_query = passed_along(query_grad[None], "pipe", -1)

    carried = None
    for step in range(1, ctx_count):
        part = kv_terms[ctx_count - step].astype(jnp.float32)
        if carried is not None:
            if step == 2:
                next_input = jnp.where(ctx_index < 0, jnp.zeros_like(next_input), next_input)
                next_input, carried = lax.optimization_barrier((next_input, carried))
            part = part + carried.astype(jnp.float32)
        carried = shifted_open(part.astype(jnp.bfloat16), "ctx", -1)
    kv_sum = kv_terms[0].astype(jnp.float32)
    if carried is not None:
        grad_query, carried = lax.optimization_barrier((grad_query, carried))
        kv_sum = kv_sum + carried.astype(jnp.float32)
    returned = passed_along(kv_sum.astype(jnp.bfloat16), "pipe", -1)
    grad_key = returned[0:1]
    grad_value = returned[1:2]
    return (next_input, grad_query, grad_key, grad_value)


def solution(mesh):
    placed = (
        P(("dp", "pipe"), "ctx", None),
        P(("dp", "pipe"), "ctx", None),
        P(("dp", "pipe"), "ctx", None),
        P(("dp", "pipe"), "ctx", None),
        P("pipe", "ctx", None, None),
        P("pipe", None),
    )
    return jax.shard_map(
        local,
        mesh=mesh,
        in_specs=placed,
        out_specs=(
            P(("dp", "pipe"), "ctx", None),
            P(("dp", "pipe"), "ctx", None),
            P(("dp", "pipe"), "ctx", None),
            P(("dp", "pipe"), "ctx", None),
        ),
        check_vma=False,
    )
```

```python
import functools

import jax
import jax.numpy as jnp
from jax import lax
from jax.experimental import pallas as pl
from jax.experimental.pallas import tpu as pltpu
from jax.sharding import PartitionSpec as P

H = 16
KVH = 4
HD = 128
BLOCK = 64


NEG_FILL = -1e30


def passed_along(value, axis, steps):
    count = lax.axis_size(axis)
    pairs = [(source, (source + steps) % count) for source in range(count)]
    return lax.ppermute(value, axis, pairs)


def shifted_open(value, axis, steps):
    count = lax.axis_size(axis)
    pairs = [(source, source + steps) for source in range(count) if 0 <= source + steps < count]
    return lax.ppermute(value, axis, pairs)


def block_masks(random_rows, global_row, ctx_index, piece_count, tok_rows):
    query_blocks, head_count, block_count = random_rows.shape
    shifts = jnp.arange(piece_count, dtype=jnp.int32)
    key_shard = ctx_index - shifts
    query_ids = ctx_index * query_blocks + jnp.arange(query_blocks, dtype=jnp.int32)
    key_ids = key_shard[:, None] * query_blocks + jnp.arange(query_blocks, dtype=jnp.int32)[None, :]
    safe_ids = jnp.clip(key_ids, 0, block_count - 1).reshape(-1)
    random_part = jnp.take(random_rows, safe_ids, axis=2).reshape(
        query_blocks, head_count, piece_count, query_blocks
    )
    random_part = jnp.transpose(random_part, (2, 1, 0, 3)) > 0
    query_global = jnp.any(query_ids[:, None] == global_row[None, :], axis=1)
    key_global = jnp.any(key_ids[:, :, None] == global_row[None, None, :], axis=2)
    nearby = jnp.abs(query_ids[None, :, None] - key_ids[:, None, :]) <= 1
    fixed_part = nearby | query_global[None, :, None] | key_global[:, None, :]
    table = (random_part | fixed_part[:, None, :, :]) & (key_shard >= 0)[:, None, None, None]
    expanded = jnp.repeat(table, tok_rows // query_blocks, axis=3)
    return expanded.astype(jnp.float32)


def piece_allowed(mask_ref, shift, group_size, tok_rows):
    query_blocks = mask_ref.shape[2]
    rows = group_size * tok_rows
    parts = [
        jnp.broadcast_to(mask_ref[shift, head, block : block + 1, :], (tok_rows // query_blocks, tok_rows))
        for head in range(group_size)
        for block in range(query_blocks)
    ]
    allowed = jnp.concatenate(parts, axis=0) > 0.5
    if shift == 0:
        row = lax.broadcasted_iota(jnp.int32, (rows, tok_rows), 0)
        col = lax.broadcasted_iota(jnp.int32, (rows, tok_rows), 1)
        allowed = allowed & (col <= row % tok_rows)
    return allowed


def dot_nt(a, b):
    return lax.dot_general(a, b, (((1,), (1,)), ((), ())), preferred_element_type=jnp.float32)


def dot_tn(a, b):
    return lax.dot_general(a, b, (((0,), (0,)), ((), ())), preferred_element_type=jnp.float32)


def stacked(ref, group_size):
    return jnp.concatenate([ref[:, head * HD : (head + 1) * HD] for head in range(group_size)], axis=0)


def all_allowed(mask_ref, piece_count, group_size, tok_rows):
    return jnp.concatenate(
        [piece_allowed(mask_ref, shift, group_size, tok_rows) for shift in range(piece_count)], axis=1
    )


def forward_kernel(piece_count, group_size, query_ref, grad_ref, kv_ref, mask_ref, out_ref, lse_ref, delta_ref):
    tok_rows = query_ref.shape[0]
    score_scale = HD ** (-0.5)
    query_rows = stacked(query_ref, group_size)
    all_keys = kv_ref[:, 0].reshape(piece_count * tok_rows, HD)
    all_values = kv_ref[:, 1].reshape(piece_count * tok_rows, HD)
    raw = dot_nt(query_rows, all_keys) * score_scale
    masked = jnp.where(all_allowed(mask_ref, piece_count, group_size, tok_rows), raw, NEG_FILL)
    row_high = jnp.max(masked, axis=1, keepdims=True)
    weights = jnp.exp(masked - row_high)
    row_total = jnp.sum(weights, axis=1, keepdims=True)
    accumulated = jnp.dot(weights.astype(jnp.bfloat16), all_values, preferred_element_type=jnp.float32)
    attended = (accumulated / row_total).astype(out_ref.dtype)
    for head in range(group_size):
        out_ref[:, head * HD : (head + 1) * HD] = attended[head * tok_rows : (head + 1) * tok_rows]
    lse_ref[0] = row_high + jnp.log(row_total)
    grad_rows = stacked(grad_ref, group_size)
    delta_ref[0] = jnp.sum(
        grad_rows.astype(jnp.float32) * attended.astype(jnp.float32), axis=1, keepdims=True
    )


def backward_kernel(
    piece_count, group_size, query_ref, grad_ref, kv_ref, mask_ref, lse_ref, delta_ref, *rest
):
    dq_ref, dkv_ref = rest[-2:]
    tok_rows = query_ref.shape[0]
    score_scale = HD ** (-0.5)
    query_rows = stacked(query_ref, group_size)
    grad_rows = stacked(grad_ref, group_size)
    all_keys = kv_ref[:, 0].reshape(piece_count * tok_rows, HD)
    all_values = kv_ref[:, 1].reshape(piece_count * tok_rows, HD)
    raw = dot_nt(query_rows, all_keys) * score_scale
    masked = jnp.where(all_allowed(mask_ref, piece_count, group_size, tok_rows), raw, NEG_FILL)
    row_probs = jnp.exp(masked - lse_ref[0])
    value_terms = dot_tn(row_probs.astype(jnp.bfloat16), grad_rows)
    prob_grads = dot_nt(grad_rows, all_values)
    score_grads = (row_probs * (prob_grads - delta_ref[0])).astype(jnp.bfloat16)
    query_grad = jnp.dot(score_grads, all_keys, preferred_element_type=jnp.float32)
    key_terms = dot_tn(score_grads, query_rows) * score_scale
    dkv_ref[:, 0] = key_terms.reshape(piece_count, tok_rows, HD).astype(dkv_ref.dtype)
    dkv_ref[:, 1] = value_terms.reshape(piece_count, tok_rows, HD).astype(dkv_ref.dtype)
    query_grad = (query_grad * score_scale).astype(dq_ref.dtype)
    for head in range(group_size):
        dq_ref[:, head * HD : (head + 1) * HD] = query_grad[head * tok_rows : (head + 1) * tok_rows]


def attention_forward(query_rows, grad_rows, kv_pieces, masks):
    tok_rows, query_width = query_rows.shape
    piece_count = kv_pieces.shape[0]
    group_size = H // KVH
    group_width = group_size * HD
    rows = group_size * tok_rows
    flops = 4 * tok_rows * tok_rows * HD * H * piece_count
    return pl.pallas_call(
        functools.partial(forward_kernel, piece_count, group_size),
        grid=(KVH,),
        in_specs=[
            pl.BlockSpec((tok_rows, group_width), lambda g: (0, g)),
            pl.BlockSpec((tok_rows, group_width), lambda g: (0, g)),
            pl.BlockSpec((piece_count, 2, tok_rows, HD), lambda g: (0, 0, 0, g)),
            pl.BlockSpec((piece_count, group_size) + masks.shape[2:], lambda g: (0, g, 0, 0)),
        ],
        out_specs=[
            pl.BlockSpec((tok_rows, group_width), lambda g: (0, g)),
            pl.BlockSpec((1, rows, 1), lambda g: (g, 0, 0)),
            pl.BlockSpec((1, rows, 1), lambda g: (g, 0, 0)),
        ],
        out_shape=[
            jax.ShapeDtypeStruct((tok_rows, query_width), jnp.bfloat16),
            jax.ShapeDtypeStruct((KVH, rows, 1), jnp.float32),
            jax.ShapeDtypeStruct((KVH, rows, 1), jnp.float32),
        ],
        cost_estimate=pl.CostEstimate(
            flops=flops,
            transcendentals=tok_rows * tok_rows * H * piece_count,
            bytes_accessed=3 * query_rows.size * 2 + kv_pieces.size * 2,
        ),
    )(query_rows, grad_rows, kv_pieces, masks)


def attention_backward(query_rows, grad_rows, kv_pieces, masks, log_total, delta, first_group, group_count, extra):
    tok_rows, query_width = query_rows.shape
    piece_count = kv_pieces.shape[0]
    group_size = H // KVH
    group_width = group_size * HD
    rows = group_size * tok_rows
    flops = 10 * tok_rows * tok_rows * HD * group_size * group_count * piece_count
    aliases = {}
    if extra and extra[0] is not None:
        aliases = {6: 0, 7: 1}
    else:
        extra = extra[1:] if extra else extra
    shift_g = lambda g: g + first_group
    return pl.pallas_call(
        functools.partial(backward_kernel, piece_count, group_size),
        grid=(group_count,),
        in_specs=[
            pl.BlockSpec((tok_rows, group_width), lambda g: (0, shift_g(g))),
            pl.BlockSpec((tok_rows, group_width), lambda g: (0, shift_g(g))),
            pl.BlockSpec((piece_count, 2, tok_rows, HD), lambda g: (0, 0, 0, shift_g(g))),
            pl.BlockSpec((piece_count, group_size) + masks.shape[2:], lambda g: (0, shift_g(g), 0, 0)),
            pl.BlockSpec((1, rows, 1), lambda g: (shift_g(g), 0, 0)),
            pl.BlockSpec((1, rows, 1), lambda g: (shift_g(g), 0, 0)),
        ]
        + [pl.BlockSpec(memory_space=pl.ANY) for _ in extra],
        out_specs=[
            pl.BlockSpec((tok_rows, group_width), lambda g: (0, shift_g(g))),
            pl.BlockSpec((piece_count, 2, tok_rows, HD), lambda g: (0, 0, 0, shift_g(g))),
        ],
        out_shape=[
            jax.ShapeDtypeStruct((tok_rows, query_width), jnp.bfloat16),
            jax.ShapeDtypeStruct(kv_pieces.shape, jnp.bfloat16),
        ],
        input_output_aliases=aliases,
        cost_estimate=pl.CostEstimate(
            flops=flops,
            transcendentals=tok_rows * tok_rows * group_size * group_count * piece_count,
            bytes_accessed=(2 * query_rows.size * 2 + 2 * kv_pieces.size * 2) * group_count // KVH,
        ),
    )(query_rows, grad_rows, kv_pieces, masks, log_total, delta, *extra)


def local(query, keys, values, grad_out, random_blocks, global_ids):
    tok_rows = query.shape[1]
    ctx_count = lax.axis_size("ctx")
    ctx_index = lax.axis_index("ctx")
    masks = block_masks(random_blocks[0], global_ids[0], ctx_index, ctx_count, tok_rows)

    own = jnp.stack([keys[0], values[0]])
    if ctx_count == 4:
        step_one = shifted_open(own, "ctx", 1)
        step_three = shifted_open(own, "ctx", 3)
        pieces = [own, step_one, shifted_open(step_one, "ctx", 1), step_three]
    else:
        pieces = [own]
        for shift in range(1, ctx_count):
            pieces.append(shifted_open(pieces[-1], "ctx", 1))
    kv_pieces = jnp.stack(pieces)

    attended, log_total, delta = attention_forward(query[0], grad_out[0], kv_pieces, masks)
    next_input = passed_along(attended[None], "pipe", 1)

    query_grad, kv_terms = attention_backward(
        query[0], grad_out[0], kv_pieces, masks, log_total, delta, 0, KVH, [None]
    )
    grad_query = passed_along(query_grad[None], "pipe", -1)

    carried = None
    for step in range(1, ctx_count):
        part = kv_terms[ctx_count - step].astype(jnp.float32)
        if carried is not None:
            if step == 2:
                next_input = jnp.where(ctx_index < 0, jnp.zeros_like(next_input), next_input)
                next_input, carried = lax.optimization_barrier((next_input, carried))
            part = part + carried.astype(jnp.float32)
        carried = shifted_open(part.astype(jnp.bfloat16), "ctx", -1)
    kv_sum = kv_terms[0].astype(jnp.float32)
    if carried is not None:
        grad_query, carried = lax.optimization_barrier((grad_query, carried))
        kv_sum = kv_sum + carried.astype(jnp.float32)
    returned = passed_along(kv_sum.astype(jnp.bfloat16), "pipe", -1)
    grad_key = returned[0:1]
    grad_value = returned[1:2]
    return (next_input, grad_query, grad_key, grad_value)


def solution(mesh):
    placed = (
        P(("dp", "pipe"), "ctx", None),
        P(("dp", "pipe"), "ctx", None),
        P(("dp", "pipe"), "ctx", None),
        P(("dp", "pipe"), "ctx", None),
        P("pipe", "ctx", None, None),
        P("pipe", None),
    )
    return jax.shard_map(
        local,
        mesh=mesh,
        in_specs=placed,
        out_specs=(
            P(("dp", "pipe"), "ctx", None),
            P(("dp", "pipe"), "ctx", None),
            P(("dp", "pipe"), "ctx", None),
            P(("dp", "pipe"), "ctx", None),
        ),
        check_vma=False,
    )
```

```python
import functools

import jax
import jax.numpy as jnp
from jax import lax
from jax.experimental import pallas as pl
from jax.experimental.pallas import tpu as pltpu
from jax.sharding import PartitionSpec as P

H = 16
KVH = 4
HD = 128
BLOCK = 64


NEG_FILL = -1e30


def passed_along(value, axis, steps):
    count = lax.axis_size(axis)
    pairs = [(source, (source + steps) % count) for source in range(count)]
    return lax.ppermute(value, axis, pairs)


def shifted_open(value, axis, steps):
    count = lax.axis_size(axis)
    pairs = [(source, source + steps) for source in range(count) if 0 <= source + steps < count]
    return lax.ppermute(value, axis, pairs)


def block_masks(random_rows, global_row, ctx_index, piece_count, tok_rows):
    query_blocks, head_count, block_count = random_rows.shape
    shifts = jnp.arange(piece_count, dtype=jnp.int32)
    key_shard = ctx_index - shifts
    query_ids = ctx_index * query_blocks + jnp.arange(query_blocks, dtype=jnp.int32)
    key_ids = key_shard[:, None] * query_blocks + jnp.arange(query_blocks, dtype=jnp.int32)[None, :]
    safe_ids = jnp.clip(key_ids, 0, block_count - 1).reshape(-1)
    random_part = jnp.take(random_rows, safe_ids, axis=2).reshape(
        query_blocks, head_count, piece_count, query_blocks
    )
    random_part = jnp.transpose(random_part, (2, 1, 0, 3)) > 0
    query_global = jnp.any(query_ids[:, None] == global_row[None, :], axis=1)
    key_global = jnp.any(key_ids[:, :, None] == global_row[None, None, :], axis=2)
    nearby = jnp.abs(query_ids[None, :, None] - key_ids[:, None, :]) <= 1
    fixed_part = nearby | query_global[None, :, None] | key_global[:, None, :]
    table = (random_part | fixed_part[:, None, :, :]) & (key_shard >= 0)[:, None, None, None]
    expanded = jnp.repeat(table, tok_rows // query_blocks, axis=3)
    return expanded.astype(jnp.float32)


def piece_allowed(mask_ref, shift, group_size, tok_rows):
    query_blocks = mask_ref.shape[2]
    rows = group_size * tok_rows
    parts = [
        jnp.broadcast_to(mask_ref[shift, head, block : block + 1, :], (tok_rows // query_blocks, tok_rows))
        for head in range(group_size)
        for block in range(query_blocks)
    ]
    allowed = jnp.concatenate(parts, axis=0) > 0.5
    if shift == 0:
        row = lax.broadcasted_iota(jnp.int32, (rows, tok_rows), 0)
        col = lax.broadcasted_iota(jnp.int32, (rows, tok_rows), 1)
        allowed = allowed & (col <= row % tok_rows)
    return allowed


def dot_nt(a, b):
    return lax.dot_general(a, b, (((1,), (1,)), ((), ())), preferred_element_type=jnp.float32)


def dot_tn(a, b):
    return lax.dot_general(a, b, (((0,), (0,)), ((), ())), preferred_element_type=jnp.float32)


def stacked(ref, group_size):
    return jnp.concatenate([ref[:, head * HD : (head + 1) * HD] for head in range(group_size)], axis=0)


def all_allowed(mask_ref, piece_count, group_size, tok_rows):
    return jnp.concatenate(
        [piece_allowed(mask_ref, shift, group_size, tok_rows) for shift in range(piece_count)], axis=1
    )


def forward_kernel(piece_count, group_size, query_ref, grad_ref, mask_ref, *refs):
    kv_refs = refs[:piece_count]
    out_ref, lse_ref, delta_ref = refs[piece_count:]
    tok_rows = query_ref.shape[0]
    score_scale = HD ** (-0.5)
    query_rows = stacked(query_ref, group_size)
    all_keys = jnp.concatenate([ref[0] for ref in kv_refs], axis=0)
    all_values = jnp.concatenate([ref[1] for ref in kv_refs], axis=0)
    raw = dot_nt(query_rows, all_keys) * score_scale
    masked = jnp.where(all_allowed(mask_ref, piece_count, group_size, tok_rows), raw, NEG_FILL)
    row_high = jnp.max(masked, axis=1, keepdims=True)
    weights = jnp.exp(masked - row_high)
    row_total = jnp.sum(weights, axis=1, keepdims=True)
    accumulated = jnp.dot(weights.astype(jnp.bfloat16), all_values, preferred_element_type=jnp.float32)
    attended = (accumulated / row_total).astype(out_ref.dtype)
    for head in range(group_size):
        out_ref[:, head * HD : (head + 1) * HD] = attended[head * tok_rows : (head + 1) * tok_rows]
    lse_ref[0] = row_high + jnp.log(row_total)
    grad_rows = stacked(grad_ref, group_size)
    delta_ref[0] = jnp.sum(
        grad_rows.astype(jnp.float32) * attended.astype(jnp.float32), axis=1, keepdims=True
    )


def backward_kernel(piece_count, group_size, query_ref, grad_ref, mask_ref, lse_ref, delta_ref, *refs):
    kv_refs = refs[:piece_count]
    dq_ref = refs[piece_count]
    dkv_refs = refs[piece_count + 1 :]
    tok_rows = query_ref.shape[0]
    score_scale = HD ** (-0.5)
    query_rows = stacked(query_ref, group_size)
    grad_rows = stacked(grad_ref, group_size)
    all_keys = jnp.concatenate([ref[0] for ref in kv_refs], axis=0)
    all_values = jnp.concatenate([ref[1] for ref in kv_refs], axis=0)
    raw = dot_nt(query_rows, all_keys) * score_scale
    masked = jnp.where(all_allowed(mask_ref, piece_count, group_size, tok_rows), raw, NEG_FILL)
    row_probs = jnp.exp(masked - lse_ref[0])
    value_terms = dot_tn(row_probs.astype(jnp.bfloat16), grad_rows)
    prob_grads = dot_nt(grad_rows, all_values)
    score_grads = (row_probs * (prob_grads - delta_ref[0])).astype(jnp.bfloat16)
    query_grad = jnp.dot(score_grads, all_keys, preferred_element_type=jnp.float32)
    key_terms = dot_tn(score_grads, query_rows) * score_scale
    for shift, ref in enumerate(dkv_refs):
        piece_rows = slice(shift * tok_rows, (shift + 1) * tok_rows)
        ref[0] = key_terms[piece_rows].astype(ref.dtype)
        ref[1] = value_terms[piece_rows].astype(ref.dtype)
    query_grad = (query_grad * score_scale).astype(dq_ref.dtype)
    for head in range(group_size):
        dq_ref[:, head * HD : (head + 1) * HD] = query_grad[head * tok_rows : (head + 1) * tok_rows]


def attention_forward(query_rows, grad_rows, pieces, masks):
    tok_rows, query_width = query_rows.shape
    piece_count = len(pieces)
    group_size = H // KVH
    group_width = group_size * HD
    rows = group_size * tok_rows
    flops = 4 * tok_rows * tok_rows * HD * H * piece_count
    piece_block = pl.BlockSpec((2, tok_rows, HD), lambda g: (0, 0, g))
    return pl.pallas_call(
        functools.partial(forward_kernel, piece_count, group_size),
        grid=(KVH,),
        in_specs=[
            pl.BlockSpec((tok_rows, group_width), lambda g: (0, g)),
            pl.BlockSpec((tok_rows, group_width), lambda g: (0, g)),
            pl.BlockSpec((piece_count, group_size) + masks.shape[2:], lambda g: (0, g, 0, 0)),
        ]
        + [piece_block] * piece_count,
        out_specs=[
            pl.BlockSpec((tok_rows, group_width), lambda g: (0, g)),
            pl.BlockSpec((1, rows, 1), lambda g: (g, 0, 0)),
            pl.BlockSpec((1, rows, 1), lambda g: (g, 0, 0)),
        ],
        out_shape=[
            jax.ShapeDtypeStruct((tok_rows, query_width), jnp.bfloat16),
            jax.ShapeDtypeStruct((KVH, rows, 1), jnp.float32),
            jax.ShapeDtypeStruct((KVH, rows, 1), jnp.float32),
        ],
        cost_estimate=pl.CostEstimate(
            flops=flops,
            transcendentals=tok_rows * tok_rows * H * piece_count,
            bytes_accessed=3 * query_rows.size * 2 + piece_count * pieces[0].size * 2,
        ),
    )(query_rows, grad_rows, masks, *pieces)


def attention_backward(query_rows, grad_rows, pieces, masks, log_total, delta):
    tok_rows, query_width = query_rows.shape
    piece_count = len(pieces)
    group_size = H // KVH
    group_width = group_size * HD
    rows = group_size * tok_rows
    flops = 10 * tok_rows * tok_rows * HD * H * piece_count
    piece_block = pl.BlockSpec((2, tok_rows, HD), lambda g: (0, 0, g))
    outs = pl.pallas_call(
        functools.partial(backward_kernel, piece_count, group_size),
        grid=(KVH,),
        in_specs=[
            pl.BlockSpec((tok_rows, group_width), lambda g: (0, g)),
            pl.BlockSpec((tok_rows, group_width), lambda g: (0, g)),
            pl.BlockSpec((piece_count, group_size) + masks.shape[2:], lambda g: (0, g, 0, 0)),
            pl.BlockSpec((1, rows, 1), lambda g: (g, 0, 0)),
            pl.BlockSpec((1, rows, 1), lambda g: (g, 0, 0)),
        ]
        + [piece_block] * piece_count,
        out_specs=[pl.BlockSpec((tok_rows, group_width), lambda g: (0, g))] + [piece_block] * piece_count,
        out_shape=[jax.ShapeDtypeStruct((tok_rows, query_width), jnp.bfloat16)]
        + [jax.ShapeDtypeStruct(pieces[0].shape, jnp.bfloat16)] * piece_count,
        cost_estimate=pl.CostEstimate(
            flops=flops,
            transcendentals=tok_rows * tok_rows * H * piece_count,
            bytes_accessed=2 * query_rows.size * 2 + 2 * piece_count * pieces[0].size * 2,
        ),
    )(query_rows, grad_rows, masks, log_total, delta, *pieces)
    return outs[0], outs[1:]


def local(query, keys, values, grad_out, random_blocks, global_ids):
    tok_rows = query.shape[1]
    ctx_count = lax.axis_size("ctx")
    ctx_index = lax.axis_index("ctx")
    masks = block_masks(random_blocks[0], global_ids[0], ctx_index, ctx_count, tok_rows)

    own = jnp.stack([keys[0], values[0]])
    if ctx_count == 4:
        step_one = shifted_open(own, "ctx", 1)
        step_three = shifted_open(own, "ctx", 3)
        pieces = [own, step_one, shifted_open(step_one, "ctx", 1), step_three]
    else:
        pieces = [own]
        for shift in range(1, ctx_count):
            pieces.append(shifted_open(pieces[-1], "ctx", 1))
    attended, log_total, delta = attention_forward(query[0], grad_out[0], pieces, masks)
    next_input = passed_along(attended[None], "pipe", 1)

    query_grad, kv_terms = attention_backward(query[0], grad_out[0], pieces, masks, log_total, delta)
    grad_query = passed_along(query_grad[None], "pipe", -1)

    carried = None
    for step in range(1, ctx_count):
        part = kv_terms[ctx_count - step].astype(jnp.float32)
        if carried is not None:
            if step == 2:
                next_input = jnp.where(ctx_index < 0, jnp.zeros_like(next_input), next_input)
                next_input, carried = lax.optimization_barrier((next_input, carried))
            part = part + carried.astype(jnp.float32)
        carried = shifted_open(part.astype(jnp.bfloat16), "ctx", -1)
    kv_sum = kv_terms[0].astype(jnp.float32)
    if carried is not None:
        grad_query, carried = lax.optimization_barrier((grad_query, carried))
        kv_sum = kv_sum + carried.astype(jnp.float32)
    returned = passed_along(kv_sum.astype(jnp.bfloat16), "pipe", -1)
    grad_key = returned[0:1]
    grad_value = returned[1:2]
    return (next_input, grad_query, grad_key, grad_value)


def solution(mesh):
    placed = (
        P(("dp", "pipe"), "ctx", None),
        P(("dp", "pipe"), "ctx", None),
        P(("dp", "pipe"), "ctx", None),
        P(("dp", "pipe"), "ctx", None),
        P("pipe", "ctx", None, None),
        P("pipe", None),
    )
    return jax.shard_map(
        local,
        mesh=mesh,
        in_specs=placed,
        out_specs=(
            P(("dp", "pipe"), "ctx", None),
            P(("dp", "pipe"), "ctx", None),
            P(("dp", "pipe"), "ctx", None),
            P(("dp", "pipe"), "ctx", None),
        ),
        check_vma=False,
    )
```

```python
import functools

import jax
import jax.numpy as jnp
from jax import lax
from jax.experimental import pallas as pl
from jax.experimental.pallas import tpu as pltpu
from jax.sharding import PartitionSpec as P

H = 16
KVH = 4
HD = 128
BLOCK = 64


NEG_FILL = -1e30


def passed_along(value, axis, steps):
    count = lax.axis_size(axis)
    pairs = [(source, (source + steps) % count) for source in range(count)]
    return lax.ppermute(value, axis, pairs)


def shifted_open(value, axis, steps):
    count = lax.axis_size(axis)
    pairs = [(source, source + steps) for source in range(count) if 0 <= source + steps < count]
    return lax.ppermute(value, axis, pairs)


def block_masks(random_rows, global_row, ctx_index, piece_count, tok_rows):
    query_blocks, head_count, block_count = random_rows.shape
    shifts = jnp.arange(piece_count, dtype=jnp.int32)
    key_shard = ctx_index - shifts
    query_ids = ctx_index * query_blocks + jnp.arange(query_blocks, dtype=jnp.int32)
    key_ids = key_shard[:, None] * query_blocks + jnp.arange(query_blocks, dtype=jnp.int32)[None, :]
    safe_ids = jnp.clip(key_ids, 0, block_count - 1).reshape(-1)
    random_part = jnp.take(random_rows, safe_ids, axis=2).reshape(
        query_blocks, head_count, piece_count, query_blocks
    )
    random_part = jnp.transpose(random_part, (2, 1, 0, 3)) > 0
    query_global = jnp.any(query_ids[:, None] == global_row[None, :], axis=1)
    key_global = jnp.any(key_ids[:, :, None] == global_row[None, None, :], axis=2)
    nearby = jnp.abs(query_ids[None, :, None] - key_ids[:, None, :]) <= 1
    fixed_part = nearby | query_global[None, :, None] | key_global[:, None, :]
    table = (random_part | fixed_part[:, None, :, :]) & (key_shard >= 0)[:, None, None, None]
    expanded = jnp.repeat(table, tok_rows // query_blocks, axis=3)
    return expanded.astype(jnp.float32)


def piece_allowed(mask_ref, shift, group_size, tok_rows):
    query_blocks = mask_ref.shape[2]
    rows = group_size * tok_rows
    parts = [
        jnp.broadcast_to(mask_ref[shift, head, block : block + 1, :], (tok_rows // query_blocks, tok_rows))
        for head in range(group_size)
        for block in range(query_blocks)
    ]
    allowed = jnp.concatenate(parts, axis=0) > 0.5
    if shift == 0:
        row = lax.broadcasted_iota(jnp.int32, (rows, tok_rows), 0)
        col = lax.broadcasted_iota(jnp.int32, (rows, tok_rows), 1)
        allowed = allowed & (col <= row % tok_rows)
    return allowed


def dot_nt(a, b):
    return lax.dot_general(a, b, (((1,), (1,)), ((), ())), preferred_element_type=jnp.float32)


def dot_tn(a, b):
    return lax.dot_general(a, b, (((0,), (0,)), ((), ())), preferred_element_type=jnp.float32)


def stacked(ref, group_size):
    return jnp.concatenate([ref[:, head * HD : (head + 1) * HD] for head in range(group_size)], axis=0)


def all_allowed(mask_ref, piece_count, group_size, tok_rows):
    return jnp.concatenate(
        [piece_allowed(mask_ref, shift, group_size, tok_rows) for shift in range(piece_count)], axis=1
    )


def attention_kernel(piece_count, group_size, query_ref, grad_ref, mask_ref, *refs):
    kv_refs = refs[:piece_count]
    out_ref, dq_ref = refs[piece_count : piece_count + 2]
    dkv_refs = refs[piece_count + 2 :]
    tok_rows = query_ref.shape[0]
    score_scale = HD ** (-0.5)
    query_rows = stacked(query_ref, group_size)
    grad_rows = stacked(grad_ref, group_size)
    all_keys = jnp.concatenate([ref[0] for ref in kv_refs], axis=0)
    all_values = jnp.concatenate([ref[1] for ref in kv_refs], axis=0)
    raw = dot_nt(query_rows, all_keys) * score_scale
    masked = jnp.where(all_allowed(mask_ref, piece_count, group_size, tok_rows), raw, NEG_FILL)
    row_high = jnp.max(masked, axis=1, keepdims=True)
    weights = jnp.exp(masked - row_high)
    row_total = jnp.sum(weights, axis=1, keepdims=True)
    accumulated = jnp.dot(weights.astype(jnp.bfloat16), all_values, preferred_element_type=jnp.float32)
    attended = (accumulated / row_total).astype(out_ref.dtype)
    for head in range(group_size):
        out_ref[:, head * HD : (head + 1) * HD] = attended[head * tok_rows : (head + 1) * tok_rows]
    log_total = row_high + jnp.log(row_total)
    delta = jnp.sum(grad_rows.astype(jnp.float32) * attended.astype(jnp.float32), axis=1, keepdims=True)

    row_probs = jnp.exp(masked - log_total)
    value_terms = dot_tn(row_probs.astype(jnp.bfloat16), grad_rows)
    prob_grads = dot_nt(grad_rows, all_values)
    score_grads = (row_probs * (prob_grads - delta)).astype(jnp.bfloat16)
    query_grad = jnp.dot(score_grads, all_keys, preferred_element_type=jnp.float32)
    key_terms = dot_tn(score_grads, query_rows) * score_scale
    for shift, ref in enumerate(dkv_refs):
        piece_rows = slice(shift * tok_rows, (shift + 1) * tok_rows)
        ref[0] = key_terms[piece_rows].astype(ref.dtype)
        ref[1] = value_terms[piece_rows].astype(ref.dtype)
    query_grad = (query_grad * score_scale).astype(dq_ref.dtype)
    for head in range(group_size):
        dq_ref[:, head * HD : (head + 1) * HD] = query_grad[head * tok_rows : (head + 1) * tok_rows]


def attention(query_rows, grad_rows, pieces, masks):
    tok_rows, query_width = query_rows.shape
    piece_count = len(pieces)
    group_size = H // KVH
    group_width = group_size * HD
    flops = 12 * tok_rows * tok_rows * HD * H * piece_count
    piece_block = pl.BlockSpec((2, tok_rows, HD), lambda g: (0, 0, g))
    group_block = pl.BlockSpec((tok_rows, group_width), lambda g: (0, g))
    outs = pl.pallas_call(
        functools.partial(attention_kernel, piece_count, group_size),
        grid=(KVH,),
        in_specs=[
            group_block,
            group_block,
            pl.BlockSpec((piece_count, group_size) + masks.shape[2:], lambda g: (0, g, 0, 0)),
        ]
        + [piece_block] * piece_count,
        out_specs=[group_block, group_block] + [piece_block] * piece_count,
        out_shape=[jax.ShapeDtypeStruct((tok_rows, query_width), jnp.bfloat16)] * 2
        + [jax.ShapeDtypeStruct(pieces[0].shape, jnp.bfloat16)] * piece_count,
        cost_estimate=pl.CostEstimate(
            flops=flops,
            transcendentals=2 * tok_rows * tok_rows * H * piece_count,
            bytes_accessed=4 * query_rows.size * 2 + 2 * piece_count * pieces[0].size * 2,
        ),
    )(query_rows, grad_rows, masks, *pieces)
    return outs[0], outs[1], outs[2:]


def local(query, keys, values, grad_out, random_blocks, global_ids):
    tok_rows = query.shape[1]
    ctx_count = lax.axis_size("ctx")
    ctx_index = lax.axis_index("ctx")
    masks = block_masks(random_blocks[0], global_ids[0], ctx_index, ctx_count, tok_rows)

    own = jnp.stack([keys[0], values[0]])
    if ctx_count == 4:
        step_one = shifted_open(own, "ctx", 1)
        step_three = shifted_open(own, "ctx", 3)
        pieces = [own, step_one, shifted_open(step_one, "ctx", 1), step_three]
    else:
        pieces = [own]
        for shift in range(1, ctx_count):
            pieces.append(shifted_open(pieces[-1], "ctx", 1))
    attended, query_grad, kv_terms = attention(query[0], grad_out[0], pieces, masks)
    next_input = passed_along(attended[None], "pipe", 1)
    grad_query = passed_along(query_grad[None], "pipe", -1)

    carried = None
    for step in range(1, ctx_count):
        part = kv_terms[ctx_count - step].astype(jnp.float32)
        if carried is not None:
            if step == ctx_count - 1:
                next_input = jnp.where(ctx_index < 0, jnp.zeros_like(next_input), next_input)
                next_input, carried = lax.optimization_barrier((next_input, carried))
            part = part + carried.astype(jnp.float32)
        carried = shifted_open(part.astype(jnp.bfloat16), "ctx", -1)
    kv_sum = kv_terms[0].astype(jnp.float32)
    if carried is not None:
        grad_query, carried = lax.optimization_barrier((grad_query, carried))
        kv_sum = kv_sum + carried.astype(jnp.float32)
    returned = passed_along(kv_sum.astype(jnp.bfloat16), "pipe", -1)
    grad_key = returned[0:1]
    grad_value = returned[1:2]
    return (next_input, grad_query, grad_key, grad_value)


def solution(mesh):
    placed = (
        P(("dp", "pipe"), "ctx", None),
        P(("dp", "pipe"), "ctx", None),
        P(("dp", "pipe"), "ctx", None),
        P(("dp", "pipe"), "ctx", None),
        P("pipe", "ctx", None, None),
        P("pipe", None),
    )
    return jax.shard_map(
        local,
        mesh=mesh,
        in_specs=placed,
        out_specs=(
            P(("dp", "pipe"), "ctx", None),
            P(("dp", "pipe"), "ctx", None),
            P(("dp", "pipe"), "ctx", None),
            P(("dp", "pipe"), "ctx", None),
        ),
        check_vma=False,
    )
```

```python
import functools

import jax
import jax.numpy as jnp
from jax import lax
from jax.experimental import pallas as pl
from jax.experimental.pallas import tpu as pltpu
from jax.sharding import PartitionSpec as P

H = 16
KVH = 4
HD = 128
BLOCK = 64


NEG_FILL = -1e30


def passed_along(value, axis, steps):
    count = lax.axis_size(axis)
    pairs = [(source, (source + steps) % count) for source in range(count)]
    return lax.ppermute(value, axis, pairs)


def shifted_open(value, axis, steps):
    count = lax.axis_size(axis)
    pairs = [(source, source + steps) for source in range(count) if 0 <= source + steps < count]
    return lax.ppermute(value, axis, pairs)


def block_masks(random_rows, global_row, ctx_index, piece_count, tok_rows):
    query_blocks, head_count, block_count = random_rows.shape
    shifts = jnp.arange(piece_count, dtype=jnp.int32)
    key_shard = ctx_index - shifts
    query_ids = ctx_index * query_blocks + jnp.arange(query_blocks, dtype=jnp.int32)
    key_ids = key_shard[:, None] * query_blocks + jnp.arange(query_blocks, dtype=jnp.int32)[None, :]
    safe_ids = jnp.clip(key_ids, 0, block_count - 1).reshape(-1)
    random_part = jnp.take(random_rows, safe_ids, axis=2).reshape(
        query_blocks, head_count, piece_count, query_blocks
    )
    random_part = jnp.transpose(random_part, (2, 1, 0, 3)) > 0
    query_global = jnp.any(query_ids[:, None] == global_row[None, :], axis=1)
    key_global = jnp.any(key_ids[:, :, None] == global_row[None, None, :], axis=2)
    nearby = jnp.abs(query_ids[None, :, None] - key_ids[:, None, :]) <= 1
    fixed_part = nearby | query_global[None, :, None] | key_global[:, None, :]
    table = (random_part | fixed_part[:, None, :, :]) & (key_shard >= 0)[:, None, None, None]
    expanded = jnp.repeat(table, tok_rows // query_blocks, axis=3)
    return expanded.astype(jnp.float32)


def piece_allowed(mask_ref, shift, group_size, tok_rows):
    query_blocks = mask_ref.shape[2]
    rows = group_size * tok_rows
    parts = [
        jnp.broadcast_to(mask_ref[shift, head, block : block + 1, :], (tok_rows // query_blocks, tok_rows))
        for head in range(group_size)
        for block in range(query_blocks)
    ]
    allowed = jnp.concatenate(parts, axis=0) > 0.5
    if shift == 0:
        row = lax.broadcasted_iota(jnp.int32, (rows, tok_rows), 0)
        col = lax.broadcasted_iota(jnp.int32, (rows, tok_rows), 1)
        allowed = allowed & (col <= row % tok_rows)
    return allowed


def dot_nt(a, b):
    return lax.dot_general(a, b, (((1,), (1,)), ((), ())), preferred_element_type=jnp.float32)


def dot_tn(a, b):
    return lax.dot_general(a, b, (((0,), (0,)), ((), ())), preferred_element_type=jnp.float32)


def stacked(ref, group_size):
    return jnp.concatenate([ref[:, head * HD : (head + 1) * HD] for head in range(group_size)], axis=0)


def all_allowed(mask_ref, piece_count, group_size, tok_rows):
    return jnp.concatenate(
        [piece_allowed(mask_ref, shift, group_size, tok_rows) for shift in range(piece_count)], axis=1
    )


def attention_kernel(piece_count, group_size, query_ref, grad_ref, mask_ref, *refs):
    kv_refs = refs[:piece_count]
    out_ref, dq_ref = refs[piece_count : piece_count + 2]
    dkv_refs = refs[piece_count + 2 :]
    tok_rows = query_ref.shape[0]
    score_scale = HD ** (-0.5)
    query_rows = stacked(query_ref, group_size)
    grad_rows = stacked(grad_ref, group_size)
    all_keys = jnp.concatenate([ref[0] for ref in kv_refs], axis=0)
    all_values = jnp.concatenate([ref[1] for ref in kv_refs], axis=0)
    raw = dot_nt(query_rows, all_keys) * score_scale
    masked = jnp.where(all_allowed(mask_ref, piece_count, group_size, tok_rows), raw, NEG_FILL)
    row_high = jnp.max(masked, axis=1, keepdims=True)
    weights = jnp.exp(masked - row_high)
    row_total = jnp.sum(weights, axis=1, keepdims=True)
    accumulated = jnp.dot(weights.astype(jnp.bfloat16), all_values, preferred_element_type=jnp.float32)
    attended = (accumulated / row_total).astype(out_ref.dtype)
    for head in range(group_size):
        out_ref[:, head * HD : (head + 1) * HD] = attended[head * tok_rows : (head + 1) * tok_rows]
    log_total = row_high + jnp.log(row_total)
    delta = jnp.sum(grad_rows.astype(jnp.float32) * attended.astype(jnp.float32), axis=1, keepdims=True)

    row_probs = jnp.exp(masked - log_total)
    value_terms = dot_tn(row_probs.astype(jnp.bfloat16), grad_rows)
    prob_grads = dot_nt(grad_rows, all_values)
    score_grads = (row_probs * (prob_grads - delta)).astype(jnp.bfloat16)
    query_grad = jnp.dot(score_grads, all_keys, preferred_element_type=jnp.float32)
    key_terms = dot_tn(score_grads, query_rows) * score_scale
    for shift, ref in enumerate(dkv_refs):
        piece_rows = slice(shift * tok_rows, (shift + 1) * tok_rows)
        ref[0] = key_terms[piece_rows].astype(ref.dtype)
        ref[1] = value_terms[piece_rows].astype(ref.dtype)
    query_grad = (query_grad * score_scale).astype(dq_ref.dtype)
    for head in range(group_size):
        dq_ref[:, head * HD : (head + 1) * HD] = query_grad[head * tok_rows : (head + 1) * tok_rows]


def attention(query_rows, grad_rows, pieces, masks):
    tok_rows, query_width = query_rows.shape
    piece_count = len(pieces)
    group_size = H // KVH
    group_width = group_size * HD
    flops = 12 * tok_rows * tok_rows * HD * H * piece_count
    piece_block = pl.BlockSpec((2, tok_rows, HD), lambda g: (0, 0, g))
    group_block = pl.BlockSpec((tok_rows, group_width), lambda g: (0, g))
    outs = pl.pallas_call(
        functools.partial(attention_kernel, piece_count, group_size),
        grid=(KVH,),
        in_specs=[
            group_block,
            group_block,
            pl.BlockSpec((piece_count, group_size) + masks.shape[2:], lambda g: (0, g, 0, 0)),
        ]
        + [piece_block] * piece_count,
        out_specs=[group_block, group_block] + [piece_block] * piece_count,
        out_shape=[jax.ShapeDtypeStruct((tok_rows, query_width), jnp.bfloat16)] * 2
        + [jax.ShapeDtypeStruct(pieces[0].shape, jnp.bfloat16)] * piece_count,
        cost_estimate=pl.CostEstimate(
            flops=flops,
            transcendentals=2 * tok_rows * tok_rows * H * piece_count,
            bytes_accessed=4 * query_rows.size * 2 + 2 * piece_count * pieces[0].size * 2,
        ),
    )(query_rows, grad_rows, masks, *pieces)
    return outs[0], outs[1], outs[2:]


def local(query, keys, values, grad_out, random_blocks, global_ids):
    tok_rows = query.shape[1]
    ctx_count = lax.axis_size("ctx")
    ctx_index = lax.axis_index("ctx")
    masks = block_masks(random_blocks[0], global_ids[0], ctx_index, ctx_count, tok_rows)

    own = jnp.stack([keys[0], values[0]])
    if ctx_count == 4:
        step_one = shifted_open(own, "ctx", 1)
        step_three = shifted_open(own, "ctx", 3)
        pieces = [own, step_one, shifted_open(step_one, "ctx", 1), step_three]
    else:
        pieces = [own]
        for shift in range(1, ctx_count):
            pieces.append(shifted_open(pieces[-1], "ctx", 1))
    attended, query_grad, kv_terms = attention(query[0], grad_out[0], pieces, masks)
    next_input = passed_along(attended[None], "pipe", 1)
    grad_query = passed_along(query_grad[None], "pipe", -1)

    carried = None
    for step in range(1, ctx_count):
        part = kv_terms[ctx_count - step].astype(jnp.float32)
        if carried is not None:
            if step == ctx_count - 1:
                next_input = jnp.where(ctx_index < 0, jnp.zeros_like(next_input), next_input)
                next_input, carried = lax.optimization_barrier((next_input, carried))
            part = part + carried.astype(jnp.float32)
        carried = shifted_open(part.astype(jnp.bfloat16), "ctx", -1)
    kv_sum = kv_terms[0].astype(jnp.float32)
    if carried is not None:
        grad_query = jnp.where(ctx_index < 0, jnp.zeros_like(grad_query), grad_query)
        grad_query, carried = lax.optimization_barrier((grad_query, carried))
        kv_sum = kv_sum + carried.astype(jnp.float32)
    returned = passed_along(kv_sum.astype(jnp.bfloat16), "pipe", -1)
    grad_key = returned[0:1]
    grad_value = returned[1:2]
    return (next_input, grad_query, grad_key, grad_value)


def solution(mesh):
    placed = (
        P(("dp", "pipe"), "ctx", None),
        P(("dp", "pipe"), "ctx", None),
        P(("dp", "pipe"), "ctx", None),
        P(("dp", "pipe"), "ctx", None),
        P("pipe", "ctx", None, None),
        P("pipe", None),
    )
    return jax.shard_map(
        local,
        mesh=mesh,
        in_specs=placed,
        out_specs=(
            P(("dp", "pipe"), "ctx", None),
            P(("dp", "pipe"), "ctx", None),
            P(("dp", "pipe"), "ctx", None),
            P(("dp", "pipe"), "ctx", None),
        ),
        check_vma=False,
    )
```

```python
import functools

import jax
import jax.numpy as jnp
from jax import lax
from jax.experimental import pallas as pl
from jax.experimental.pallas import tpu as pltpu
from jax.sharding import PartitionSpec as P

H = 16
KVH = 4
HD = 128
BLOCK = 64


NEG_FILL = -1e30


def passed_along(value, axis, steps):
    count = lax.axis_size(axis)
    pairs = [(source, (source + steps) % count) for source in range(count)]
    return lax.ppermute(value, axis, pairs)


def shifted_open(value, axis, steps):
    count = lax.axis_size(axis)
    pairs = [(source, source + steps) for source in range(count) if 0 <= source + steps < count]
    return lax.ppermute(value, axis, pairs)


def block_masks(random_rows, global_row, ctx_index, piece_count, tok_rows):
    query_blocks, head_count, block_count = random_rows.shape
    shifts = jnp.arange(piece_count, dtype=jnp.int32)
    key_shard = ctx_index - shifts
    query_ids = ctx_index * query_blocks + jnp.arange(query_blocks, dtype=jnp.int32)
    key_ids = key_shard[:, None] * query_blocks + jnp.arange(query_blocks, dtype=jnp.int32)[None, :]
    safe_ids = jnp.clip(key_ids, 0, block_count - 1).reshape(-1)
    random_part = jnp.take(random_rows, safe_ids, axis=2).reshape(
        query_blocks, head_count, piece_count, query_blocks
    )
    random_part = jnp.transpose(random_part, (2, 1, 0, 3)) > 0
    query_global = jnp.any(query_ids[:, None] == global_row[None, :], axis=1)
    key_global = jnp.any(key_ids[:, :, None] == global_row[None, None, :], axis=2)
    nearby = jnp.abs(query_ids[None, :, None] - key_ids[:, None, :]) <= 1
    fixed_part = nearby | query_global[None, :, None] | key_global[:, None, :]
    table = (random_part | fixed_part[:, None, :, :]) & (key_shard >= 0)[:, None, None, None]
    expanded = jnp.repeat(table, tok_rows // query_blocks, axis=3)
    return expanded.astype(jnp.float32)


def piece_allowed(mask_ref, shift, group_size, tok_rows):
    query_blocks = mask_ref.shape[2]
    rows = group_size * tok_rows
    parts = [
        jnp.broadcast_to(mask_ref[shift, head, block : block + 1, :], (tok_rows // query_blocks, tok_rows))
        for head in range(group_size)
        for block in range(query_blocks)
    ]
    allowed = jnp.concatenate(parts, axis=0) > 0.5
    if shift == 0:
        row = lax.broadcasted_iota(jnp.int32, (rows, tok_rows), 0)
        col = lax.broadcasted_iota(jnp.int32, (rows, tok_rows), 1)
        allowed = allowed & (col <= row % tok_rows)
    return allowed


def dot_nt(a, b):
    return lax.dot_general(a, b, (((1,), (1,)), ((), ())), preferred_element_type=jnp.float32)


def dot_tn(a, b):
    return lax.dot_general(a, b, (((0,), (0,)), ((), ())), preferred_element_type=jnp.float32)


def stacked(ref, group_size):
    return jnp.concatenate([ref[:, head * HD : (head + 1) * HD] for head in range(group_size)], axis=0)


def all_allowed(mask_ref, piece_count, group_size, tok_rows):
    return jnp.concatenate(
        [piece_allowed(mask_ref, shift, group_size, tok_rows) for shift in range(piece_count)], axis=1
    )


def attention_kernel(piece_count, group_size, query_ref, grad_ref, mask_ref, *refs):
    kv_refs = refs[:piece_count]
    out_ref, dq_ref = refs[piece_count : piece_count + 2]
    dkv_refs = refs[piece_count + 2 :]
    tok_rows = query_ref.shape[0]
    score_scale = HD ** (-0.5)
    query_rows = stacked(query_ref, group_size)
    grad_rows = stacked(grad_ref, group_size)
    all_keys = jnp.concatenate([ref[0] for ref in kv_refs], axis=0)
    all_values = jnp.concatenate([ref[1] for ref in kv_refs], axis=0)
    raw = dot_nt(query_rows, all_keys) * score_scale
    masked = jnp.where(all_allowed(mask_ref, piece_count, group_size, tok_rows), raw, NEG_FILL)
    row_high = jnp.max(masked, axis=1, keepdims=True)
    weights = jnp.exp(masked - row_high)
    row_total = jnp.sum(weights, axis=1, keepdims=True)
    accumulated = jnp.dot(weights.astype(jnp.bfloat16), all_values, preferred_element_type=jnp.float32)
    attended = (accumulated / row_total).astype(out_ref.dtype)
    for head in range(group_size):
        out_ref[:, head * HD : (head + 1) * HD] = attended[head * tok_rows : (head + 1) * tok_rows]
    log_total = row_high + jnp.log(row_total)
    delta = jnp.sum(grad_rows.astype(jnp.float32) * attended.astype(jnp.float32), axis=1, keepdims=True)

    row_probs = jnp.exp(masked - log_total)
    value_terms = dot_tn(row_probs.astype(jnp.bfloat16), grad_rows)
    prob_grads = dot_nt(grad_rows, all_values)
    score_grads = (row_probs * (prob_grads - delta)).astype(jnp.bfloat16)
    query_grad = jnp.dot(score_grads, all_keys, preferred_element_type=jnp.float32)
    key_terms = dot_tn(score_grads, query_rows) * score_scale
    for shift, ref in enumerate(dkv_refs):
        piece_rows = slice(shift * tok_rows, (shift + 1) * tok_rows)
        ref[0] = key_terms[piece_rows].astype(ref.dtype)
        ref[1] = value_terms[piece_rows].astype(ref.dtype)
    query_grad = (query_grad * score_scale).astype(dq_ref.dtype)
    for head in range(group_size):
        dq_ref[:, head * HD : (head + 1) * HD] = query_grad[head * tok_rows : (head + 1) * tok_rows]


def attention(query_rows, grad_rows, pieces, masks):
    tok_rows, query_width = query_rows.shape
    piece_count = len(pieces)
    group_size = H // KVH
    group_width = group_size * HD
    flops = 12 * tok_rows * tok_rows * HD * H * piece_count
    piece_block = pl.BlockSpec((2, tok_rows, HD), lambda g: (0, 0, g))
    group_block = pl.BlockSpec((tok_rows, group_width), lambda g: (0, g))
    outs = pl.pallas_call(
        functools.partial(attention_kernel, piece_count, group_size),
        grid=(KVH,),
        in_specs=[
            group_block,
            group_block,
            pl.BlockSpec((piece_count, group_size) + masks.shape[2:], lambda g: (0, g, 0, 0)),
        ]
        + [piece_block] * piece_count,
        out_specs=[group_block, group_block] + [piece_block] * piece_count,
        out_shape=[jax.ShapeDtypeStruct((tok_rows, query_width), jnp.bfloat16)] * 2
        + [jax.ShapeDtypeStruct(pieces[0].shape, jnp.bfloat16)] * piece_count,
        cost_estimate=pl.CostEstimate(
            flops=flops,
            transcendentals=2 * tok_rows * tok_rows * H * piece_count,
            bytes_accessed=4 * query_rows.size * 2 + 2 * piece_count * pieces[0].size * 2,
        ),
    )(query_rows, grad_rows, masks, *pieces)
    return outs[0], outs[1], outs[2:]


def local(query, keys, values, grad_out, random_blocks, global_ids):
    tok_rows = query.shape[1]
    ctx_count = lax.axis_size("ctx")
    ctx_index = lax.axis_index("ctx")
    masks = block_masks(random_blocks[0], global_ids[0], ctx_index, ctx_count, tok_rows)

    own = jnp.stack([keys[0], values[0]])
    pieces = [own]
    for shift in range(1, ctx_count):
        pieces.append(shifted_open(pieces[-1], "ctx", 1))

    attended, query_grad, kv_terms = attention(query[0], grad_out[0], pieces, masks)
    next_input = passed_along(attended[None], "pipe", 1)
    grad_query = passed_along(query_grad[None], "pipe", -1)

    carried = None
    for step in range(1, ctx_count):
        part = kv_terms[ctx_count - step].astype(jnp.float32)
        if carried is not None:
            if step == ctx_count - 1:
                next_input = jnp.where(ctx_index < 0, jnp.zeros_like(next_input), next_input)
                next_input, carried = lax.optimization_barrier((next_input, carried))
            part = part + carried.astype(jnp.float32)
        carried = shifted_open(part.astype(jnp.bfloat16), "ctx", -1)
    kv_sum = kv_terms[0].astype(jnp.float32)
    if carried is not None:
        grad_query = jnp.where(ctx_index < 0, jnp.zeros_like(grad_query), grad_query)
        grad_query, carried = lax.optimization_barrier((grad_query, carried))
        kv_sum = kv_sum + carried.astype(jnp.float32)
    returned = passed_along(kv_sum.astype(jnp.bfloat16), "pipe", -1)
    grad_key = returned[0:1]
    grad_value = returned[1:2]
    return (next_input, grad_query, grad_key, grad_value)


def solution(mesh):
    placed = (
        P(("dp", "pipe"), "ctx", None),
        P(("dp", "pipe"), "ctx", None),
        P(("dp", "pipe"), "ctx", None),
        P(("dp", "pipe"), "ctx", None),
        P("pipe", "ctx", None, None),
        P("pipe", None),
    )
    return jax.shard_map(
        local,
        mesh=mesh,
        in_specs=placed,
        out_specs=(
            P(("dp", "pipe"), "ctx", None),
            P(("dp", "pipe"), "ctx", None),
            P(("dp", "pipe"), "ctx", None),
            P(("dp", "pipe"), "ctx", None),
        ),
        check_vma=False,
    )
```

```python
import functools

import jax
import jax.numpy as jnp
from jax import lax
from jax.experimental import pallas as pl
from jax.experimental.pallas import tpu as pltpu
from jax.sharding import PartitionSpec as P

H = 16
KVH = 4
HD = 128
BLOCK = 64


NEG_FILL = -1e30


def passed_along(value, axis, steps):
    count = lax.axis_size(axis)
    pairs = [(source, (source + steps) % count) for source in range(count)]
    return lax.ppermute(value, axis, pairs)


def shifted_open(value, axis, steps):
    count = lax.axis_size(axis)
    pairs = [(source, source + steps) for source in range(count) if 0 <= source + steps < count]
    return lax.ppermute(value, axis, pairs)


def block_masks(random_rows, global_row, ctx_index, piece_count, tok_rows):
    query_blocks, head_count, block_count = random_rows.shape
    shifts = jnp.arange(piece_count, dtype=jnp.int32)
    key_shard = ctx_index - shifts
    query_ids = ctx_index * query_blocks + jnp.arange(query_blocks, dtype=jnp.int32)
    key_ids = key_shard[:, None] * query_blocks + jnp.arange(query_blocks, dtype=jnp.int32)[None, :]
    safe_ids = jnp.clip(key_ids, 0, block_count - 1).reshape(-1)
    random_part = jnp.take(random_rows, safe_ids, axis=2).reshape(
        query_blocks, head_count, piece_count, query_blocks
    )
    random_part = jnp.transpose(random_part, (2, 1, 0, 3)) > 0
    query_global = jnp.any(query_ids[:, None] == global_row[None, :], axis=1)
    key_global = jnp.any(key_ids[:, :, None] == global_row[None, None, :], axis=2)
    nearby = jnp.abs(query_ids[None, :, None] - key_ids[:, None, :]) <= 1
    fixed_part = nearby | query_global[None, :, None] | key_global[:, None, :]
    table = (random_part | fixed_part[:, None, :, :]) & (key_shard >= 0)[:, None, None, None]
    expanded = jnp.repeat(table, tok_rows // query_blocks, axis=3)
    return expanded.astype(jnp.float32)


def piece_allowed(mask_ref, shift, group_size, tok_rows):
    query_blocks = mask_ref.shape[2]
    rows = group_size * tok_rows
    parts = [
        jnp.broadcast_to(mask_ref[shift, head, block : block + 1, :], (tok_rows // query_blocks, tok_rows))
        for head in range(group_size)
        for block in range(query_blocks)
    ]
    allowed = jnp.concatenate(parts, axis=0) > 0.5
    if shift == 0:
        row = lax.broadcasted_iota(jnp.int32, (rows, tok_rows), 0)
        col = lax.broadcasted_iota(jnp.int32, (rows, tok_rows), 1)
        allowed = allowed & (col <= row % tok_rows)
    return allowed


def dot_nt(a, b):
    return lax.dot_general(a, b, (((1,), (1,)), ((), ())), preferred_element_type=jnp.float32)


def dot_tn(a, b):
    return lax.dot_general(a, b, (((0,), (0,)), ((), ())), preferred_element_type=jnp.float32)


def stacked(ref, group_size):
    return jnp.concatenate([ref[:, head * HD : (head + 1) * HD] for head in range(group_size)], axis=0)


def all_allowed(mask_ref, piece_count, group_size, tok_rows):
    return jnp.concatenate(
        [piece_allowed(mask_ref, shift, group_size, tok_rows) for shift in range(piece_count)], axis=1
    )


def attention_kernel(piece_count, group_size, query_ref, grad_ref, mask_ref, *refs):
    kv_refs = refs[:piece_count]
    out_ref, dq_ref = refs[piece_count : piece_count + 2]
    dkv_refs = refs[piece_count + 2 :]
    tok_rows = query_ref.shape[0]
    score_scale = HD ** (-0.5)
    query_rows = stacked(query_ref, group_size)
    grad_rows = stacked(grad_ref, group_size)
    all_keys = jnp.concatenate([ref[0] for ref in kv_refs], axis=0)
    all_values = jnp.concatenate([ref[1] for ref in kv_refs], axis=0)
    raw = dot_nt(query_rows, all_keys) * score_scale
    masked = jnp.where(all_allowed(mask_ref, piece_count, group_size, tok_rows), raw, NEG_FILL)
    row_high = jnp.max(masked, axis=1, keepdims=True)
    weights = jnp.exp(masked - row_high)
    row_total = jnp.sum(weights, axis=1, keepdims=True)
    accumulated = jnp.dot(weights.astype(jnp.bfloat16), all_values, preferred_element_type=jnp.float32)
    attended = (accumulated / row_total).astype(out_ref.dtype)
    for head in range(group_size):
        out_ref[:, head * HD : (head + 1) * HD] = attended[head * tok_rows : (head + 1) * tok_rows]
    log_total = row_high + jnp.log(row_total)
    delta = jnp.sum(grad_rows.astype(jnp.float32) * attended.astype(jnp.float32), axis=1, keepdims=True)

    row_probs = jnp.exp(masked - log_total)
    value_terms = dot_tn(row_probs.astype(jnp.bfloat16), grad_rows)
    prob_grads = dot_nt(grad_rows, all_values)
    score_grads = (row_probs * (prob_grads - delta)).astype(jnp.bfloat16)
    query_grad = jnp.dot(score_grads, all_keys, preferred_element_type=jnp.float32)
    key_terms = dot_tn(score_grads, query_rows) * score_scale
    for shift, ref in enumerate(dkv_refs):
        piece_rows = slice(shift * tok_rows, (shift + 1) * tok_rows)
        ref[0] = key_terms[piece_rows].astype(ref.dtype)
        ref[1] = value_terms[piece_rows].astype(ref.dtype)
    query_grad = (query_grad * score_scale).astype(dq_ref.dtype)
    for head in range(group_size):
        dq_ref[:, head * HD : (head + 1) * HD] = query_grad[head * tok_rows : (head + 1) * tok_rows]


def attention(query_rows, grad_rows, pieces, masks):
    tok_rows, query_width = query_rows.shape
    piece_count = len(pieces)
    group_size = H // KVH
    group_width = group_size * HD
    flops = 12 * tok_rows * tok_rows * HD * H * piece_count
    piece_block = pl.BlockSpec((2, tok_rows, HD), lambda g: (0, 0, g))
    group_block = pl.BlockSpec((tok_rows, group_width), lambda g: (0, g))
    outs = pl.pallas_call(
        functools.partial(attention_kernel, piece_count, group_size),
        grid=(KVH,),
        in_specs=[
            group_block,
            group_block,
            pl.BlockSpec((piece_count, group_size) + masks.shape[2:], lambda g: (0, g, 0, 0)),
        ]
        + [piece_block] * piece_count,
        out_specs=[group_block, group_block] + [piece_block] * piece_count,
        out_shape=[jax.ShapeDtypeStruct((tok_rows, query_width), jnp.bfloat16)] * 2
        + [jax.ShapeDtypeStruct(pieces[0].shape, jnp.bfloat16)] * piece_count,
        cost_estimate=pl.CostEstimate(
            flops=flops,
            transcendentals=2 * tok_rows * tok_rows * H * piece_count,
            bytes_accessed=4 * query_rows.size * 2 + 2 * piece_count * pieces[0].size * 2,
        ),
    )(query_rows, grad_rows, masks, *pieces)
    return outs[0], outs[1], outs[2:]


def local(query, keys, values, grad_out, random_blocks, global_ids):
    tok_rows = query.shape[1]
    ctx_count = lax.axis_size("ctx")
    ctx_index = lax.axis_index("ctx")
    masks = block_masks(random_blocks[0], global_ids[0], ctx_index, ctx_count, tok_rows)

    own = jnp.stack([keys[0], values[0]])
    if ctx_count == 4:
        step_one = shifted_open(own, "ctx", 1)
        step_three = shifted_open(own, "ctx", 3)
        pieces = [own, step_one, shifted_open(step_one, "ctx", 1), step_three]
    else:
        pieces = [own]
        for shift in range(1, ctx_count):
            pieces.append(shifted_open(pieces[-1], "ctx", 1))
    attended, query_grad, kv_terms = attention(query[0], grad_out[0], pieces, masks)
    next_input = passed_along(attended[None], "pipe", 1)
    grad_query = passed_along(query_grad[None], "pipe", -1)

    pipe_count = lax.axis_size("pipe")
    own_part = passed_along(kv_terms[0], "pipe", -1)
    carried = None
    for step in range(1, ctx_count):
        part = kv_terms[ctx_count - step].astype(jnp.float32)
        if carried is not None:
            if step == ctx_count - 1:
                next_input = jnp.where(ctx_index < 0, jnp.zeros_like(next_input), next_input)
                next_input, own_part, carried = lax.optimization_barrier((next_input, own_part, carried))
            part = part + carried.astype(jnp.float32)
        if step < ctx_count - 1:
            carried = shifted_open(part.astype(jnp.bfloat16), "ctx", -1)
        else:
            pairs = [
                (pipe * ctx_count + ctx, ((pipe - 1) % pipe_count) * ctx_count + ctx - 1)
                for pipe in range(pipe_count)
                for ctx in range(1, ctx_count)
            ]
            carried = lax.ppermute(part.astype(jnp.bfloat16), ("pipe", "ctx"), pairs)
    kv_sum = own_part.astype(jnp.float32)
    if carried is not None:
        grad_query = jnp.where(ctx_index < 0, jnp.zeros_like(grad_query), grad_query)
        grad_query, carried = lax.optimization_barrier((grad_query, carried))
        kv_sum = kv_sum + carried.astype(jnp.float32)
    returned = kv_sum.astype(jnp.bfloat16)
    grad_key = returned[0:1]
    grad_value = returned[1:2]
    return (next_input, grad_query, grad_key, grad_value)


def solution(mesh):
    placed = (
        P(("dp", "pipe"), "ctx", None),
        P(("dp", "pipe"), "ctx", None),
        P(("dp", "pipe"), "ctx", None),
        P(("dp", "pipe"), "ctx", None),
        P("pipe", "ctx", None, None),
        P("pipe", None),
    )
    return jax.shard_map(
        local,
        mesh=mesh,
        in_specs=placed,
        out_specs=(
            P(("dp", "pipe"), "ctx", None),
            P(("dp", "pipe"), "ctx", None),
            P(("dp", "pipe"), "ctx", None),
            P(("dp", "pipe"), "ctx", None),
        ),
        check_vma=False,
    )
```

```python
import functools

import jax
import jax.numpy as jnp
from jax import lax
from jax.experimental import pallas as pl
from jax.experimental.pallas import tpu as pltpu
from jax.sharding import PartitionSpec as P

H = 16
KVH = 4
HD = 128
BLOCK = 64


NEG_FILL = -1e30


def passed_along(value, axis, steps):
    count = lax.axis_size(axis)
    pairs = [(source, (source + steps) % count) for source in range(count)]
    return lax.ppermute(value, axis, pairs)


def shifted_open(value, axis, steps):
    count = lax.axis_size(axis)
    pairs = [(source, source + steps) for source in range(count) if 0 <= source + steps < count]
    return lax.ppermute(value, axis, pairs)


def block_masks(random_rows, global_row, ctx_index, piece_count, tok_rows):
    query_blocks, head_count, block_count = random_rows.shape
    shifts = jnp.arange(piece_count, dtype=jnp.int32)
    key_shard = ctx_index - shifts
    query_ids = ctx_index * query_blocks + jnp.arange(query_blocks, dtype=jnp.int32)
    key_ids = key_shard[:, None] * query_blocks + jnp.arange(query_blocks, dtype=jnp.int32)[None, :]
    safe_ids = jnp.clip(key_ids, 0, block_count - 1).reshape(-1)
    random_part = jnp.take(random_rows, safe_ids, axis=2).reshape(
        query_blocks, head_count, piece_count, query_blocks
    )
    random_part = jnp.transpose(random_part, (2, 1, 0, 3)) > 0
    query_global = jnp.any(query_ids[:, None] == global_row[None, :], axis=1)
    key_global = jnp.any(key_ids[:, :, None] == global_row[None, None, :], axis=2)
    nearby = jnp.abs(query_ids[None, :, None] - key_ids[:, None, :]) <= 1
    fixed_part = nearby | query_global[None, :, None] | key_global[:, None, :]
    table = (random_part | fixed_part[:, None, :, :]) & (key_shard >= 0)[:, None, None, None]
    expanded = jnp.repeat(table, tok_rows // query_blocks, axis=3)
    return jnp.where(expanded, 0.0, NEG_FILL).astype(jnp.float32)


def piece_fill(mask_ref, shift, group_size, tok_rows):
    query_blocks = mask_ref.shape[2]
    rows = group_size * tok_rows
    parts = [
        jnp.broadcast_to(mask_ref[shift, head, block : block + 1, :], (tok_rows // query_blocks, tok_rows))
        for head in range(group_size)
        for block in range(query_blocks)
    ]
    fill = jnp.concatenate(parts, axis=0)
    if shift == 0:
        row = lax.broadcasted_iota(jnp.int32, (rows, tok_rows), 0)
        col = lax.broadcasted_iota(jnp.int32, (rows, tok_rows), 1)
        fill = jnp.where(col <= row % tok_rows, fill, NEG_FILL)
    return fill


def dot_nt(a, b):
    return lax.dot_general(a, b, (((1,), (1,)), ((), ())), preferred_element_type=jnp.float32)


def dot_tn(a, b):
    return lax.dot_general(a, b, (((0,), (0,)), ((), ())), preferred_element_type=jnp.float32)


def stacked(ref, group_size):
    return jnp.concatenate([ref[:, head * HD : (head + 1) * HD] for head in range(group_size)], axis=0)


def all_fill(mask_ref, piece_count, group_size, tok_rows):
    return jnp.concatenate(
        [piece_fill(mask_ref, shift, group_size, tok_rows) for shift in range(piece_count)], axis=1
    )


def attention_kernel(piece_count, group_size, query_ref, grad_ref, mask_ref, *refs):
    kv_refs = refs[:piece_count]
    out_ref, dq_ref = refs[piece_count : piece_count + 2]
    dkv_refs = refs[piece_count + 2 :]
    tok_rows = query_ref.shape[0]
    score_scale = HD ** (-0.5)
    query_rows = stacked(query_ref, group_size)
    grad_rows = stacked(grad_ref, group_size)
    all_keys = jnp.concatenate([ref[0] for ref in kv_refs], axis=0)
    all_values = jnp.concatenate([ref[1] for ref in kv_refs], axis=0)
    raw = dot_nt(query_rows, all_keys) * score_scale
    masked = raw + all_fill(mask_ref, piece_count, group_size, tok_rows)
    row_high = jnp.max(masked, axis=1, keepdims=True)
    weights = jnp.exp(masked - row_high)
    row_total = jnp.sum(weights, axis=1, keepdims=True)
    accumulated = jnp.dot(weights.astype(jnp.bfloat16), all_values, preferred_element_type=jnp.float32)
    attended = (accumulated / row_total).astype(out_ref.dtype)
    for head in range(group_size):
        out_ref[:, head * HD : (head + 1) * HD] = attended[head * tok_rows : (head + 1) * tok_rows]
    delta = jnp.sum(grad_rows.astype(jnp.float32) * attended.astype(jnp.float32), axis=1, keepdims=True)

    row_probs = weights * (1.0 / row_total)
    value_terms = dot_tn(row_probs.astype(jnp.bfloat16), grad_rows)
    prob_grads = dot_nt(grad_rows, all_values)
    score_grads = (row_probs * (prob_grads - delta)).astype(jnp.bfloat16)
    query_grad = jnp.dot(score_grads, all_keys, preferred_element_type=jnp.float32)
    key_terms = dot_tn(score_grads, query_rows) * score_scale
    for shift, ref in enumerate(dkv_refs):
        piece_rows = slice(shift * tok_rows, (shift + 1) * tok_rows)
        ref[0] = key_terms[piece_rows].astype(ref.dtype)
        ref[1] = value_terms[piece_rows].astype(ref.dtype)
    query_grad = (query_grad * score_scale).astype(dq_ref.dtype)
    for head in range(group_size):
        dq_ref[:, head * HD : (head + 1) * HD] = query_grad[head * tok_rows : (head + 1) * tok_rows]


def attention(query_rows, grad_rows, pieces, masks):
    tok_rows, query_width = query_rows.shape
    piece_count = len(pieces)
    group_size = H // KVH
    group_width = group_size * HD
    flops = 12 * tok_rows * tok_rows * HD * H * piece_count
    piece_block = pl.BlockSpec((2, tok_rows, HD), lambda g: (0, 0, g))
    group_block = pl.BlockSpec((tok_rows, group_width), lambda g: (0, g))
    outs = pl.pallas_call(
        functools.partial(attention_kernel, piece_count, group_size),
        grid=(KVH,),
        in_specs=[
            group_block,
            group_block,
            pl.BlockSpec((piece_count, group_size) + masks.shape[2:], lambda g: (0, g, 0, 0)),
        ]
        + [piece_block] * piece_count,
        out_specs=[group_block, group_block] + [piece_block] * piece_count,
        out_shape=[jax.ShapeDtypeStruct((tok_rows, query_width), jnp.bfloat16)] * 2
        + [jax.ShapeDtypeStruct(pieces[0].shape, jnp.bfloat16)] * piece_count,
        cost_estimate=pl.CostEstimate(
            flops=flops,
            transcendentals=2 * tok_rows * tok_rows * H * piece_count,
            bytes_accessed=4 * query_rows.size * 2 + 2 * piece_count * pieces[0].size * 2,
        ),
    )(query_rows, grad_rows, masks, *pieces)
    return outs[0], outs[1], outs[2:]


def local(query, keys, values, grad_out, random_blocks, global_ids):
    tok_rows = query.shape[1]
    ctx_count = lax.axis_size("ctx")
    ctx_index = lax.axis_index("ctx")
    masks = block_masks(random_blocks[0], global_ids[0], ctx_index, ctx_count, tok_rows)

    own = jnp.stack([keys[0], values[0]])
    if ctx_count == 4:
        step_one = shifted_open(own, "ctx", 1)
        step_three = shifted_open(own, "ctx", 3)
        pieces = [own, step_one, shifted_open(step_one, "ctx", 1), step_three]
    else:
        pieces = [own]
        for shift in range(1, ctx_count):
            pieces.append(shifted_open(pieces[-1], "ctx", 1))
    attended, query_grad, kv_terms = attention(query[0], grad_out[0], pieces, masks)
    next_input = passed_along(attended[None], "pipe", 1)
    grad_query = passed_along(query_grad[None], "pipe", -1)

    carried = None
    for step in range(1, ctx_count):
        part = kv_terms[ctx_count - step].astype(jnp.float32)
        if carried is not None:
            if step == ctx_count - 1:
                next_input = jnp.where(ctx_index < 0, jnp.zeros_like(next_input), next_input)
                next_input, carried = lax.optimization_barrier((next_input, carried))
            part = part + carried.astype(jnp.float32)
        carried = shifted_open(part.astype(jnp.bfloat16), "ctx", -1)
    kv_sum = kv_terms[0].astype(jnp.float32)
    if carried is not None:
        grad_query = jnp.where(ctx_index < 0, jnp.zeros_like(grad_query), grad_query)
        grad_query, carried = lax.optimization_barrier((grad_query, carried))
        kv_sum = kv_sum + carried.astype(jnp.float32)
    returned = passed_along(kv_sum.astype(jnp.bfloat16), "pipe", -1)
    grad_key = returned[0:1]
    grad_value = returned[1:2]
    return (next_input, grad_query, grad_key, grad_value)


def solution(mesh):
    placed = (
        P(("dp", "pipe"), "ctx", None),
        P(("dp", "pipe"), "ctx", None),
        P(("dp", "pipe"), "ctx", None),
        P(("dp", "pipe"), "ctx", None),
        P("pipe", "ctx", None, None),
        P("pipe", None),
    )
    return jax.shard_map(
        local,
        mesh=mesh,
        in_specs=placed,
        out_specs=(
            P(("dp", "pipe"), "ctx", None),
            P(("dp", "pipe"), "ctx", None),
            P(("dp", "pipe"), "ctx", None),
            P(("dp", "pipe"), "ctx", None),
        ),
        check_vma=False,
    )
```

```python
import functools

import jax
import jax.numpy as jnp
from jax import lax
from jax.experimental import pallas as pl
from jax.experimental.pallas import tpu as pltpu
from jax.sharding import PartitionSpec as P

H = 16
KVH = 4
HD = 128
BLOCK = 64


NEG_FILL = -1e30


def passed_along(value, axis, steps):
    count = lax.axis_size(axis)
    pairs = [(source, (source + steps) % count) for source in range(count)]
    return lax.ppermute(value, axis, pairs)


def shifted_open(value, axis, steps):
    count = lax.axis_size(axis)
    pairs = [(source, source + steps) for source in range(count) if 0 <= source + steps < count]
    return lax.ppermute(value, axis, pairs)


def block_masks(random_rows, global_row, ctx_index, piece_count, tok_rows):
    query_blocks, head_count, block_count = random_rows.shape
    shifts = jnp.arange(piece_count, dtype=jnp.int32)
    key_shard = ctx_index - shifts
    query_ids = ctx_index * query_blocks + jnp.arange(query_blocks, dtype=jnp.int32)
    key_ids = key_shard[:, None] * query_blocks + jnp.arange(query_blocks, dtype=jnp.int32)[None, :]
    safe_ids = jnp.clip(key_ids, 0, block_count - 1).reshape(-1)
    random_part = jnp.take(random_rows, safe_ids, axis=2).reshape(
        query_blocks, head_count, piece_count, query_blocks
    )
    random_part = jnp.transpose(random_part, (2, 1, 0, 3)) > 0
    query_global = jnp.any(query_ids[:, None] == global_row[None, :], axis=1)
    key_global = jnp.any(key_ids[:, :, None] == global_row[None, None, :], axis=2)
    nearby = jnp.abs(query_ids[None, :, None] - key_ids[:, None, :]) <= 1
    fixed_part = nearby | query_global[None, :, None] | key_global[:, None, :]
    table = (random_part | fixed_part[:, None, :, :]) & (key_shard >= 0)[:, None, None, None]
    expanded = jnp.repeat(table, tok_rows // query_blocks, axis=3)
    return jnp.where(expanded, 0.0, NEG_FILL).astype(jnp.float32)


def piece_fill(mask_ref, shift, group_size, tok_rows):
    query_blocks = mask_ref.shape[2]
    rows = group_size * tok_rows
    parts = [
        jnp.broadcast_to(mask_ref[shift, head, block : block + 1, :], (tok_rows // query_blocks, tok_rows))
        for head in range(group_size)
        for block in range(query_blocks)
    ]
    fill = jnp.concatenate(parts, axis=0)
    if shift == 0:
        row = lax.broadcasted_iota(jnp.int32, (rows, tok_rows), 0)
        col = lax.broadcasted_iota(jnp.int32, (rows, tok_rows), 1)
        fill = jnp.where(col <= row % tok_rows, fill, NEG_FILL)
    return fill


def dot_nt(a, b):
    return lax.dot_general(a, b, (((1,), (1,)), ((), ())), preferred_element_type=jnp.float32)


def dot_tn(a, b):
    return lax.dot_general(a, b, (((0,), (0,)), ((), ())), preferred_element_type=jnp.float32)


def stacked(ref, group_size):
    return jnp.concatenate([ref[:, head * HD : (head + 1) * HD] for head in range(group_size)], axis=0)


def all_fill(mask_ref, piece_count, group_size, tok_rows):
    return jnp.concatenate(
        [piece_fill(mask_ref, shift, group_size, tok_rows) for shift in range(piece_count)], axis=1
    )


def group_kernel(piece_count, group_size, sub, query_ref, grad_ref, mask_ref, kv_refs, out_ref, dq_ref, dkv_refs):
    tok_rows = query_ref.shape[0]
    score_scale = HD ** (-0.5)
    width = group_size * HD
    cols = slice(sub * width, (sub + 1) * width)
    lanes = slice(sub * HD, (sub + 1) * HD)
    heads = slice(sub * group_size, (sub + 1) * group_size)
    query_rows = stacked(query_ref.at[:, cols], group_size)
    grad_rows = stacked(grad_ref.at[:, cols], group_size)
    all_keys = jnp.concatenate([ref[0, :, lanes] for ref in kv_refs], axis=0)
    all_values = jnp.concatenate([ref[1, :, lanes] for ref in kv_refs], axis=0)
    raw = dot_nt(query_rows, all_keys) * score_scale
    masked = raw + all_fill(mask_ref.at[:, heads], piece_count, group_size, tok_rows)
    row_high = jnp.max(masked, axis=1, keepdims=True)
    weights = jnp.exp(masked - row_high)
    row_total = jnp.sum(weights, axis=1, keepdims=True)
    accumulated = jnp.dot(weights.astype(jnp.bfloat16), all_values, preferred_element_type=jnp.float32)
    attended = (accumulated / row_total).astype(out_ref.dtype)
    for head in range(group_size):
        out_ref[:, sub * width + head * HD : sub * width + (head + 1) * HD] = attended[
            head * tok_rows : (head + 1) * tok_rows
        ]
    delta = jnp.sum(grad_rows.astype(jnp.float32) * attended.astype(jnp.float32), axis=1, keepdims=True)

    row_probs = weights * (1.0 / row_total)
    value_terms = dot_tn(row_probs.astype(jnp.bfloat16), grad_rows)
    prob_grads = dot_nt(grad_rows, all_values)
    score_grads = (row_probs * (prob_grads - delta)).astype(jnp.bfloat16)
    query_grad = jnp.dot(score_grads, all_keys, preferred_element_type=jnp.float32)
    key_terms = dot_tn(score_grads, query_rows) * score_scale
    for shift, ref in enumerate(dkv_refs):
        piece_rows = slice(shift * tok_rows, (shift + 1) * tok_rows)
        ref[0, :, lanes] = key_terms[piece_rows].astype(ref.dtype)
        ref[1, :, lanes] = value_terms[piece_rows].astype(ref.dtype)
    query_grad = (query_grad * score_scale).astype(dq_ref.dtype)
    for head in range(group_size):
        dq_ref[:, sub * width + head * HD : sub * width + (head + 1) * HD] = query_grad[
            head * tok_rows : (head + 1) * tok_rows
        ]


def attention_kernel(piece_count, group_size, per_step, query_ref, grad_ref, mask_ref, *refs):
    kv_refs = refs[:piece_count]
    out_ref, dq_ref = refs[piece_count : piece_count + 2]
    dkv_refs = refs[piece_count + 2 :]
    for sub in range(per_step):
        group_kernel(
            piece_count, group_size, sub, query_ref, grad_ref, mask_ref, kv_refs, out_ref, dq_ref, dkv_refs
        )


def attention(query_rows, grad_rows, pieces, masks):
    tok_rows, query_width = query_rows.shape
    piece_count = len(pieces)
    group_size = H // KVH
    per_step = 2 if KVH % 2 == 0 else 1
    group_width = group_size * HD * per_step
    flops = 12 * tok_rows * tok_rows * HD * H * piece_count
    piece_block = pl.BlockSpec((2, tok_rows, HD * per_step), lambda g: (0, 0, g))
    group_block = pl.BlockSpec((tok_rows, group_width), lambda g: (0, g))
    outs = pl.pallas_call(
        functools.partial(attention_kernel, piece_count, group_size, per_step),
        grid=(KVH // per_step,),
        in_specs=[
            group_block,
            group_block,
            pl.BlockSpec((piece_count, group_size * per_step) + masks.shape[2:], lambda g: (0, g, 0, 0)),
        ]
        + [piece_block] * piece_count,
        out_specs=[group_block, group_block] + [piece_block] * piece_count,
        out_shape=[jax.ShapeDtypeStruct((tok_rows, query_width), jnp.bfloat16)] * 2
        + [jax.ShapeDtypeStruct(pieces[0].shape, jnp.bfloat16)] * piece_count,
        cost_estimate=pl.CostEstimate(
            flops=flops,
            transcendentals=2 * tok_rows * tok_rows * H * piece_count,
            bytes_accessed=4 * query_rows.size * 2 + 2 * piece_count * pieces[0].size * 2,
        ),
    )(query_rows, grad_rows, masks, *pieces)
    return outs[0], outs[1], outs[2:]


def local(query, keys, values, grad_out, random_blocks, global_ids):
    tok_rows = query.shape[1]
    ctx_count = lax.axis_size("ctx")
    ctx_index = lax.axis_index("ctx")
    masks = block_masks(random_blocks[0], global_ids[0], ctx_index, ctx_count, tok_rows)

    own = jnp.stack([keys[0], values[0]])
    if ctx_count == 4:
        step_one = shifted_open(own, "ctx", 1)
        step_three = shifted_open(own, "ctx", 3)
        pieces = [own, step_one, shifted_open(step_one, "ctx", 1), step_three]
    else:
        pieces = [own]
        for shift in range(1, ctx_count):
            pieces.append(shifted_open(pieces[-1], "ctx", 1))
    attended, query_grad, kv_terms = attention(query[0], grad_out[0], pieces, masks)
    next_input = passed_along(attended[None], "pipe", 1)
    grad_query = passed_along(query_grad[None], "pipe", -1)

    carried = None
    for step in range(1, ctx_count):
        part = kv_terms[ctx_count - step].astype(jnp.float32)
        if carried is not None:
            if step == ctx_count - 1:
                next_input = jnp.where(ctx_index < 0, jnp.zeros_like(next_input), next_input)
                next_input, carried = lax.optimization_barrier((next_input, carried))
            part = part + carried.astype(jnp.float32)
        carried = shifted_open(part.astype(jnp.bfloat16), "ctx", -1)
    kv_sum = kv_terms[0].astype(jnp.float32)
    if carried is not None:
        grad_query = jnp.where(ctx_index < 0, jnp.zeros_like(grad_query), grad_query)
        grad_query, carried = lax.optimization_barrier((grad_query, carried))
        kv_sum = kv_sum + carried.astype(jnp.float32)
    returned = passed_along(kv_sum.astype(jnp.bfloat16), "pipe", -1)
    grad_key = returned[0:1]
    grad_value = returned[1:2]
    return (next_input, grad_query, grad_key, grad_value)


def solution(mesh):
    placed = (
        P(("dp", "pipe"), "ctx", None),
        P(("dp", "pipe"), "ctx", None),
        P(("dp", "pipe"), "ctx", None),
        P(("dp", "pipe"), "ctx", None),
        P("pipe", "ctx", None, None),
        P("pipe", None),
    )
    return jax.shard_map(
        local,
        mesh=mesh,
        in_specs=placed,
        out_specs=(
            P(("dp", "pipe"), "ctx", None),
            P(("dp", "pipe"), "ctx", None),
            P(("dp", "pipe"), "ctx", None),
            P(("dp", "pipe"), "ctx", None),
        ),
        check_vma=False,
    )
```

```python
import functools

import jax
import jax.numpy as jnp
from jax import lax
from jax.experimental import pallas as pl
from jax.experimental.pallas import tpu as pltpu
from jax.sharding import PartitionSpec as P

H = 16
KVH = 4
HD = 128
BLOCK = 64


NEG_FILL = -1e30


def passed_along(value, axis, steps):
    count = lax.axis_size(axis)
    pairs = [(source, (source + steps) % count) for source in range(count)]
    return lax.ppermute(value, axis, pairs)


def shifted_open(value, axis, steps):
    count = lax.axis_size(axis)
    pairs = [(source, source + steps) for source in range(count) if 0 <= source + steps < count]
    return lax.ppermute(value, axis, pairs)


def block_masks(random_rows, global_row, ctx_index, piece_count, tok_rows):
    query_blocks, head_count, block_count = random_rows.shape
    shifts = jnp.arange(piece_count, dtype=jnp.int32)
    key_shard = ctx_index - shifts
    query_ids = ctx_index * query_blocks + jnp.arange(query_blocks, dtype=jnp.int32)
    key_ids = key_shard[:, None] * query_blocks + jnp.arange(query_blocks, dtype=jnp.int32)[None, :]
    safe_ids = jnp.clip(key_ids, 0, block_count - 1).reshape(-1)
    random_part = jnp.take(random_rows, safe_ids, axis=2).reshape(
        query_blocks, head_count, piece_count, query_blocks
    )
    random_part = jnp.transpose(random_part, (2, 1, 0, 3)) > 0
    query_global = jnp.any(query_ids[:, None] == global_row[None, :], axis=1)
    key_global = jnp.any(key_ids[:, :, None] == global_row[None, None, :], axis=2)
    nearby = jnp.abs(query_ids[None, :, None] - key_ids[:, None, :]) <= 1
    fixed_part = nearby | query_global[None, :, None] | key_global[:, None, :]
    table = (random_part | fixed_part[:, None, :, :]) & (key_shard >= 0)[:, None, None, None]
    expanded = jnp.repeat(table, tok_rows // query_blocks, axis=3)
    return jnp.where(expanded, 0.0, NEG_FILL).astype(jnp.float32)


def piece_fill(mask_ref, shift, group_size, tok_rows):
    query_blocks = mask_ref.shape[2]
    rows = group_size * tok_rows
    parts = [
        jnp.broadcast_to(mask_ref[shift, head, block : block + 1, :], (tok_rows // query_blocks, tok_rows))
        for head in range(group_size)
        for block in range(query_blocks)
    ]
    fill = jnp.concatenate(parts, axis=0)
    if shift == 0:
        row = lax.broadcasted_iota(jnp.int32, (rows, tok_rows), 0)
        col = lax.broadcasted_iota(jnp.int32, (rows, tok_rows), 1)
        fill = jnp.where(col <= row % tok_rows, fill, NEG_FILL)
    return fill


def dot_nt(a, b):
    return lax.dot_general(a, b, (((1,), (1,)), ((), ())), preferred_element_type=jnp.float32)


def dot_tn(a, b):
    return lax.dot_general(a, b, (((0,), (0,)), ((), ())), preferred_element_type=jnp.float32)


def stacked(ref, group_size):
    return jnp.concatenate([ref[:, head * HD : (head + 1) * HD] for head in range(group_size)], axis=0)


def all_fill(mask_ref, piece_count, group_size, tok_rows):
    return jnp.concatenate(
        [piece_fill(mask_ref, shift, group_size, tok_rows) for shift in range(piece_count)], axis=1
    )


def attention_kernel(piece_count, group_size, query_ref, grad_ref, mask_ref, *refs):
    kv_refs = refs[:piece_count]
    out_ref, dq_ref = refs[piece_count : piece_count + 2]
    dkv_refs = refs[piece_count + 2 :]
    tok_rows = query_ref.shape[0]
    score_scale = HD ** (-0.5)
    query_rows = stacked(query_ref, group_size)
    grad_rows = stacked(grad_ref, group_size)
    all_keys = jnp.concatenate([ref[0] for ref in kv_refs], axis=0)
    all_values = jnp.concatenate([ref[1] for ref in kv_refs], axis=0)
    raw = dot_nt(query_rows, all_keys) * score_scale
    masked = raw + all_fill(mask_ref, piece_count, group_size, tok_rows)
    row_high = jnp.max(masked, axis=1, keepdims=True)
    weights = jnp.exp(masked - row_high)
    row_total = jnp.sum(weights, axis=1, keepdims=True)
    accumulated = jnp.dot(weights.astype(jnp.bfloat16), all_values, preferred_element_type=jnp.float32)
    attended = (accumulated / row_total).astype(out_ref.dtype)
    for head in range(group_size):
        out_ref[:, head * HD : (head + 1) * HD] = attended[head * tok_rows : (head + 1) * tok_rows]
    delta = jnp.sum(grad_rows.astype(jnp.float32) * attended.astype(jnp.float32), axis=1, keepdims=True)

    row_probs = weights * (1.0 / row_total)
    value_terms = dot_tn(row_probs.astype(jnp.bfloat16), grad_rows)
    prob_grads = dot_nt(grad_rows, all_values)
    score_grads = (row_probs * (prob_grads - delta)).astype(jnp.bfloat16)
    query_grad = jnp.dot(score_grads, all_keys, preferred_element_type=jnp.float32)
    key_terms = dot_tn(score_grads, query_rows) * score_scale
    for shift, ref in enumerate(dkv_refs):
        piece_rows = slice(shift * tok_rows, (shift + 1) * tok_rows)
        ref[0] = key_terms[piece_rows].astype(ref.dtype)
        ref[1] = value_terms[piece_rows].astype(ref.dtype)
    query_grad = (query_grad * score_scale).astype(dq_ref.dtype)
    for head in range(group_size):
        dq_ref[:, head * HD : (head + 1) * HD] = query_grad[head * tok_rows : (head + 1) * tok_rows]


def attention(query_rows, grad_rows, pieces, masks):
    tok_rows, query_width = query_rows.shape
    piece_count = len(pieces)
    group_size = H // KVH
    group_width = group_size * HD
    flops = 12 * tok_rows * tok_rows * HD * H * piece_count
    piece_block = pl.BlockSpec((2, tok_rows, HD), lambda g: (0, 0, g))
    group_block = pl.BlockSpec((tok_rows, group_width), lambda g: (0, g))
    outs = pl.pallas_call(
        functools.partial(attention_kernel, piece_count, group_size),
        grid=(KVH,),
        in_specs=[
            group_block,
            group_block,
            pl.BlockSpec((piece_count, group_size) + masks.shape[2:], lambda g: (0, g, 0, 0)),
        ]
        + [piece_block] * piece_count,
        out_specs=[group_block, group_block] + [piece_block] * piece_count,
        out_shape=[jax.ShapeDtypeStruct((tok_rows, query_width), jnp.bfloat16)] * 2
        + [jax.ShapeDtypeStruct(pieces[0].shape, jnp.bfloat16)] * piece_count,
        cost_estimate=pl.CostEstimate(
            flops=flops,
            transcendentals=2 * tok_rows * tok_rows * H * piece_count,
            bytes_accessed=4 * query_rows.size * 2 + 2 * piece_count * pieces[0].size * 2,
        ),
    )(query_rows, grad_rows, masks, *pieces)
    return outs[0], outs[1], outs[2:]


def local(query, keys, values, grad_out, random_blocks, global_ids):
    tok_rows = query.shape[1]
    ctx_count = lax.axis_size("ctx")
    ctx_index = lax.axis_index("ctx")
    masks = block_masks(random_blocks[0], global_ids[0], ctx_index, ctx_count, tok_rows)

    own = jnp.stack([keys[0], values[0]])
    if ctx_count == 4:
        step_one = shifted_open(own, "ctx", 1)
        step_three = shifted_open(own, "ctx", 3)
        pieces = [own, step_one, shifted_open(step_one, "ctx", 1), step_three]
    else:
        pieces = [own]
        for shift in range(1, ctx_count):
            pieces.append(shifted_open(pieces[-1], "ctx", 1))
    attended, query_grad, kv_terms = attention(query[0], grad_out[0], pieces, masks)
    grad_query = passed_along(query_grad[None], "pipe", -1)

    carried = None
    next_input = None
    for step in range(1, ctx_count):
        part = kv_terms[ctx_count - step].astype(jnp.float32)
        if carried is not None:
            part = part + carried.astype(jnp.float32)
        carried = shifted_open(part.astype(jnp.bfloat16), "ctx", -1)
        if step == 1:
            attended, carried = lax.optimization_barrier((attended, carried))
            next_input = passed_along(attended[None], "pipe", 1)
    if next_input is None:
        next_input = passed_along(attended[None], "pipe", 1)
    kv_sum = kv_terms[0].astype(jnp.float32)
    if carried is not None:
        next_input = jnp.where(ctx_index < 0, jnp.zeros_like(next_input), next_input)
        grad_query = jnp.where(ctx_index < 0, jnp.zeros_like(grad_query), grad_query)
        next_input, grad_query, carried = lax.optimization_barrier((next_input, grad_query, carried))
        kv_sum = kv_sum + carried.astype(jnp.float32)
    returned = passed_along(kv_sum.astype(jnp.bfloat16), "pipe", -1)
    grad_key = returned[0:1]
    grad_value = returned[1:2]
    return (next_input, grad_query, grad_key, grad_value)


def solution(mesh):
    placed = (
        P(("dp", "pipe"), "ctx", None),
        P(("dp", "pipe"), "ctx", None),
        P(("dp", "pipe"), "ctx", None),
        P(("dp", "pipe"), "ctx", None),
        P("pipe", "ctx", None, None),
        P("pipe", None),
    )
    return jax.shard_map(
        local,
        mesh=mesh,
        in_specs=placed,
        out_specs=(
            P(("dp", "pipe"), "ctx", None),
            P(("dp", "pipe"), "ctx", None),
            P(("dp", "pipe"), "ctx", None),
            P(("dp", "pipe"), "ctx", None),
        ),
        check_vma=False,
    )
```

```python
import functools

import jax
import jax.numpy as jnp
from jax import lax
from jax.experimental import pallas as pl
from jax.experimental.pallas import tpu as pltpu
from jax.sharding import PartitionSpec as P

H = 16
KVH = 4
HD = 128
BLOCK = 64


NEG_FILL = -1e30


def passed_along(value, axis, steps):
    count = lax.axis_size(axis)
    pairs = [(source, (source + steps) % count) for source in range(count)]
    return lax.ppermute(value, axis, pairs)


def shifted_open(value, axis, steps):
    count = lax.axis_size(axis)
    pairs = [(source, source + steps) for source in range(count) if 0 <= source + steps < count]
    return lax.ppermute(value, axis, pairs)


def block_masks(random_rows, global_row, ctx_index, piece_count, tok_rows):
    query_blocks, head_count, block_count = random_rows.shape
    shifts = jnp.arange(piece_count, dtype=jnp.int32)
    key_shard = ctx_index - shifts
    query_ids = ctx_index * query_blocks + jnp.arange(query_blocks, dtype=jnp.int32)
    key_ids = key_shard[:, None] * query_blocks + jnp.arange(query_blocks, dtype=jnp.int32)[None, :]
    safe_ids = jnp.clip(key_ids, 0, block_count - 1).reshape(-1)
    random_part = jnp.take(random_rows, safe_ids, axis=2).reshape(
        query_blocks, head_count, piece_count, query_blocks
    )
    random_part = jnp.transpose(random_part, (2, 1, 0, 3)) > 0
    query_global = jnp.any(query_ids[:, None] == global_row[None, :], axis=1)
    key_global = jnp.any(key_ids[:, :, None] == global_row[None, None, :], axis=2)
    nearby = jnp.abs(query_ids[None, :, None] - key_ids[:, None, :]) <= 1
    fixed_part = nearby | query_global[None, :, None] | key_global[:, None, :]
    table = (random_part | fixed_part[:, None, :, :]) & (key_shard >= 0)[:, None, None, None]
    expanded = jnp.repeat(table, tok_rows // query_blocks, axis=3)
    return jnp.where(expanded, 0.0, NEG_FILL).astype(jnp.float32)


def piece_fill(mask_ref, shift, group_size, tok_rows):
    query_blocks = mask_ref.shape[2]
    rows = group_size * tok_rows
    parts = [
        jnp.broadcast_to(mask_ref[shift, head, block : block + 1, :], (tok_rows // query_blocks, tok_rows))
        for head in range(group_size)
        for block in range(query_blocks)
    ]
    fill = jnp.concatenate(parts, axis=0)
    if shift == 0:
        row = lax.broadcasted_iota(jnp.int32, (rows, tok_rows), 0)
        col = lax.broadcasted_iota(jnp.int32, (rows, tok_rows), 1)
        fill = jnp.where(col <= row % tok_rows, fill, NEG_FILL)
    return fill


def dot_nt(a, b):
    return lax.dot_general(a, b, (((1,), (1,)), ((), ())), preferred_element_type=jnp.float32)


def dot_tn(a, b):
    return lax.dot_general(a, b, (((0,), (0,)), ((), ())), preferred_element_type=jnp.float32)


def stacked(ref, group_size):
    return jnp.concatenate([ref[:, head * HD : (head + 1) * HD] for head in range(group_size)], axis=0)


def all_fill(mask_ref, piece_count, group_size, tok_rows):
    return jnp.concatenate(
        [piece_fill(mask_ref, shift, group_size, tok_rows) for shift in range(piece_count)], axis=1
    )


def attention_kernel(piece_count, group_size, query_ref, grad_ref, mask_ref, *refs):
    kv_refs = refs[:piece_count]
    out_ref, dq_ref = refs[piece_count : piece_count + 2]
    dkv_refs = refs[piece_count + 2 :]
    tok_rows = query_ref.shape[0]
    score_scale = HD ** (-0.5)
    query_rows = stacked(query_ref, group_size)
    grad_rows = stacked(grad_ref, group_size)
    all_keys = jnp.concatenate([ref[0] for ref in kv_refs], axis=0)
    all_values = jnp.concatenate([ref[1] for ref in kv_refs], axis=0)
    raw = dot_nt(query_rows, all_keys) * score_scale
    masked = raw + all_fill(mask_ref, piece_count, group_size, tok_rows)
    row_high = jnp.max(masked, axis=1, keepdims=True)
    weights = jnp.exp(masked - row_high)
    row_total = jnp.sum(weights, axis=1, keepdims=True)
    accumulated = jnp.dot(weights.astype(jnp.bfloat16), all_values, preferred_element_type=jnp.float32)
    attended = (accumulated / row_total).astype(out_ref.dtype)
    for head in range(group_size):
        out_ref[:, head * HD : (head + 1) * HD] = attended[head * tok_rows : (head + 1) * tok_rows]
    delta = jnp.sum(grad_rows.astype(jnp.float32) * attended.astype(jnp.float32), axis=1, keepdims=True)

    row_probs = weights * (1.0 / row_total)
    value_terms = dot_tn(row_probs.astype(jnp.bfloat16), grad_rows)
    prob_grads = dot_nt(grad_rows, all_values)
    score_grads = (row_probs * (prob_grads - delta)).astype(jnp.bfloat16)
    query_grad = jnp.dot(score_grads, all_keys, preferred_element_type=jnp.float32)
    key_terms = dot_tn(score_grads, query_rows) * score_scale
    for shift, ref in enumerate(dkv_refs):
        piece_rows = slice(shift * tok_rows, (shift + 1) * tok_rows)
        ref[0] = key_terms[piece_rows].astype(ref.dtype)
        ref[1] = value_terms[piece_rows].astype(ref.dtype)
    query_grad = (query_grad * score_scale).astype(dq_ref.dtype)
    for head in range(group_size):
        dq_ref[:, head * HD : (head + 1) * HD] = query_grad[head * tok_rows : (head + 1) * tok_rows]


def attention(query_rows, grad_rows, pieces, masks):
    tok_rows, query_width = query_rows.shape
    piece_count = len(pieces)
    group_size = H // KVH
    group_width = group_size * HD
    flops = 12 * tok_rows * tok_rows * HD * H * piece_count
    piece_block = pl.BlockSpec((2, tok_rows, HD), lambda g: (0, 0, g))
    group_block = pl.BlockSpec((tok_rows, group_width), lambda g: (0, g))
    outs = pl.pallas_call(
        functools.partial(attention_kernel, piece_count, group_size),
        grid=(KVH,),
        in_specs=[
            group_block,
            group_block,
            pl.BlockSpec((piece_count, group_size) + masks.shape[2:], lambda g: (0, g, 0, 0)),
        ]
        + [piece_block] * piece_count,
        out_specs=[group_block, group_block] + [piece_block] * piece_count,
        out_shape=[jax.ShapeDtypeStruct((tok_rows, query_width), jnp.bfloat16)] * 2
        + [jax.ShapeDtypeStruct(pieces[0].shape, jnp.bfloat16)] * piece_count,
        cost_estimate=pl.CostEstimate(
            flops=flops,
            transcendentals=2 * tok_rows * tok_rows * H * piece_count,
            bytes_accessed=4 * query_rows.size * 2 + 2 * piece_count * pieces[0].size * 2,
        ),
    )(query_rows, grad_rows, masks, *pieces)
    return outs[0], outs[1], outs[2:]


def local(query, keys, values, grad_out, random_blocks, global_ids):
    tok_rows = query.shape[1]
    ctx_count = lax.axis_size("ctx")
    ctx_index = lax.axis_index("ctx")
    masks = block_masks(random_blocks[0], global_ids[0], ctx_index, ctx_count, tok_rows)

    own = jnp.stack([keys[0], values[0]])
    if ctx_count == 4:
        step_one = shifted_open(own, "ctx", 1)
        own_later, step_one = lax.optimization_barrier((own, step_one))
        step_three = shifted_open(own_later, "ctx", 3)
        pieces = [own, step_one, shifted_open(step_one, "ctx", 1), step_three]
    else:
        pieces = [own]
        for shift in range(1, ctx_count):
            pieces.append(shifted_open(pieces[-1], "ctx", 1))
    attended, query_grad, kv_terms = attention(query[0], grad_out[0], pieces, masks)
    grad_query = passed_along(query_grad[None], "pipe", -1)

    carried = None
    next_input = None
    for step in range(1, ctx_count):
        part = kv_terms[ctx_count - step].astype(jnp.float32)
        if carried is not None:
            part = part + carried.astype(jnp.float32)
        carried = shifted_open(part.astype(jnp.bfloat16), "ctx", -1)
        if step == 1:
            attended, carried = lax.optimization_barrier((attended, carried))
            next_input = passed_along(attended[None], "pipe", 1)
    if next_input is None:
        next_input = passed_along(attended[None], "pipe", 1)
    kv_sum = kv_terms[0].astype(jnp.float32)
    if carried is not None:
        next_input = jnp.where(ctx_index < 0, jnp.zeros_like(next_input), next_input)
        grad_query = jnp.where(ctx_index < 0, jnp.zeros_like(grad_query), grad_query)
        next_input, grad_query, carried = lax.optimization_barrier((next_input, grad_query, carried))
        kv_sum = kv_sum + carried.astype(jnp.float32)
    returned = passed_along(kv_sum.astype(jnp.bfloat16), "pipe", -1)
    grad_key = returned[0:1]
    grad_value = returned[1:2]
    return (next_input, grad_query, grad_key, grad_value)


def solution(mesh):
    placed = (
        P(("dp", "pipe"), "ctx", None),
        P(("dp", "pipe"), "ctx", None),
        P(("dp", "pipe"), "ctx", None),
        P(("dp", "pipe"), "ctx", None),
        P("pipe", "ctx", None, None),
        P("pipe", None),
    )
    return jax.shard_map(
        local,
        mesh=mesh,
        in_specs=placed,
        out_specs=(
            P(("dp", "pipe"), "ctx", None),
            P(("dp", "pipe"), "ctx", None),
            P(("dp", "pipe"), "ctx", None),
            P(("dp", "pipe"), "ctx", None),
        ),
        check_vma=False,
    )
```
